256 devices in a mesh: dist: 64 (over z, x, core), sky: 4 (over y).
Axes of the slice: x: 4, y: 4, z: 8, core: 2. Of those that a mesh axis runs over, the one named last changes fastest.
Arguments:
- coarse_field: float32 [8, 512, 4096], P(None, 'dist', 'sky'), may hold values from -6 to 6
- excitations: bfloat16 [8, 1024, 16384], P(None, 'dist', 'sky'), may hold values from -6 to 6
- refine_weights: float32 [2, 4, 3, 9], replicated, may hold values from -0.875 to 0.875
- refine_sqrt: bfloat16 [2, 4, 2, 4], replicated, may hold values from -1.5 to 1.5
- halo_index: int32 [9, 4096], P(None, 'sky'), may hold values from 0 to 1279, as said below
- star_extinction: float32 [1024, 16384], P('dist', 'sky'), may hold values from 0 to 3
- star_counts: int32 [1024, 16384], P('dist', 'sky'), may hold values from 0 to 4
Outputs:
- extinction: bfloat16 [8, 1024, 16384], P(None, 'dist', 'sky')
- excitation_grad: float32 [8, 1024, 16384], P(None, 'dist', 'sky')
The draws below stay inside these ranges and needn't reach their ends.
Inputs may be any that keep to these rules, and one draw needn't show every extreme that they name: halo_index[m, P] names the coarse pixel (P // 1024) * 1024 - 128 + halo_index[m, P], which lies within 128 pixels of P and never outside 0 .. 4095; halo_index[4, P] = 128 + P % 1024.
All inputs are finite; a program needn't handle non-finite values.
Results may differ from the reference program's by a relative error of at most 0.001.
Values sent between devices are 32-bit elements; how exact they have to be, the bound alone decides.
No kernel may reach another device: no remote copies, remote signals or barrier semaphores. Data moves between devices by JAX's collectives and lax.ppermute only.
A program may use at most 128 MiB of HBM per device.

```python
import jax
import jax.numpy as jnp
from jax import lax

SAMPLES = 8
PC = 1024
BAND = 128
NPC = 4096
NSC = 512
NPF = 16384
NSF = 1024


def draw_halo_index(key, part):
    columns = jnp.arange(NPC, dtype=jnp.int32)
    tile_of = columns // PC
    offset_in = (columns % PC)[None, :]
    slot_ids = jnp.arange(9, dtype=jnp.int32)[:, None]
    jumps = jax.random.randint(key, (9, NPC), -BAND, BAND + 1, dtype=jnp.int32)
    jumps = jnp.where((slot_ids == 0) & (offset_in == 0), -BAND, jumps)
    jumps = jnp.where((slot_ids == 8) & (offset_in == PC - 1), BAND, jumps)
    picked = offset_in + BAND + jumps
    lowest = jnp.where(tile_of == 0, BAND, 0)[None, :]
    highest = jnp.where(tile_of == NPC // PC - 1, PC + BAND - 1, PC + 2 * BAND - 1)[None, :]
    picked = jnp.clip(picked, lowest, highest)
    picked = jnp.where(slot_ids == 4, offset_in + BAND, picked)
    return picked.astype(jnp.int32)


def with_ends(array, own_key, least, largest):
    longest = array.shape.index(max(array.shape))
    spots = []
    for shift in (0, 1):
        where = [jax.random.randint(jax.random.fold_in(own_key, axis), (), 0, length) for axis, length in enumerate(array.shape)]
        where[longest] = (where[longest] + shift) % array.shape[longest]
        spots.append(tuple(where))
    return array.at[spots[0]].set(least).at[spots[1]].set(largest)


def levels(own_key, dims, cuts, least, largest):
    loudness = 1.0
    for axis_at, blocks in cuts:
        steps = jax.random.uniform(jax.random.fold_in(jax.random.fold_in(own_key, 6), axis_at), (blocks,), jnp.float32, least / len(cuts), largest / len(cuts))
        loudness = loudness * jnp.repeat(jnp.exp(steps), dims[axis_at] // blocks).reshape((-1,) + (1,) * (len(dims) - 1 - axis_at))
    return loudness


def bell_draw(key, shape, scale, reach, pieces=(), kind=jnp.bfloat16):
    result = jax.random.normal(key, shape, jnp.float32) * scale
    if len(pieces) > 0:
        result = levels(key, shape, pieces, -0.22, 0.18) * result
    return jnp.clip(result, min=-reach, max=reach).astype(kind)


def setup_inputs(seed: int = 0) -> dict:
    seeds = jax.random.split(jax.random.key(seed), 8)
    coarse_field = bell_draw(seeds[0], (SAMPLES, NSC, NPC), 1.0, 6.0, ((1, 64), (2, 4)), jnp.float32)
    excitations = bell_draw(seeds[1], (SAMPLES, NSF, NPF), 1.0, 6.0, ((1, 64), (2, 4)))
    refine_weights = bell_draw(seeds[2], (2, 4, 3, 9), 54 ** -0.5, 0.875, (), jnp.float32)
    refine_sqrt = bell_draw(seeds[3], (2, 4, 2, 4), 16 ** -0.5, 1.5)
    halo_index = draw_halo_index(jax.random.fold_in(seeds[7], 71), 0)
    star_extinction = jnp.clip(3.0 * jax.random.uniform(seeds[5], (NSF, NPF), jnp.float32) ** levels(seeds[5], (NSF, NPF), ((0, 64), (1, 4)), -0.2, 0.2), 0.0, 3.0)
    star_counts = with_ends(jax.random.randint(seeds[6], (NSF, NPF), 0, 5), jax.random.fold_in(seeds[6], 1), 0, 4).astype(jnp.int32)
    return {"coarse_field": coarse_field, "excitations": excitations, "refine_weights": refine_weights, "refine_sqrt": refine_sqrt, "halo_index": halo_index, "star_extinction": star_extinction, "star_counts": star_counts}


exact_mode = lax.Precision.HIGHEST

def shell_step(first, count, total):
    shells = first + jnp.arange(count, dtype=jnp.int32)
    middle = (shells.astype(jnp.float32) + 0.5) / total
    return 3.0 * jnp.exp(3.0 * middle - 3.0) / total

def reference(coarse_field, excitations, refine_weights, refine_sqrt, halo_index, star_extinction, star_counts):
    tiles = NPC // PC
    columns = jnp.arange(NPC, dtype=jnp.int32)
    sources = (columns // PC * PC - BAND)[None, :] + halo_index.astype(jnp.int32)
    weights = refine_weights.astype(jnp.float32)
    mixing = refine_sqrt.astype(jnp.float32)
    widths = shell_step(0, NSF, NSF)
    counts = star_counts.astype(jnp.float32)

    def one_sample(inputs):
        coarse, excite = inputs
        padded = jnp.pad(coarse, ((1, 1), (0, 0)))
        nearby = padded[:, sources].reshape(NSC + 2, 9, tiles, PC)
        local_part = excite.astype(jnp.float32).reshape(NSC, 2, tiles, 4, PC)
        refined = jnp.einsum('sagbc,tqab->stgqc', local_part, mixing, precision=exact_mode)
        for offset in range(3):
            refined = refined + jnp.einsum('smgc,tqm->stgqc', nearby[offset:offset + NSC], weights[:, :, offset, :], precision=exact_mode)
        refined = refined.reshape(NSF, NPF)
        density = jnp.exp(refined) * widths[:, None]
        cumulative = jnp.cumsum(density, axis=0)
        misfit = counts * (cumulative - star_extinction)
        back = jnp.flip(jnp.cumsum(jnp.flip(misfit, 0), axis=0), 0)
        flowing = (density * back).reshape(NSC, 2, tiles, 4, PC)
        gradient = jnp.einsum('stgqc,tqab->sagbc', flowing, mixing, precision=exact_mode).reshape(NSF, NPF)
        return (cumulative.astype(jnp.bfloat16), gradient)
    extinction, excitation_grad = lax.map(one_sample, (coarse_field, excitations))
    return (extinction, excitation_grad)
```

```python
import jax
import jax.numpy as jnp
from jax import lax
from jax.sharding import PartitionSpec as P

BAND = 128


exact_mode = lax.Precision.HIGHEST


def with_halo(block, sides, width):
    for axis, dim in sides:
        count = lax.axis_size(axis)
        forward = [(i, i + 1) for i in range(count - 1)]
        backward = [(target, source) for source, target in forward]
        low = lax.ppermute(
            lax.slice_in_dim(block, block.shape[dim] - width, None, axis=dim), axis, forward
        )
        high = lax.ppermute(lax.slice_in_dim(block, 0, width, axis=dim), axis, backward)
        block = jnp.concatenate([low, block, high], axis=dim)
    return block


def block_carries(totals, partial, weight, axis):
    count = lax.axis_size(axis)
    rows, pixels = totals.shape
    width = pixels // count
    packed = jnp.concatenate([totals, partial, weight], axis=0)
    packed = packed.reshape(packed.shape[0], count, width).transpose(1, 0, 2)
    mine = lax.all_to_all(packed, axis, 0, 0, tiled=True)
    block_totals = mine[:, :rows]
    block_partial = mine[:, rows : 2 * rows]
    block_weight = mine[:, 2 * rows :]
    zero = jnp.zeros_like(block_totals[:1])
    ahead = jnp.cumsum(block_totals, axis=0)
    carry_in = jnp.concatenate([zero, ahead[:-1]], axis=0)
    block_misfit = block_partial + block_weight * carry_in
    behind = jnp.flip(jnp.cumsum(jnp.flip(block_misfit, 0), axis=0), 0)
    carry_out = jnp.concatenate([behind[1:], zero], axis=0)
    back = lax.all_to_all(jnp.concatenate([carry_in, carry_out], axis=1), axis, 0, 0, tiled=True)
    back = back.transpose(1, 0, 2).reshape(2 * rows, pixels)
    return back[:rows], back[rows:]


def shards(
    coarse_field, excitations, refine_weights, refine_sqrt, halo_index, star_extinction, star_counts
):
    samples, coarse_shells, coarse_pixels = coarse_field.shape
    fine_shells = 2 * coarse_shells
    fine_pixels = 4 * coarse_pixels
    dist_count = lax.axis_size("dist")
    dist_rank = lax.axis_index("dist")
    all_shells = fine_shells * dist_count
    blocked = coarse_field.reshape(samples, coarse_shells, coarse_pixels // BAND, BAND)
    extended = with_halo(blocked, (("dist", 1), ("sky", 2)), 1)
    extended = extended.reshape(samples, coarse_shells + 2, coarse_pixels + 2 * BAND)
    nearby = extended[:, :, halo_index]
    local_part = excitations.reshape(samples, coarse_shells, 2, 4, coarse_pixels)
    refined = jnp.einsum(
        "ksabc,tqab->kstqc", local_part, refine_sqrt, preferred_element_type=jnp.float32
    )
    for offset in range(3):
        refined = refined + jnp.einsum(
            "ksmc,tqm->kstqc",
            nearby[:, offset : offset + coarse_shells],
            refine_weights[:, :, offset, :],
            precision=exact_mode,
        )
    refined = refined.reshape(samples, fine_shells, fine_pixels)
    shells = dist_rank * fine_shells + jnp.arange(fine_shells, dtype=jnp.int32)
    middle = (shells.astype(jnp.float32) + 0.5) / all_shells
    widths = 3.0 * jnp.exp(3.0 * middle - 3.0) / all_shells
    density = jnp.exp(refined) * widths[None, :, None]
    local_cum = jnp.cumsum(density, axis=1)
    totals = local_cum[:, -1, :]
    counts = star_counts.astype(jnp.float32)
    partial = jnp.sum(counts[None] * (local_cum - star_extinction[None]), axis=1)
    weight = jnp.sum(counts, axis=0, keepdims=True)
    carry_in, carry_out = block_carries(totals, partial, weight, "dist")
    cumulative = local_cum + carry_in[:, None, :]
    misfit = counts[None] * (cumulative - star_extinction[None])
    local_back = jnp.flip(jnp.cumsum(jnp.flip(misfit, 1), axis=1), 1)
    back = local_back + carry_out[:, None, :]
    flowing = (density * back).reshape(samples, coarse_shells, 2, 4, coarse_pixels)
    gradient = jnp.einsum(
        "kstqc,tqab->ksabc", flowing, refine_sqrt.astype(jnp.float32), precision=exact_mode
    )
    return (cumulative.astype(jnp.bfloat16), gradient.reshape(samples, fine_shells, fine_pixels))


def solution(mesh):
    placed = (
        P(None, "dist", "sky"),
        P(None, "dist", "sky"),
        P(),
        P(),
        P(None, "sky"),
        P("dist", "sky"),
        P("dist", "sky"),
    )
    return jax.shard_map(
        shards,
        mesh=mesh,
        in_specs=placed,
        out_specs=(P(None, "dist", "sky"), P(None, "dist", "sky")),
        check_vma=False,
    )
```

```python
import jax
import jax.numpy as jnp
from jax import lax
from jax.sharding import PartitionSpec as P

BAND = 128


exact_mode = lax.Precision.HIGHEST


def with_halo(block, sides, width):
    for axis, dim in sides:
        count = lax.axis_size(axis)
        forward = [(i, i + 1) for i in range(count - 1)]
        backward = [(target, source) for source, target in forward]
        low = lax.ppermute(
            lax.slice_in_dim(block, block.shape[dim] - width, None, axis=dim), axis, forward
        )
        high = lax.ppermute(lax.slice_in_dim(block, 0, width, axis=dim), axis, backward)
        block = jnp.concatenate([low, block, high], axis=dim)
    return block


def block_carries(totals, partial, weight, axis):
    count = lax.axis_size(axis)
    rows, pixels = totals.shape
    width = pixels // count
    packed = jnp.concatenate([totals, partial, weight], axis=0)
    packed = packed.reshape(packed.shape[0], count, width).transpose(1, 0, 2)
    mine = lax.all_to_all(packed, axis, 0, 0, tiled=True)
    block_totals = mine[:, :rows]
    block_partial = mine[:, rows : 2 * rows]
    block_weight = mine[:, 2 * rows :]
    zero = jnp.zeros_like(block_totals[:1])
    ahead = jnp.cumsum(block_totals, axis=0)
    carry_in = jnp.concatenate([zero, ahead[:-1]], axis=0)
    block_misfit = block_partial + block_weight * carry_in
    behind = jnp.flip(jnp.cumsum(jnp.flip(block_misfit, 0), axis=0), 0)
    carry_out = jnp.concatenate([behind[1:], zero], axis=0)
    back = lax.all_to_all(jnp.concatenate([carry_in, carry_out], axis=1), axis, 0, 0, tiled=True)
    back = back.transpose(1, 0, 2).reshape(2 * rows, pixels)
    return back[:rows], back[rows:]


def split_three(values):
    high = lax.reduce_precision(values, exponent_bits=8, mantissa_bits=7)
    rest = values - high
    middle = lax.reduce_precision(rest, exponent_bits=8, mantissa_bits=7)
    low = rest - middle
    return jnp.stack([high, middle, low]).astype(jnp.bfloat16)


def gather_nearby(extended, halo_index):
    samples, shells, _ = extended.shape
    slots, pixels = halo_index.shape
    blocks = pixels // BAND
    window = 3 * BAND
    windows = jnp.stack(
        [extended[:, :, b * BAND : b * BAND + window] for b in range(blocks)]
    ).reshape(blocks, samples * shells, window)
    pieces = split_three(windows).transpose(1, 0, 2, 3).reshape(blocks, 3 * samples * shells, window)
    starts = (jnp.arange(blocks, dtype=jnp.int32) * BAND)[None, :, None]
    local = halo_index.reshape(slots, blocks, BAND) - starts
    spots = jnp.arange(window, dtype=jnp.int32)[None, :, None, None]
    onehot = (local.transpose(1, 0, 2)[:, None] == spots).astype(jnp.bfloat16)
    onehot = onehot.reshape(blocks, window, slots * BAND)
    picked = jnp.einsum("bxw,bwn->bxn", pieces, onehot, preferred_element_type=jnp.float32)
    picked = picked.reshape(blocks, 3, samples, shells, slots, BAND)
    picked = (picked[:, 0] + picked[:, 1]) + picked[:, 2]
    return picked.transpose(1, 2, 3, 0, 4).reshape(samples, shells, slots, pixels)


def shards(
    coarse_field, excitations, refine_weights, refine_sqrt, halo_index, star_extinction, star_counts
):
    samples, coarse_shells, coarse_pixels = coarse_field.shape
    fine_shells = 2 * coarse_shells
    fine_pixels = 4 * coarse_pixels
    dist_count = lax.axis_size("dist")
    dist_rank = lax.axis_index("dist")
    all_shells = fine_shells * dist_count
    blocked = coarse_field.reshape(samples, coarse_shells, coarse_pixels // BAND, BAND)
    extended = with_halo(blocked, (("dist", 1), ("sky", 2)), 1)
    extended = extended.reshape(samples, coarse_shells + 2, coarse_pixels + 2 * BAND)
    nearby = gather_nearby(extended, halo_index)
    local_part = excitations.reshape(samples, coarse_shells, 2, 4, coarse_pixels)
    refined = jnp.einsum(
        "ksabc,tqab->kstqc", local_part, refine_sqrt, preferred_element_type=jnp.float32
    )
    for offset in range(3):
        refined = refined + jnp.einsum(
            "ksmc,tqm->kstqc",
            nearby[:, offset : offset + coarse_shells],
            refine_weights[:, :, offset, :],
            precision=exact_mode,
        )
    refined = refined.reshape(samples, fine_shells, fine_pixels)
    shells = dist_rank * fine_shells + jnp.arange(fine_shells, dtype=jnp.int32)
    middle = (shells.astype(jnp.float32) + 0.5) / all_shells
    widths = 3.0 * jnp.exp(3.0 * middle - 3.0) / all_shells
    density = jnp.exp(refined) * widths[None, :, None]
    local_cum = jnp.cumsum(density, axis=1)
    totals = local_cum[:, -1, :]
    counts = star_counts.astype(jnp.float32)
    partial = jnp.sum(counts[None] * (local_cum - star_extinction[None]), axis=1)
    weight = jnp.sum(counts, axis=0, keepdims=True)
    carry_in, carry_out = block_carries(totals, partial, weight, "dist")
    cumulative = local_cum + carry_in[:, None, :]
    misfit = counts[None] * (cumulative - star_extinction[None])
    local_back = jnp.flip(jnp.cumsum(jnp.flip(misfit, 1), axis=1), 1)
    back = local_back + carry_out[:, None, :]
    flowing = (density * back).reshape(samples, coarse_shells, 2, 4, coarse_pixels)
    gradient = jnp.einsum(
        "kstqc,tqab->ksabc", flowing, refine_sqrt.astype(jnp.float32), precision=exact_mode
    )
    return (cumulative.astype(jnp.bfloat16), gradient.reshape(samples, fine_shells, fine_pixels))


def solution(mesh):
    placed = (
        P(None, "dist", "sky"),
        P(None, "dist", "sky"),
        P(),
        P(),
        P(None, "sky"),
        P("dist", "sky"),
        P("dist", "sky"),
    )
    return jax.shard_map(
        shards,
        mesh=mesh,
        in_specs=placed,
        out_specs=(P(None, "dist", "sky"), P(None, "dist", "sky")),
        check_vma=False,
    )
```

```python
import jax
import jax.numpy as jnp
from jax import lax
from jax.experimental import pallas as pl
from jax.experimental.pallas import tpu as pltpu
from jax.sharding import PartitionSpec as P

BAND = 128


exact_mode = lax.Precision.HIGHEST


def with_halo(block, sides, width):
    for axis, dim in sides:
        count = lax.axis_size(axis)
        forward = [(i, i + 1) for i in range(count - 1)]
        backward = [(target, source) for source, target in forward]
        low = lax.ppermute(
            lax.slice_in_dim(block, block.shape[dim] - width, None, axis=dim), axis, forward
        )
        high = lax.ppermute(lax.slice_in_dim(block, 0, width, axis=dim), axis, backward)
        block = jnp.concatenate([low, block, high], axis=dim)
    return block


def block_carries(totals, partial, weight, axis):
    count = lax.axis_size(axis)
    rows, pixels = totals.shape
    width = pixels // count
    packed = jnp.concatenate([totals, partial, weight], axis=0)
    packed = packed.reshape(packed.shape[0], count, width).transpose(1, 0, 2)
    mine = lax.all_to_all(packed, axis, 0, 0, tiled=True)
    block_totals = mine[:, :rows]
    block_partial = mine[:, rows : 2 * rows]
    block_weight = mine[:, 2 * rows :]
    zero = jnp.zeros_like(block_totals[:1])
    ahead = jnp.cumsum(block_totals, axis=0)
    carry_in = jnp.concatenate([zero, ahead[:-1]], axis=0)
    block_misfit = block_partial + block_weight * carry_in
    behind = jnp.flip(jnp.cumsum(jnp.flip(block_misfit, 0), axis=0), 0)
    carry_out = jnp.concatenate([behind[1:], zero], axis=0)
    back = lax.all_to_all(jnp.concatenate([carry_in, carry_out], axis=1), axis, 0, 0, tiled=True)
    back = back.transpose(1, 0, 2).reshape(2 * rows, pixels)
    return back[:rows], back[rows:]


def split_three(values):
    high = lax.reduce_precision(values, exponent_bits=8, mantissa_bits=7)
    rest = values - high
    middle = lax.reduce_precision(rest, exponent_bits=8, mantissa_bits=7)
    low = rest - middle
    return jnp.stack([high, middle, low]).astype(jnp.bfloat16)


def gather_nearby(extended, halo_index):
    samples, shells, _ = extended.shape
    slots, pixels = halo_index.shape
    blocks = pixels // BAND
    window = 3 * BAND
    windows = jnp.stack(
        [extended[:, :, b * BAND : b * BAND + window] for b in range(blocks)]
    ).reshape(blocks, samples * shells, window)
    pieces = split_three(windows).transpose(1, 0, 2, 3).reshape(blocks, 3 * samples * shells, window)
    starts = (jnp.arange(blocks, dtype=jnp.int32) * BAND)[None, :, None]
    local = halo_index.reshape(slots, blocks, BAND) - starts
    spots = jnp.arange(window, dtype=jnp.int32)[None, :, None, None]
    onehot = (local.transpose(1, 0, 2)[:, None] == spots).astype(jnp.bfloat16)
    onehot = onehot.reshape(blocks, window, slots * BAND)
    picked = jnp.einsum("bxw,bwn->bxn", pieces, onehot, preferred_element_type=jnp.float32)
    picked = picked.reshape(blocks, 3, samples, shells, slots, BAND)
    picked = (picked[:, 0] + picked[:, 1]) + picked[:, 2]
    return picked.transpose(1, 2, 3, 0, 4).reshape(samples, shells, slots, pixels)


INTERPRET = False
LANES = 128


def shifted(values, amount, toward_end):
    rows = values.shape[0]
    row = lax.broadcasted_iota(jnp.int32, values.shape, 0)
    forward = pltpu.roll(values, amount, 0)
    backward = pltpu.roll(values, rows - amount, 0)
    probe = pltpu.roll(row, amount, 0)
    plain = probe == jnp.where(row >= amount, row - amount, row + rows - amount)
    if toward_end:
        moved = jnp.where(plain, forward, backward)
        return jnp.where(row >= amount, moved, 0.0)
    moved = jnp.where(plain, backward, forward)
    return jnp.where(row < rows - amount, moved, 0.0)


def running(values, toward_end):
    for amount in (1, 2, 4):
        values = values + shifted(values, amount, toward_end)
    return values


def forward_kernel(
    weights_ref, sqrt_ref, pieces_ref, onehot_ref, excite_ref, counts_ref, stars_ref, widths_ref,
    density_ref, local_ref, sums_ref, picked_ref,
):
    blocks = onehot_ref.shape[0]
    slots = onehot_ref.shape[2] // LANES
    tile = blocks * LANES

    def one_block(b, carry):
        picked = jnp.dot(pieces_ref[0, b], onehot_ref[b], preferred_element_type=jnp.float32)
        picked_ref[...] = (picked[0:16] + picked[16:32]) + picked[32:48]
        acc = {}
        for t in range(2):
            for q in range(4):
                total = None
                for u in range(2):
                    for r in range(4):
                        lanes = pl.ds(pl.multiple_of(r * tile + b * LANES, LANES), LANES)
                        term = sqrt_ref[((t * 4 + q) * 2 + u) * 4 + r] * excite_ref[0, u, :, lanes].astype(jnp.float32)
                        total = term if total is None else total + term
                acc[t, q] = total
        for j in range(3):
            for m in range(slots):
                near = picked_ref[pl.ds(j, 8), pl.ds(m * LANES, LANES)]
                for t in range(2):
                    for q in range(4):
                        acc[t, q] = acc[t, q] + weights_ref[((t * 4 + q) * 3 + j) * 9 + m] * near
        for q in range(4):
            lanes = pl.ds(pl.multiple_of(q * tile + b * LANES, LANES), LANES)
            even = jnp.exp(acc[0, q]) * widths_ref[0]
            odd = jnp.exp(acc[1, q]) * widths_ref[1]
            density_ref[0, 0, :, lanes] = even
            density_ref[0, 1, :, lanes] = odd
            through = running(even + odd, True)
            before = shifted(through, 1, True) + even
            local_ref[0, 0, :, lanes] = before
            local_ref[0, 1, :, lanes] = through
            misfit = counts_ref[0, :, lanes] * (before - stars_ref[0, :, lanes]) + counts_ref[1, :, lanes] * (
                through - stars_ref[1, :, lanes]
            )
            sums_ref[0, 0:1, lanes] = through[7:8]
            sums_ref[0, 1:2, lanes] = jnp.sum(misfit, axis=0, keepdims=True)
        return carry

    lax.fori_loop(0, blocks, one_block, 0)


def backward_kernel(
    sqrt_ref, density_ref, local_ref, carries_ref, counts_ref, stars_ref, extinct_ref, grad_ref
):
    tile = density_ref.shape[3] // 4
    blocks = tile // LANES

    def one_block(b, carry):
        flow = {}
        for q in range(4):
            lanes = pl.ds(pl.multiple_of(q * tile + b * LANES, LANES), LANES)
            into = carries_ref[0, 0:1, lanes]
            past = carries_ref[0, 1:2, lanes]
            even = local_ref[0, 0, :, lanes] + into
            odd = local_ref[0, 1, :, lanes] + into
            extinct_ref[0, 0, :, lanes] = even.astype(extinct_ref.dtype)
            extinct_ref[0, 1, :, lanes] = odd.astype(extinct_ref.dtype)
            miss_even = counts_ref[0, :, lanes] * (even - stars_ref[0, :, lanes])
            miss_odd = counts_ref[1, :, lanes] * (odd - stars_ref[1, :, lanes])
            behind = running(miss_even + miss_odd, False)
            back_even = behind + past
            back_odd = (shifted(behind, 1, False) + miss_odd) + past
            flow[0, q] = density_ref[0, 0, :, lanes] * back_even
            flow[1, q] = density_ref[0, 1, :, lanes] * back_odd
        for u in range(2):
            for r in range(4):
                total = None
                for t in range(2):
                    for q in range(4):
                        term = sqrt_ref[((t * 4 + q) * 2 + u) * 4 + r] * flow[t, q]
                        total = term if total is None else total + term
                lanes = pl.ds(pl.multiple_of(r * tile + b * LANES, LANES), LANES)
                grad_ref[0, u, :, lanes] = total
        return carry

    lax.fori_loop(0, blocks, one_block, 0)


def by_parity(values):
    lead = values.shape[:-2]
    shells, width = values.shape[-2:]
    values = values.reshape(lead + (shells // 2, 2, width))
    return jnp.swapaxes(values, -2, -3)


def from_parity(values):
    lead = values.shape[:-3]
    _, shells, width = values.shape[-3:]
    return jnp.swapaxes(values, -2, -3).reshape(lead + (2 * shells, width))


def local_forward(extended, halo_index, excitations, refine_weights, refine_sqrt, counts, stars, widths):
    samples, shells, _ = extended.shape
    slots, pixels = halo_index.shape
    blocks = pixels // BAND
    window = 3 * BAND
    fine_shells = excitations.shape[1]
    fine_pixels = excitations.shape[2]
    windows = jnp.stack(
        [extended[:, :, b * BAND : b * BAND + window] for b in range(blocks)], axis=1
    )
    pieces = split_three(windows)
    pieces = jnp.pad(pieces, ((0, 0), (0, 0), (0, 0), (0, 16 - shells), (0, 0)))
    pieces = pieces.transpose(1, 2, 0, 3, 4).reshape(samples, blocks, 3 * 16, window)
    starts = (jnp.arange(blocks, dtype=jnp.int32) * BAND)[None, :, None]
    local = halo_index.reshape(slots, blocks, BAND) - starts
    spots = jnp.arange(window, dtype=jnp.int32)[None, :, None, None]
    onehot = (local.transpose(1, 0, 2)[:, None] == spots).astype(jnp.bfloat16)
    onehot = onehot.reshape(blocks, window, slots * BAND)
    excite = by_parity(excitations)
    half = fine_shells // 2
    wide = jnp.broadcast_to(widths.reshape(half, 2).T[:, :, None], (2, half, LANES))
    smem = pl.BlockSpec(memory_space=pltpu.SMEM)
    whole = lambda shape: pl.BlockSpec(shape, lambda k: (0,) * len(shape))
    per_sample = lambda shape: pl.BlockSpec(shape, lambda k: (k,) + (0,) * (len(shape) - 1))
    return pl.pallas_call(
        forward_kernel,
        grid=(samples,),
        in_specs=[
            smem,
            smem,
            per_sample((1, blocks, 48, window)),
            whole((blocks, window, slots * BAND)),
            per_sample((1, 2, half, fine_pixels)),
            whole((2, half, fine_pixels)),
            whole((2, half, fine_pixels)),
            whole((2, half, LANES)),
        ],
        out_specs=[
            per_sample((1, 2, half, fine_pixels)),
            per_sample((1, 2, half, fine_pixels)),
            per_sample((1, 2, fine_pixels)),
        ],
        out_shape=[
            jax.ShapeDtypeStruct((samples, 2, half, fine_pixels), jnp.float32),
            jax.ShapeDtypeStruct((samples, 2, half, fine_pixels), jnp.float32),
            jax.ShapeDtypeStruct((samples, 2, fine_pixels), jnp.float32),
        ],
        scratch_shapes=[pltpu.VMEM((16, slots * BAND), jnp.float32)],
        interpret=INTERPRET,
    )(
        refine_weights.reshape(-1),
        refine_sqrt.astype(jnp.float32).reshape(-1),
        pieces,
        onehot,
        excite,
        by_parity(counts),
        by_parity(stars),
        wide,
    )


def local_backward(refine_sqrt, density, local_cum, carries, counts, stars):
    samples, _, half, fine_pixels = density.shape
    smem = pl.BlockSpec(memory_space=pltpu.SMEM)
    whole = lambda shape: pl.BlockSpec(shape, lambda k: (0,) * len(shape))
    per_sample = lambda shape: pl.BlockSpec(shape, lambda k: (k,) + (0,) * (len(shape) - 1))
    extinct, grad = pl.pallas_call(
        backward_kernel,
        grid=(samples,),
        in_specs=[
            smem,
            per_sample((1, 2, half, fine_pixels)),
            per_sample((1, 2, half, fine_pixels)),
            per_sample((1, 2, fine_pixels)),
            whole((2, half, fine_pixels)),
            whole((2, half, fine_pixels)),
        ],
        out_specs=[
            per_sample((1, 2, half, fine_pixels)),
            per_sample((1, 2, half, fine_pixels)),
        ],
        out_shape=[
            jax.ShapeDtypeStruct((samples, 2, half, fine_pixels), jnp.bfloat16),
            jax.ShapeDtypeStruct((samples, 2, half, fine_pixels), jnp.float32),
        ],
        interpret=INTERPRET,
    )(refine_sqrt.astype(jnp.float32).reshape(-1), density, local_cum, carries, by_parity(counts), by_parity(stars))
    return from_parity(extinct), from_parity(grad)


def shards(
    coarse_field, excitations, refine_weights, refine_sqrt, halo_index, star_extinction, star_counts
):
    samples, coarse_shells, coarse_pixels = coarse_field.shape
    fine_shells = 2 * coarse_shells
    fine_pixels = 4 * coarse_pixels
    dist_count = lax.axis_size("dist")
    dist_rank = lax.axis_index("dist")
    all_shells = fine_shells * dist_count
    blocked = coarse_field.reshape(samples, coarse_shells, coarse_pixels // BAND, BAND)
    extended = with_halo(blocked, (("dist", 1), ("sky", 2)), 1)
    extended = extended.reshape(samples, coarse_shells + 2, coarse_pixels + 2 * BAND)
    shells = dist_rank * fine_shells + jnp.arange(fine_shells, dtype=jnp.int32)
    middle = (shells.astype(jnp.float32) + 0.5) / all_shells
    widths = 3.0 * jnp.exp(3.0 * middle - 3.0) / all_shells
    counts = star_counts.astype(jnp.float32)
    density, local_cum, sums = local_forward(
        extended, halo_index, excitations, refine_weights, refine_sqrt, counts, star_extinction, widths
    )
    weight = jnp.sum(counts, axis=0, keepdims=True)
    carry_in, carry_out = block_carries(sums[:, 0], sums[:, 1], weight, "dist")
    carries = jnp.stack([carry_in, carry_out], axis=1)
    return local_backward(refine_sqrt, density, local_cum, carries, counts, star_extinction)


def solution(mesh):
    placed = (
        P(None, "dist", "sky"),
        P(None, "dist", "sky"),
        P(),
        P(),
        P(None, "sky"),
        P("dist", "sky"),
        P("dist", "sky"),
    )
    return jax.shard_map(
        shards,
        mesh=mesh,
        in_specs=placed,
        out_specs=(P(None, "dist", "sky"), P(None, "dist", "sky")),
        check_vma=False,
    )
```

```python
import jax
import jax.numpy as jnp
from jax import lax
from jax.experimental import pallas as pl
from jax.experimental.pallas import tpu as pltpu
from jax.sharding import PartitionSpec as P

BAND = 128
DIST = ("dist_outer", "dist_inner")


exact_mode = lax.Precision.HIGHEST


def with_halo(block, sides, width):
    for axis, dim in sides:
        count = lax.axis_size(axis)
        forward = [(i, i + 1) for i in range(count - 1)]
        backward = [(target, source) for source, target in forward]
        low = lax.ppermute(
            lax.slice_in_dim(block, block.shape[dim] - width, None, axis=dim), axis, forward
        )
        high = lax.ppermute(lax.slice_in_dim(block, 0, width, axis=dim), axis, backward)
        block = jnp.concatenate([low, block, high], axis=dim)
    return block


def exclusive(values, reverse):
    zero = jnp.zeros_like(values[:1])
    if reverse:
        behind = jnp.flip(jnp.cumsum(jnp.flip(values, 0), axis=0), 0)
        return jnp.concatenate([behind[1:], zero], axis=0)
    ahead = jnp.cumsum(values, axis=0)
    return jnp.concatenate([zero, ahead[:-1]], axis=0)


def spread(packed, axis):
    count = lax.axis_size(axis)
    height, width = packed.shape
    packed = packed.reshape(height, count, width // count).transpose(1, 0, 2)
    return lax.all_to_all(packed, axis, 0, 0, tiled=True)


def gather_back(parts, axis):
    parts = lax.all_to_all(parts, axis, 0, 0, tiled=True)
    count, height, width = parts.shape
    return parts.transpose(1, 0, 2).reshape(height, count * width)


def block_carries(totals, partial, weight, outer, inner):
    rows = totals.shape[0]
    mine = spread(jnp.concatenate([totals, partial, weight], axis=0), inner)
    block_totals = mine[:, :rows]
    block_weight = mine[:, 2 * rows :]
    within_in = exclusive(block_totals, False)
    block_misfit = mine[:, rows : 2 * rows] + block_weight * within_in
    within_out = exclusive(block_misfit, True)
    weight_out = exclusive(block_weight, True)
    group = jnp.concatenate(
        [jnp.sum(block_totals, axis=0), jnp.sum(block_misfit, axis=0), jnp.sum(block_weight, axis=0)], axis=0
    )
    groups = spread(group, outer)
    group_in = exclusive(groups[:, :rows], False)
    group_misfit = groups[:, rows : 2 * rows] + groups[:, 2 * rows :] * group_in
    group_out = exclusive(group_misfit, True)
    shared = gather_back(jnp.concatenate([group_in, group_out], axis=1), outer)
    before = shared[:rows][None]
    after = shared[rows:][None]
    carry_in = within_in + before
    carry_out = (within_out + before * weight_out) + after
    back = gather_back(jnp.concatenate([carry_in, carry_out], axis=1), inner)
    return back[:rows], back[rows:]


def split_three(values):
    high = lax.reduce_precision(values, exponent_bits=8, mantissa_bits=7)
    rest = values - high
    middle = lax.reduce_precision(rest, exponent_bits=8, mantissa_bits=7)
    low = rest - middle
    return jnp.stack([high, middle, low]).astype(jnp.bfloat16)


def gather_nearby(extended, halo_index):
    samples, shells, _ = extended.shape
    slots, pixels = halo_index.shape
    blocks = pixels // BAND
    window = 3 * BAND
    windows = jnp.stack(
        [extended[:, :, b * BAND : b * BAND + window] for b in range(blocks)]
    ).reshape(blocks, samples * shells, window)
    pieces = split_three(windows).transpose(1, 0, 2, 3).reshape(blocks, 3 * samples * shells, window)
    starts = (jnp.arange(blocks, dtype=jnp.int32) * BAND)[None, :, None]
    local = halo_index.reshape(slots, blocks, BAND) - starts
    spots = jnp.arange(window, dtype=jnp.int32)[None, :, None, None]
    onehot = (local.transpose(1, 0, 2)[:, None] == spots).astype(jnp.bfloat16)
    onehot = onehot.reshape(blocks, window, slots * BAND)
    picked = jnp.einsum("bxw,bwn->bxn", pieces, onehot, preferred_element_type=jnp.float32)
    picked = picked.reshape(blocks, 3, samples, shells, slots, BAND)
    picked = (picked[:, 0] + picked[:, 1]) + picked[:, 2]
    return picked.transpose(1, 2, 3, 0, 4).reshape(samples, shells, slots, pixels)


INTERPRET = False
LANES = 128


def shifted(values, amount, toward_end):
    rows = values.shape[0]
    row = lax.broadcasted_iota(jnp.int32, values.shape, 0)
    forward = pltpu.roll(values, amount, 0)
    backward = pltpu.roll(values, rows - amount, 0)
    probe = pltpu.roll(row, amount, 0)
    plain = probe == jnp.where(row >= amount, row - amount, row + rows - amount)
    if toward_end:
        moved = jnp.where(plain, forward, backward)
        return jnp.where(row >= amount, moved, 0.0)
    moved = jnp.where(plain, backward, forward)
    return jnp.where(row < rows - amount, moved, 0.0)


def running(values, toward_end):
    for amount in (1, 2, 4):
        values = values + shifted(values, amount, toward_end)
    return values


def forward_kernel(
    weights_ref, sqrt_ref, pieces_ref, onehot_ref, excite_ref, counts_ref, stars_ref, widths_ref,
    density_ref, local_ref, sums_ref, picked_ref,
):
    blocks = onehot_ref.shape[0]
    slots = onehot_ref.shape[2] // LANES
    tile = blocks * LANES

    def one_block(b, carry):
        picked = jnp.dot(pieces_ref[0, b], onehot_ref[b], preferred_element_type=jnp.float32)
        picked_ref[...] = (picked[0:16] + picked[16:32]) + picked[32:48]
        acc = {}
        for t in range(2):
            for q in range(4):
                total = None
                for u in range(2):
                    for r in range(4):
                        lanes = pl.ds(pl.multiple_of(r * tile + b * LANES, LANES), LANES)
                        term = sqrt_ref[((t * 4 + q) * 2 + u) * 4 + r] * excite_ref[0, u, :, lanes].astype(jnp.float32)
                        total = term if total is None else total + term
                acc[t, q] = total
        for j in range(3):
            for m in range(slots):
                near = picked_ref[pl.ds(j, 8), pl.ds(m * LANES, LANES)]
                for t in range(2):
                    for q in range(4):
                        acc[t, q] = acc[t, q] + weights_ref[((t * 4 + q) * 3 + j) * 9 + m] * near
        for q in range(4):
            lanes = pl.ds(pl.multiple_of(q * tile + b * LANES, LANES), LANES)
            even = jnp.exp(acc[0, q]) * widths_ref[0]
            odd = jnp.exp(acc[1, q]) * widths_ref[1]
            density_ref[0, 0, :, lanes] = even
            density_ref[0, 1, :, lanes] = odd
            through = running(even + odd, True)
            before = shifted(through, 1, True) + even
            local_ref[0, 0, :, lanes] = before
            local_ref[0, 1, :, lanes] = through
            misfit = counts_ref[0, :, lanes] * (before - stars_ref[0, :, lanes]) + counts_ref[1, :, lanes] * (
                through - stars_ref[1, :, lanes]
            )
            sums_ref[0, 0:1, lanes] = through[7:8]
            sums_ref[0, 1:2, lanes] = jnp.sum(misfit, axis=0, keepdims=True)
        return carry

    lax.fori_loop(0, blocks, one_block, 0)


def backward_kernel(
    sqrt_ref, density_ref, local_ref, carries_ref, counts_ref, stars_ref, extinct_ref, grad_ref
):
    tile = density_ref.shape[3] // 4
    blocks = tile // LANES

    def one_block(b, carry):
        flow = {}
        for q in range(4):
            lanes = pl.ds(pl.multiple_of(q * tile + b * LANES, LANES), LANES)
            into = carries_ref[0, 0:1, lanes]
            past = carries_ref[0, 1:2, lanes]
            even = local_ref[0, 0, :, lanes] + into
            odd = local_ref[0, 1, :, lanes] + into
            extinct_ref[0, 0, :, lanes] = even.astype(extinct_ref.dtype)
            extinct_ref[0, 1, :, lanes] = odd.astype(extinct_ref.dtype)
            miss_even = counts_ref[0, :, lanes] * (even - stars_ref[0, :, lanes])
            miss_odd = counts_ref[1, :, lanes] * (odd - stars_ref[1, :, lanes])
            behind = running(miss_even + miss_odd, False)
            back_even = behind + past
            back_odd = (shifted(behind, 1, False) + miss_odd) + past
            flow[0, q] = density_ref[0, 0, :, lanes] * back_even
            flow[1, q] = density_ref[0, 1, :, lanes] * back_odd
        for u in range(2):
            for r in range(4):
                total = None
                for t in range(2):
                    for q in range(4):
                        term = sqrt_ref[((t * 4 + q) * 2 + u) * 4 + r] * flow[t, q]
                        total = term if total is None else total + term
                lanes = pl.ds(pl.multiple_of(r * tile + b * LANES, LANES), LANES)
                grad_ref[0, u, :, lanes] = total
        return carry

    lax.fori_loop(0, blocks, one_block, 0)


def by_parity(values):
    lead = values.shape[:-2]
    shells, width = values.shape[-2:]
    values = values.reshape(lead + (shells // 2, 2, width))
    return jnp.swapaxes(values, -2, -3)


def from_parity(values):
    lead = values.shape[:-3]
    _, shells, width = values.shape[-3:]
    return jnp.swapaxes(values, -2, -3).reshape(lead + (2 * shells, width))


def local_forward(extended, halo_index, excitations, refine_weights, refine_sqrt, counts, stars, widths):
    samples, shells, _ = extended.shape
    slots, pixels = halo_index.shape
    blocks = pixels // BAND
    window = 3 * BAND
    fine_shells = excitations.shape[1]
    fine_pixels = excitations.shape[2]
    windows = jnp.stack(
        [extended[:, :, b * BAND : b * BAND + window] for b in range(blocks)], axis=1
    )
    pieces = split_three(windows)
    pieces = jnp.pad(pieces, ((0, 0), (0, 0), (0, 0), (0, 16 - shells), (0, 0)))
    pieces = pieces.transpose(1, 2, 0, 3, 4).reshape(samples, blocks, 3 * 16, window)
    starts = (jnp.arange(blocks, dtype=jnp.int32) * BAND)[None, :, None]
    local = halo_index.reshape(slots, blocks, BAND) - starts
    spots = jnp.arange(window, dtype=jnp.int32)[None, :, None, None]
    onehot = (local.transpose(1, 0, 2)[:, None] == spots).astype(jnp.bfloat16)
    onehot = onehot.reshape(blocks, window, slots * BAND)
    excite = by_parity(excitations)
    half = fine_shells // 2
    wide = jnp.broadcast_to(widths.reshape(half, 2).T[:, :, None], (2, half, LANES))
    smem = pl.BlockSpec(memory_space=pltpu.SMEM)
    whole = lambda shape: pl.BlockSpec(shape, lambda k: (0,) * len(shape))
    per_sample = lambda shape: pl.BlockSpec(shape, lambda k: (k,) + (0,) * (len(shape) - 1))
    return pl.pallas_call(
        forward_kernel,
        grid=(samples,),
        in_specs=[
            smem,
            smem,
            per_sample((1, blocks, 48, window)),
            whole((blocks, window, slots * BAND)),
            per_sample((1, 2, half, fine_pixels)),
            whole((2, half, fine_pixels)),
            whole((2, half, fine_pixels)),
            whole((2, half, LANES)),
        ],
        out_specs=[
            per_sample((1, 2, half, fine_pixels)),
            per_sample((1, 2, half, fine_pixels)),
            per_sample((1, 2, fine_pixels)),
        ],
        out_shape=[
            jax.ShapeDtypeStruct((samples, 2, half, fine_pixels), jnp.float32),
            jax.ShapeDtypeStruct((samples, 2, half, fine_pixels), jnp.float32),
            jax.ShapeDtypeStruct((samples, 2, fine_pixels), jnp.float32),
        ],
        scratch_shapes=[pltpu.VMEM((16, slots * BAND), jnp.float32)],
        interpret=INTERPRET,
    )(
        refine_weights.reshape(-1),
        refine_sqrt.astype(jnp.float32).reshape(-1),
        pieces,
        onehot,
        excite,
        by_parity(counts),
        by_parity(stars),
        wide,
    )


def local_backward(refine_sqrt, density, local_cum, carries, counts, stars):
    samples, _, half, fine_pixels = density.shape
    smem = pl.BlockSpec(memory_space=pltpu.SMEM)
    whole = lambda shape: pl.BlockSpec(shape, lambda k: (0,) * len(shape))
    per_sample = lambda shape: pl.BlockSpec(shape, lambda k: (k,) + (0,) * (len(shape) - 1))
    extinct, grad = pl.pallas_call(
        backward_kernel,
        grid=(samples,),
        in_specs=[
            smem,
            per_sample((1, 2, half, fine_pixels)),
            per_sample((1, 2, half, fine_pixels)),
            per_sample((1, 2, fine_pixels)),
            whole((2, half, fine_pixels)),
            whole((2, half, fine_pixels)),
        ],
        out_specs=[
            per_sample((1, 2, half, fine_pixels)),
            per_sample((1, 2, half, fine_pixels)),
        ],
        out_shape=[
            jax.ShapeDtypeStruct((samples, 2, half, fine_pixels), jnp.bfloat16),
            jax.ShapeDtypeStruct((samples, 2, half, fine_pixels), jnp.float32),
        ],
        interpret=INTERPRET,
    )(refine_sqrt.astype(jnp.float32).reshape(-1), density, local_cum, carries, by_parity(counts), by_parity(stars))
    return from_parity(extinct), from_parity(grad)


def shards(
    coarse_field, excitations, refine_weights, refine_sqrt, halo_index, star_extinction, star_counts
):
    samples, coarse_shells, coarse_pixels = coarse_field.shape
    fine_shells = 2 * coarse_shells
    fine_pixels = 4 * coarse_pixels
    dist_count = lax.axis_size(DIST)
    dist_rank = lax.axis_index(DIST)
    all_shells = fine_shells * dist_count
    blocked = coarse_field.reshape(samples, coarse_shells, coarse_pixels // BAND, BAND)
    extended = with_halo(blocked, ((DIST, 1), ("sky", 2)), 1)
    extended = extended.reshape(samples, coarse_shells + 2, coarse_pixels + 2 * BAND)
    shells = dist_rank * fine_shells + jnp.arange(fine_shells, dtype=jnp.int32)
    middle = (shells.astype(jnp.float32) + 0.5) / all_shells
    widths = 3.0 * jnp.exp(3.0 * middle - 3.0) / all_shells
    counts = star_counts.astype(jnp.float32)
    density, local_cum, sums = local_forward(
        extended, halo_index, excitations, refine_weights, refine_sqrt, counts, star_extinction, widths
    )
    weight = jnp.sum(counts, axis=0, keepdims=True)
    carry_in, carry_out = block_carries(sums[:, 0], sums[:, 1], weight, *DIST)
    carries = jnp.stack([carry_in, carry_out], axis=1)
    return local_backward(refine_sqrt, density, local_cum, carries, counts, star_extinction)


def solution(mesh):
    dist_count = mesh.shape["dist"]
    inner = 8 if dist_count % 8 == 0 else dist_count
    devices = mesh.devices.reshape(dist_count // inner, inner, mesh.shape["sky"])
    split = jax.sharding.Mesh(devices, DIST + ("sky",))
    placed = (
        P(None, DIST, "sky"),
        P(None, DIST, "sky"),
        P(),
        P(),
        P(None, "sky"),
        P(DIST, "sky"),
        P(DIST, "sky"),
    )
    return jax.shard_map(
        shards,
        mesh=split,
        in_specs=placed,
        out_specs=(P(None, DIST, "sky"), P(None, DIST, "sky")),
        check_vma=False,
    )
```

```python
import jax
import jax.numpy as jnp
from jax import lax
from jax.experimental import pallas as pl
from jax.experimental.pallas import tpu as pltpu
from jax.sharding import PartitionSpec as P

BAND = 128


exact_mode = lax.Precision.HIGHEST


def with_halo(block, sides, width):
    for axis, dim in sides:
        count = lax.axis_size(axis)
        forward = [(i, i + 1) for i in range(count - 1)]
        backward = [(target, source) for source, target in forward]
        low = lax.ppermute(
            lax.slice_in_dim(block, block.shape[dim] - width, None, axis=dim), axis, forward
        )
        high = lax.ppermute(lax.slice_in_dim(block, 0, width, axis=dim), axis, backward)
        block = jnp.concatenate([low, block, high], axis=dim)
    return block


def block_carries(totals, partial, weight, axis):
    count = lax.axis_size(axis)
    rows, pixels = totals.shape
    width = pixels // count
    packed = jnp.concatenate([totals, partial, weight], axis=0)
    packed = packed.reshape(packed.shape[0], count, width).transpose(1, 0, 2)
    mine = lax.all_to_all(packed, axis, 0, 0, tiled=True)
    block_totals = mine[:, :rows]
    block_partial = mine[:, rows : 2 * rows]
    block_weight = mine[:, 2 * rows :]
    blocks, height, width = block_totals.shape
    order = jnp.arange(blocks, dtype=jnp.int32)
    earlier = (order[None, :] < order[:, None]).astype(jnp.float32)
    flat = lambda values: values.reshape(blocks, -1)
    carry_in = jnp.dot(earlier, flat(block_totals), precision=exact_mode).reshape(blocks, height, width)
    block_misfit = block_partial + block_weight * carry_in
    carry_out = jnp.dot(earlier.T, flat(block_misfit), precision=exact_mode).reshape(blocks, height, width)
    back = lax.all_to_all(jnp.concatenate([carry_in, carry_out], axis=1), axis, 0, 0, tiled=True)
    back = back.transpose(1, 0, 2).reshape(2 * rows, pixels)
    return back[:rows], back[rows:]


def split_three(values):
    high = lax.reduce_precision(values, exponent_bits=8, mantissa_bits=7)
    rest = values - high
    middle = lax.reduce_precision(rest, exponent_bits=8, mantissa_bits=7)
    low = rest - middle
    return jnp.stack([high, middle, low]).astype(jnp.bfloat16)


def gather_nearby(extended, halo_index):
    samples, shells, _ = extended.shape
    slots, pixels = halo_index.shape
    blocks = pixels // BAND
    window = 3 * BAND
    windows = jnp.stack(
        [extended[:, :, b * BAND : b * BAND + window] for b in range(blocks)]
    ).reshape(blocks, samples * shells, window)
    pieces = split_three(windows).transpose(1, 0, 2, 3).reshape(blocks, 3 * samples * shells, window)
    starts = (jnp.arange(blocks, dtype=jnp.int32) * BAND)[None, :, None]
    local = halo_index.reshape(slots, blocks, BAND) - starts
    spots = jnp.arange(window, dtype=jnp.int32)[None, :, None, None]
    onehot = (local.transpose(1, 0, 2)[:, None] == spots).astype(jnp.bfloat16)
    onehot = onehot.reshape(blocks, window, slots * BAND)
    picked = jnp.einsum("bxw,bwn->bxn", pieces, onehot, preferred_element_type=jnp.float32)
    picked = picked.reshape(blocks, 3, samples, shells, slots, BAND)
    picked = (picked[:, 0] + picked[:, 1]) + picked[:, 2]
    return picked.transpose(1, 2, 3, 0, 4).reshape(samples, shells, slots, pixels)


INTERPRET = False
LANES = 128


def shifted(values, amount, toward_end):
    rows = values.shape[0]
    row = lax.broadcasted_iota(jnp.int32, values.shape, 0)
    forward = pltpu.roll(values, amount, 0)
    backward = pltpu.roll(values, rows - amount, 0)
    probe = pltpu.roll(row, amount, 0)
    plain = probe == jnp.where(row >= amount, row - amount, row + rows - amount)
    if toward_end:
        moved = jnp.where(plain, forward, backward)
        return jnp.where(row >= amount, moved, 0.0)
    moved = jnp.where(plain, backward, forward)
    return jnp.where(row < rows - amount, moved, 0.0)


def running(values, toward_end):
    for amount in (1, 2, 4):
        values = values + shifted(values, amount, toward_end)
    return values


def forward_kernel(
    weights_ref, sqrt_ref, pieces_ref, onehot_ref, excite_ref, counts_ref, stars_ref, widths_ref,
    density_ref, local_ref, sums_ref, picked_ref,
):
    blocks = onehot_ref.shape[0]
    slots = onehot_ref.shape[2] // LANES
    tile = blocks * LANES

    def one_block(b, carry):
        picked = jnp.dot(pieces_ref[0, b], onehot_ref[b], preferred_element_type=jnp.float32)
        picked_ref[...] = (picked[0:16] + picked[16:32]) + picked[32:48]
        acc = {}
        for t in range(2):
            for q in range(4):
                total = None
                for u in range(2):
                    for r in range(4):
                        lanes = pl.ds(pl.multiple_of(r * tile + b * LANES, LANES), LANES)
                        term = sqrt_ref[((t * 4 + q) * 2 + u) * 4 + r] * excite_ref[0, u, :, lanes].astype(jnp.float32)
                        total = term if total is None else total + term
                acc[t, q] = total
        for j in range(3):
            for m in range(slots):
                near = picked_ref[pl.ds(j, 8), pl.ds(m * LANES, LANES)]
                for t in range(2):
                    for q in range(4):
                        acc[t, q] = acc[t, q] + weights_ref[((t * 4 + q) * 3 + j) * 9 + m] * near
        for q in range(4):
            lanes = pl.ds(pl.multiple_of(q * tile + b * LANES, LANES), LANES)
            even = jnp.exp(acc[0, q]) * widths_ref[0]
            odd = jnp.exp(acc[1, q]) * widths_ref[1]
            density_ref[0, 0, :, lanes] = even
            density_ref[0, 1, :, lanes] = odd
            through = running(even + odd, True)
            before = shifted(through, 1, True) + even
            local_ref[0, 0, :, lanes] = before
            local_ref[0, 1, :, lanes] = through
            misfit = counts_ref[0, :, lanes] * (before - stars_ref[0, :, lanes]) + counts_ref[1, :, lanes] * (
                through - stars_ref[1, :, lanes]
            )
            sums_ref[0, 0:1, lanes] = through[7:8]
            sums_ref[0, 1:2, lanes] = jnp.sum(misfit, axis=0, keepdims=True)
        return carry

    lax.fori_loop(0, blocks, one_block, 0)


def backward_kernel(
    sqrt_ref, density_ref, local_ref, carries_ref, counts_ref, stars_ref, extinct_ref, grad_ref
):
    tile = density_ref.shape[3] // 4
    blocks = tile // LANES

    def one_block(b, carry):
        flow = {}
        for q in range(4):
            lanes = pl.ds(pl.multiple_of(q * tile + b * LANES, LANES), LANES)
            into = carries_ref[0, 0:1, lanes]
            past = carries_ref[0, 1:2, lanes]
            even = local_ref[0, 0, :, lanes] + into
            odd = local_ref[0, 1, :, lanes] + into
            extinct_ref[0, 0, :, lanes] = even.astype(extinct_ref.dtype)
            extinct_ref[0, 1, :, lanes] = odd.astype(extinct_ref.dtype)
            miss_even = counts_ref[0, :, lanes] * (even - stars_ref[0, :, lanes])
            miss_odd = counts_ref[1, :, lanes] * (odd - stars_ref[1, :, lanes])
            behind = running(miss_even + miss_odd, False)
            back_even = behind + past
            back_odd = (shifted(behind, 1, False) + miss_odd) + past
            flow[0, q] = density_ref[0, 0, :, lanes] * back_even
            flow[1, q] = density_ref[0, 1, :, lanes] * back_odd
        for u in range(2):
            for r in range(4):
                total = None
                for t in range(2):
                    for q in range(4):
                        term = sqrt_ref[((t * 4 + q) * 2 + u) * 4 + r] * flow[t, q]
                        total = term if total is None else total + term
                lanes = pl.ds(pl.multiple_of(r * tile + b * LANES, LANES), LANES)
                grad_ref[0, u, :, lanes] = total
        return carry

    lax.fori_loop(0, blocks, one_block, 0)


def by_parity(values):
    lead = values.shape[:-2]
    shells, width = values.shape[-2:]
    values = values.reshape(lead + (shells // 2, 2, width))
    return jnp.swapaxes(values, -2, -3)


def from_parity(values):
    lead = values.shape[:-3]
    _, shells, width = values.shape[-3:]
    return jnp.swapaxes(values, -2, -3).reshape(lead + (2 * shells, width))


def tiles(values):
    flat = values.reshape(-1)
    return jnp.broadcast_to(flat[:, None, None], (flat.shape[0], 8, LANES))


def local_forward(extended, halo_index, excitations, refine_weights, refine_sqrt, counts, stars, widths):
    samples, shells, _ = extended.shape
    slots, pixels = halo_index.shape
    blocks = pixels // BAND
    window = 3 * BAND
    fine_shells = excitations.shape[1]
    fine_pixels = excitations.shape[2]
    windows = jnp.stack(
        [extended[:, :, b * BAND : b * BAND + window] for b in range(blocks)], axis=1
    )
    pieces = split_three(windows)
    pieces = jnp.pad(pieces, ((0, 0), (0, 0), (0, 0), (0, 16 - shells), (0, 0)))
    pieces = pieces.transpose(1, 2, 0, 3, 4).reshape(samples, blocks, 3 * 16, window)
    starts = (jnp.arange(blocks, dtype=jnp.int32) * BAND)[None, :, None]
    local = halo_index.reshape(slots, blocks, BAND) - starts
    spots = jnp.arange(window, dtype=jnp.int32)[None, :, None, None]
    onehot = (local.transpose(1, 0, 2)[:, None] == spots).astype(jnp.bfloat16)
    onehot = onehot.reshape(blocks, window, slots * BAND)
    excite = by_parity(excitations)
    half = fine_shells // 2
    wide = jnp.broadcast_to(widths.reshape(half, 2).T[:, :, None], (2, half, LANES))
    smem = pl.BlockSpec(memory_space=pltpu.SMEM)
    whole = lambda shape: pl.BlockSpec(shape, lambda k: (0,) * len(shape))
    per_sample = lambda shape: pl.BlockSpec(shape, lambda k: (k,) + (0,) * (len(shape) - 1))
    return pl.pallas_call(
        forward_kernel,
        grid=(samples,),
        in_specs=[
            whole((2 * 4 * 3 * slots, 8, LANES)),
            whole((2 * 4 * 2 * 4, 8, LANES)),
            per_sample((1, blocks, 48, window)),
            whole((blocks, window, slots * BAND)),
            per_sample((1, 2, half, fine_pixels)),
            whole((2, half, fine_pixels)),
            whole((2, half, fine_pixels)),
            whole((2, half, LANES)),
        ],
        out_specs=[
            per_sample((1, 2, half, fine_pixels)),
            per_sample((1, 2, half, fine_pixels)),
            per_sample((1, 2, fine_pixels)),
        ],
        out_shape=[
            jax.ShapeDtypeStruct((samples, 2, half, fine_pixels), jnp.float32),
            jax.ShapeDtypeStruct((samples, 2, half, fine_pixels), jnp.float32),
            jax.ShapeDtypeStruct((samples, 2, fine_pixels), jnp.float32),
        ],
        scratch_shapes=[pltpu.VMEM((16, slots * BAND), jnp.float32)],
        interpret=INTERPRET,
    )(
        tiles(refine_weights),
        tiles(refine_sqrt.astype(jnp.float32)),
        pieces,
        onehot,
        excite,
        by_parity(counts),
        by_parity(stars),
        wide,
    )


def local_backward(refine_sqrt, density, local_cum, carries, counts, stars):
    samples, _, half, fine_pixels = density.shape
    smem = pl.BlockSpec(memory_space=pltpu.SMEM)
    whole = lambda shape: pl.BlockSpec(shape, lambda k: (0,) * len(shape))
    per_sample = lambda shape: pl.BlockSpec(shape, lambda k: (k,) + (0,) * (len(shape) - 1))
    extinct, grad = pl.pallas_call(
        backward_kernel,
        grid=(samples,),
        in_specs=[
            smem,
            per_sample((1, 2, half, fine_pixels)),
            per_sample((1, 2, half, fine_pixels)),
            per_sample((1, 2, fine_pixels)),
            whole((2, half, fine_pixels)),
            whole((2, half, fine_pixels)),
        ],
        out_specs=[
            per_sample((1, 2, half, fine_pixels)),
            per_sample((1, 2, half, fine_pixels)),
        ],
        out_shape=[
            jax.ShapeDtypeStruct((samples, 2, half, fine_pixels), jnp.bfloat16),
            jax.ShapeDtypeStruct((samples, 2, half, fine_pixels), jnp.float32),
        ],
        interpret=INTERPRET,
    )(refine_sqrt.astype(jnp.float32).reshape(-1), density, local_cum, carries, by_parity(counts), by_parity(stars))
    return from_parity(extinct), from_parity(grad)


def shards(
    coarse_field, excitations, refine_weights, refine_sqrt, halo_index, star_extinction, star_counts
):
    samples, coarse_shells, coarse_pixels = coarse_field.shape
    fine_shells = 2 * coarse_shells
    fine_pixels = 4 * coarse_pixels
    dist_count = lax.axis_size("dist")
    dist_rank = lax.axis_index("dist")
    all_shells = fine_shells * dist_count
    blocked = coarse_field.reshape(samples, coarse_shells, coarse_pixels // BAND, BAND)
    extended = with_halo(blocked, (("dist", 1), ("sky", 2)), 1)
    extended = extended.reshape(samples, coarse_shells + 2, coarse_pixels + 2 * BAND)
    shells = dist_rank * fine_shells + jnp.arange(fine_shells, dtype=jnp.int32)
    middle = (shells.astype(jnp.float32) + 0.5) / all_shells
    widths = 3.0 * jnp.exp(3.0 * middle - 3.0) / all_shells
    counts = star_counts.astype(jnp.float32)
    density, local_cum, sums = local_forward(
        extended, halo_index, excitations, refine_weights, refine_sqrt, counts, star_extinction, widths
    )
    weight = jnp.sum(counts, axis=0, keepdims=True)
    carry_in, carry_out = block_carries(sums[:, 0], sums[:, 1], weight, "dist")
    carries = jnp.stack([carry_in, carry_out], axis=1)
    return local_backward(refine_sqrt, density, local_cum, carries, counts, star_extinction)


def solution(mesh):
    placed = (
        P(None, "dist", "sky"),
        P(None, "dist", "sky"),
        P(),
        P(),
        P(None, "sky"),
        P("dist", "sky"),
        P("dist", "sky"),
    )
    return jax.shard_map(
        shards,
        mesh=mesh,
        in_specs=placed,
        out_specs=(P(None, "dist", "sky"), P(None, "dist", "sky")),
        check_vma=False,
    )
```

```python
import jax
import jax.numpy as jnp
from jax import lax
from jax.experimental import pallas as pl
from jax.experimental.pallas import tpu as pltpu
from jax.sharding import PartitionSpec as P

BAND = 128


exact_mode = lax.Precision.HIGHEST


def with_halo(block, band):
    dist = lax.axis_size("dist")
    sky = lax.axis_size("sky")

    def moved(piece, step_dist, step_sky):
        pairs = []
        for d in range(dist):
            for s in range(sky):
                if 0 <= d + step_dist < dist and 0 <= s + step_sky < sky:
                    pairs.append((d * sky + s, (d + step_dist) * sky + s + step_sky))
        return lax.ppermute(piece, ("dist", "sky"), pairs)

    last_row = block[:, -1:]
    first_row = block[:, :1]
    rows_low = moved(last_row, 1, 0)
    rows_high = moved(first_row, -1, 0)
    left = moved(block[:, :, -band:], 0, 1)
    right = moved(block[:, :, :band], 0, -1)
    corner_ll = moved(last_row[:, :, -band:], 1, 1)
    corner_lh = moved(last_row[:, :, :band], 1, -1)
    corner_hl = moved(first_row[:, :, -band:], -1, 1)
    corner_hh = moved(first_row[:, :, :band], -1, -1)
    low = jnp.concatenate([corner_ll, rows_low, corner_lh], axis=2)
    middle = jnp.concatenate([left, block, right], axis=2)
    high = jnp.concatenate([corner_hl, rows_high, corner_hh], axis=2)
    return jnp.concatenate([low, middle, high], axis=1)


def block_carries(totals, partial, weight, axis):
    count = lax.axis_size(axis)
    rows, pixels = totals.shape
    width = pixels // count
    packed = jnp.concatenate([totals, partial, weight], axis=0)
    packed = packed.reshape(packed.shape[0], count, width).transpose(1, 0, 2)
    mine = lax.all_to_all(packed, axis, 0, 0, tiled=True)
    block_totals = mine[:, :rows]
    block_partial = mine[:, rows : 2 * rows]
    block_weight = mine[:, 2 * rows :]
    blocks, height, width = block_totals.shape
    order = jnp.arange(blocks, dtype=jnp.int32)
    earlier = (order[None, :] < order[:, None]).astype(jnp.float32)
    flat = lambda values: values.reshape(blocks, -1)
    carry_in = jnp.dot(earlier, flat(block_totals), precision=exact_mode).reshape(blocks, height, width)
    block_misfit = block_partial + block_weight * carry_in
    carry_out = jnp.dot(earlier.T, flat(block_misfit), precision=exact_mode).reshape(blocks, height, width)
    back = lax.all_to_all(jnp.concatenate([carry_in, carry_out], axis=1), axis, 0, 0, tiled=True)
    back = back.transpose(1, 0, 2).reshape(2 * rows, pixels)
    return back[:rows], back[rows:]


def split_three(values):
    high = lax.reduce_precision(values, exponent_bits=8, mantissa_bits=7)
    rest = values - high
    middle = lax.reduce_precision(rest, exponent_bits=8, mantissa_bits=7)
    low = rest - middle
    return jnp.stack([high, middle, low]).astype(jnp.bfloat16)


def gather_nearby(extended, halo_index):
    samples, shells, _ = extended.shape
    slots, pixels = halo_index.shape
    blocks = pixels // BAND
    window = 3 * BAND
    windows = jnp.stack(
        [extended[:, :, b * BAND : b * BAND + window] for b in range(blocks)]
    ).reshape(blocks, samples * shells, window)
    pieces = split_three(windows).transpose(1, 0, 2, 3).reshape(blocks, 3 * samples * shells, window)
    starts = (jnp.arange(blocks, dtype=jnp.int32) * BAND)[None, :, None]
    local = halo_index.reshape(slots, blocks, BAND) - starts
    spots = jnp.arange(window, dtype=jnp.int32)[None, :, None, None]
    onehot = (local.transpose(1, 0, 2)[:, None] == spots).astype(jnp.bfloat16)
    onehot = onehot.reshape(blocks, window, slots * BAND)
    picked = jnp.einsum("bxw,bwn->bxn", pieces, onehot, preferred_element_type=jnp.float32)
    picked = picked.reshape(blocks, 3, samples, shells, slots, BAND)
    picked = (picked[:, 0] + picked[:, 1]) + picked[:, 2]
    return picked.transpose(1, 2, 3, 0, 4).reshape(samples, shells, slots, pixels)


INTERPRET = False
LANES = 128


def shifted(values, amount, toward_end):
    rows = values.shape[0]
    row = lax.broadcasted_iota(jnp.int32, values.shape, 0)
    forward = pltpu.roll(values, amount, 0)
    backward = pltpu.roll(values, rows - amount, 0)
    probe = pltpu.roll(row, amount, 0)
    plain = probe == jnp.where(row >= amount, row - amount, row + rows - amount)
    if toward_end:
        moved = jnp.where(plain, forward, backward)
        return jnp.where(row >= amount, moved, 0.0)
    moved = jnp.where(plain, backward, forward)
    return jnp.where(row < rows - amount, moved, 0.0)


def running(values, toward_end):
    for amount in (1, 2, 4):
        values = values + shifted(values, amount, toward_end)
    return values


def forward_kernel(
    weights_ref, sqrt_ref, pieces_ref, onehot_ref, excite_ref, counts_ref, stars_ref, widths_ref,
    density_ref, local_ref, sums_ref, picked_ref,
):
    blocks = onehot_ref.shape[0]
    slots = onehot_ref.shape[2] // LANES
    tile = blocks * LANES

    def one_block(b, carry):
        picked = jnp.dot(pieces_ref[0, b], onehot_ref[b], preferred_element_type=jnp.float32)
        picked_ref[...] = (picked[0:16] + picked[16:32]) + picked[32:48]
        acc = {}
        for t in range(2):
            for q in range(4):
                total = None
                for u in range(2):
                    for r in range(4):
                        lanes = pl.ds(pl.multiple_of(r * tile + b * LANES, LANES), LANES)
                        term = sqrt_ref[((t * 4 + q) * 2 + u) * 4 + r] * excite_ref[0, u, :, lanes].astype(jnp.float32)
                        total = term if total is None else total + term
                acc[t, q] = total
        for j in range(3):
            for m in range(slots):
                near = picked_ref[pl.ds(j, 8), pl.ds(m * LANES, LANES)]
                for t in range(2):
                    for q in range(4):
                        acc[t, q] = acc[t, q] + weights_ref[((t * 4 + q) * 3 + j) * 9 + m] * near
        for q in range(4):
            lanes = pl.ds(pl.multiple_of(q * tile + b * LANES, LANES), LANES)
            even = jnp.exp(acc[0, q]) * widths_ref[0]
            odd = jnp.exp(acc[1, q]) * widths_ref[1]
            density_ref[0, 0, :, lanes] = even
            density_ref[0, 1, :, lanes] = odd
            through = running(even + odd, True)
            before = shifted(through, 1, True) + even
            local_ref[0, 0, :, lanes] = before
            local_ref[0, 1, :, lanes] = through
            misfit = counts_ref[0, :, lanes] * (before - stars_ref[0, :, lanes]) + counts_ref[1, :, lanes] * (
                through - stars_ref[1, :, lanes]
            )
            sums_ref[0, 0:1, lanes] = through[7:8]
            sums_ref[0, 1:2, lanes] = jnp.sum(misfit, axis=0, keepdims=True)
        return carry

    lax.fori_loop(0, blocks, one_block, 0)


def backward_kernel(
    sqrt_ref, density_ref, local_ref, carries_ref, counts_ref, stars_ref, extinct_ref, grad_ref
):
    tile = density_ref.shape[3] // 4
    blocks = tile // LANES

    def one_block(b, carry):
        flow = {}
        for q in range(4):
            lanes = pl.ds(pl.multiple_of(q * tile + b * LANES, LANES), LANES)
            into = carries_ref[0, 0:1, lanes]
            past = carries_ref[0, 1:2, lanes]
            even = local_ref[0, 0, :, lanes] + into
            odd = local_ref[0, 1, :, lanes] + into
            extinct_ref[0, 0, :, lanes] = even.astype(extinct_ref.dtype)
            extinct_ref[0, 1, :, lanes] = odd.astype(extinct_ref.dtype)
            miss_even = counts_ref[0, :, lanes] * (even - stars_ref[0, :, lanes])
            miss_odd = counts_ref[1, :, lanes] * (odd - stars_ref[1, :, lanes])
            behind = running(miss_even + miss_odd, False)
            back_even = behind + past
            back_odd = (shifted(behind, 1, False) + miss_odd) + past
            flow[0, q] = density_ref[0, 0, :, lanes] * back_even
            flow[1, q] = density_ref[0, 1, :, lanes] * back_odd
        for u in range(2):
            for r in range(4):
                total = None
                for t in range(2):
                    for q in range(4):
                        term = sqrt_ref[((t * 4 + q) * 2 + u) * 4 + r] * flow[t, q]
                        total = term if total is None else total + term
                lanes = pl.ds(pl.multiple_of(r * tile + b * LANES, LANES), LANES)
                grad_ref[0, u, :, lanes] = total
        return carry

    lax.fori_loop(0, blocks, one_block, 0)


def by_parity(values):
    lead = values.shape[:-2]
    shells, width = values.shape[-2:]
    values = values.reshape(lead + (shells // 2, 2, width))
    return jnp.swapaxes(values, -2, -3)


def from_parity(values):
    lead = values.shape[:-3]
    _, shells, width = values.shape[-3:]
    return jnp.swapaxes(values, -2, -3).reshape(lead + (2 * shells, width))


def tiles(values):
    flat = values.reshape(-1)
    return jnp.broadcast_to(flat[:, None, None], (flat.shape[0], 8, LANES))


def local_forward(extended, halo_index, excitations, refine_weights, refine_sqrt, counts, stars, widths):
    samples, shells, _ = extended.shape
    slots, pixels = halo_index.shape
    blocks = pixels // BAND
    window = 3 * BAND
    fine_shells = excitations.shape[1]
    fine_pixels = excitations.shape[2]
    windows = jnp.stack(
        [extended[:, :, b * BAND : b * BAND + window] for b in range(blocks)], axis=1
    )
    pieces = split_three(windows)
    pieces = jnp.pad(pieces, ((0, 0), (0, 0), (0, 0), (0, 16 - shells), (0, 0)))
    pieces = pieces.transpose(1, 2, 0, 3, 4).reshape(samples, blocks, 3 * 16, window)
    starts = (jnp.arange(blocks, dtype=jnp.int32) * BAND)[None, :, None]
    local = halo_index.reshape(slots, blocks, BAND) - starts
    spots = jnp.arange(window, dtype=jnp.int32)[None, :, None, None]
    onehot = (local.transpose(1, 0, 2)[:, None] == spots).astype(jnp.bfloat16)
    onehot = onehot.reshape(blocks, window, slots * BAND)
    excite = by_parity(excitations)
    half = fine_shells // 2
    wide = jnp.broadcast_to(widths.reshape(half, 2).T[:, :, None], (2, half, LANES))
    smem = pl.BlockSpec(memory_space=pltpu.SMEM)
    whole = lambda shape: pl.BlockSpec(shape, lambda k: (0,) * len(shape))
    per_sample = lambda shape: pl.BlockSpec(shape, lambda k: (k,) + (0,) * (len(shape) - 1))
    return pl.pallas_call(
        forward_kernel,
        grid=(samples,),
        in_specs=[
            whole((2 * 4 * 3 * slots, 8, LANES)),
            whole((2 * 4 * 2 * 4, 8, LANES)),
            per_sample((1, blocks, 48, window)),
            whole((blocks, window, slots * BAND)),
            per_sample((1, 2, half, fine_pixels)),
            whole((2, half, fine_pixels)),
            whole((2, half, fine_pixels)),
            whole((2, half, LANES)),
        ],
        out_specs=[
            per_sample((1, 2, half, fine_pixels)),
            per_sample((1, 2, half, fine_pixels)),
            per_sample((1, 2, fine_pixels)),
        ],
        out_shape=[
            jax.ShapeDtypeStruct((samples, 2, half, fine_pixels), jnp.float32),
            jax.ShapeDtypeStruct((samples, 2, half, fine_pixels), jnp.float32),
            jax.ShapeDtypeStruct((samples, 2, fine_pixels), jnp.float32),
        ],
        scratch_shapes=[pltpu.VMEM((16, slots * BAND), jnp.float32)],
        interpret=INTERPRET,
    )(
        tiles(refine_weights),
        tiles(refine_sqrt.astype(jnp.float32)),
        pieces,
        onehot,
        excite,
        by_parity(counts),
        by_parity(stars),
        wide,
    )


def local_backward(refine_sqrt, density, local_cum, carries, counts, stars):
    samples, _, half, fine_pixels = density.shape
    smem = pl.BlockSpec(memory_space=pltpu.SMEM)
    whole = lambda shape: pl.BlockSpec(shape, lambda k: (0,) * len(shape))
    per_sample = lambda shape: pl.BlockSpec(shape, lambda k: (k,) + (0,) * (len(shape) - 1))
    extinct, grad = pl.pallas_call(
        backward_kernel,
        grid=(samples,),
        in_specs=[
            smem,
            per_sample((1, 2, half, fine_pixels)),
            per_sample((1, 2, half, fine_pixels)),
            per_sample((1, 2, fine_pixels)),
            whole((2, half, fine_pixels)),
            whole((2, half, fine_pixels)),
        ],
        out_specs=[
            per_sample((1, 2, half, fine_pixels)),
            per_sample((1, 2, half, fine_pixels)),
        ],
        out_shape=[
            jax.ShapeDtypeStruct((samples, 2, half, fine_pixels), jnp.bfloat16),
            jax.ShapeDtypeStruct((samples, 2, half, fine_pixels), jnp.float32),
        ],
        interpret=INTERPRET,
    )(refine_sqrt.astype(jnp.float32).reshape(-1), density, local_cum, carries, by_parity(counts), by_parity(stars))
    return from_parity(extinct), from_parity(grad)


def shards(
    coarse_field, excitations, refine_weights, refine_sqrt, halo_index, star_extinction, star_counts
):
    samples, coarse_shells, coarse_pixels = coarse_field.shape
    fine_shells = 2 * coarse_shells
    fine_pixels = 4 * coarse_pixels
    dist_count = lax.axis_size("dist")
    dist_rank = lax.axis_index("dist")
    all_shells = fine_shells * dist_count
    extended = with_halo(coarse_field, BAND)
    shells = dist_rank * fine_shells + jnp.arange(fine_shells, dtype=jnp.int32)
    middle = (shells.astype(jnp.float32) + 0.5) / all_shells
    widths = 3.0 * jnp.exp(3.0 * middle - 3.0) / all_shells
    counts = star_counts.astype(jnp.float32)
    density, local_cum, sums = local_forward(
        extended, halo_index, excitations, refine_weights, refine_sqrt, counts, star_extinction, widths
    )
    weight = jnp.sum(counts, axis=0, keepdims=True)
    carry_in, carry_out = block_carries(sums[:, 0], sums[:, 1], weight, "dist")
    carries = jnp.stack([carry_in, carry_out], axis=1)
    return local_backward(refine_sqrt, density, local_cum, carries, counts, star_extinction)


def solution(mesh):
    placed = (
        P(None, "dist", "sky"),
        P(None, "dist", "sky"),
        P(),
        P(),
        P(None, "sky"),
        P("dist", "sky"),
        P("dist", "sky"),
    )
    return jax.shard_map(
        shards,
        mesh=mesh,
        in_specs=placed,
        out_specs=(P(None, "dist", "sky"), P(None, "dist", "sky")),
        check_vma=False,
    )
```

```python
import jax
import jax.numpy as jnp
from jax import lax
from jax.experimental import pallas as pl
from jax.experimental.pallas import tpu as pltpu
from jax.sharding import PartitionSpec as P

BAND = 128


exact_mode = lax.Precision.HIGHEST


def with_halo(block, sides, width):
    for axis, dim in sides:
        count = lax.axis_size(axis)
        forward = [(i, i + 1) for i in range(count - 1)]
        backward = [(target, source) for source, target in forward]
        low = lax.ppermute(
            lax.slice_in_dim(block, block.shape[dim] - width, None, axis=dim), axis, forward
        )
        high = lax.ppermute(lax.slice_in_dim(block, 0, width, axis=dim), axis, backward)
        block = jnp.concatenate([low, block, high], axis=dim)
    return block


def block_carries(totals, partial, weight, axis):
    count = lax.axis_size(axis)
    rows, pixels = totals.shape
    width = pixels // count
    packed = jnp.concatenate([totals, partial, weight], axis=0)
    packed = packed.reshape(packed.shape[0], count, width).transpose(1, 0, 2)
    mine = lax.all_to_all(packed, axis, 0, 0, tiled=True)
    block_totals = mine[:, :rows]
    block_partial = mine[:, rows : 2 * rows]
    block_weight = mine[:, 2 * rows :]
    blocks, height, width = block_totals.shape
    order = jnp.arange(blocks, dtype=jnp.int32)
    earlier = (order[None, :] < order[:, None]).astype(jnp.float32)
    flat = lambda values: values.reshape(blocks, -1)
    carry_in = jnp.dot(earlier, flat(block_totals), precision=exact_mode).reshape(blocks, height, width)
    block_misfit = block_partial + block_weight * carry_in
    carry_out = jnp.dot(earlier.T, flat(block_misfit), precision=exact_mode).reshape(blocks, height, width)
    back = lax.all_to_all(jnp.concatenate([carry_in, carry_out], axis=1), axis, 0, 0, tiled=True)
    back = back.transpose(1, 0, 2).reshape(2 * rows, pixels)
    return back[:rows], back[rows:]


def split_three(values):
    high = lax.reduce_precision(values, exponent_bits=8, mantissa_bits=7)
    rest = values - high
    middle = lax.reduce_precision(rest, exponent_bits=8, mantissa_bits=7)
    low = rest - middle
    return jnp.stack([high, middle, low]).astype(jnp.bfloat16)


def gather_nearby(extended, halo_index):
    samples, shells, _ = extended.shape
    slots, pixels = halo_index.shape
    blocks = pixels // BAND
    window = 3 * BAND
    windows = jnp.stack(
        [extended[:, :, b * BAND : b * BAND + window] for b in range(blocks)]
    ).reshape(blocks, samples * shells, window)
    pieces = split_three(windows).transpose(1, 0, 2, 3).reshape(blocks, 3 * samples * shells, window)
    starts = (jnp.arange(blocks, dtype=jnp.int32) * BAND)[None, :, None]
    local = halo_index.reshape(slots, blocks, BAND) - starts
    spots = jnp.arange(window, dtype=jnp.int32)[None, :, None, None]
    onehot = (local.transpose(1, 0, 2)[:, None] == spots).astype(jnp.bfloat16)
    onehot = onehot.reshape(blocks, window, slots * BAND)
    picked = jnp.einsum("bxw,bwn->bxn", pieces, onehot, preferred_element_type=jnp.float32)
    picked = picked.reshape(blocks, 3, samples, shells, slots, BAND)
    picked = (picked[:, 0] + picked[:, 1]) + picked[:, 2]
    return picked.transpose(1, 2, 3, 0, 4).reshape(samples, shells, slots, pixels)


INTERPRET = False
LANES = 128


def shifted(values, amount, toward_end):
    rows = values.shape[0]
    row = lax.broadcasted_iota(jnp.int32, values.shape, 0)
    forward = pltpu.roll(values, amount, 0)
    backward = pltpu.roll(values, rows - amount, 0)
    probe = pltpu.roll(row, amount, 0)
    plain = probe == jnp.where(row >= amount, row - amount, row + rows - amount)
    if toward_end:
        moved = jnp.where(plain, forward, backward)
        return jnp.where(row >= amount, moved, 0.0)
    moved = jnp.where(plain, backward, forward)
    return jnp.where(row < rows - amount, moved, 0.0)


def running(values, toward_end):
    for amount in (1, 2, 4):
        values = values + shifted(values, amount, toward_end)
    return values


def forward_kernel(
    weights_ref, sqrt_ref, pieces_ref, onehot_ref, excite_ref, counts_ref, stars_ref, widths_ref,
    density_ref, local_ref, sums_ref, picked_ref,
):
    blocks = onehot_ref.shape[0]
    slots = onehot_ref.shape[2] // LANES
    tile = blocks * LANES

    def one_block(b, carry):
        picked = jnp.dot(pieces_ref[0, b], onehot_ref[b], preferred_element_type=jnp.float32)
        picked_ref[...] = (picked[0:16] + picked[16:32]) + picked[32:48]
        acc = {}
        for t in range(2):
            for q in range(4):
                total = None
                for u in range(2):
                    for r in range(4):
                        lanes = pl.ds(pl.multiple_of(r * tile + b * LANES, LANES), LANES)
                        term = sqrt_ref[((t * 4 + q) * 2 + u) * 4 + r] * excite_ref[0, u, :, lanes].astype(jnp.float32)
                        total = term if total is None else total + term
                acc[t, q] = total
        for j in range(3):
            for m in range(slots):
                near = picked_ref[pl.ds(j, 8), pl.ds(m * LANES, LANES)]
                for t in range(2):
                    for q in range(4):
                        acc[t, q] = acc[t, q] + weights_ref[((t * 4 + q) * 3 + j) * 9 + m] * near
        for q in range(4):
            lanes = pl.ds(pl.multiple_of(q * tile + b * LANES, LANES), LANES)
            even = jnp.exp(acc[0, q]) * widths_ref[0]
            odd = jnp.exp(acc[1, q]) * widths_ref[1]
            density_ref[0, 0, :, lanes] = even
            density_ref[0, 1, :, lanes] = odd
            through = running(even + odd, True)
            before = shifted(through, 1, True) + even
            local_ref[0, 0, :, lanes] = before
            local_ref[0, 1, :, lanes] = through
            misfit = counts_ref[0, :, lanes] * (before - stars_ref[0, :, lanes]) + counts_ref[1, :, lanes] * (
                through - stars_ref[1, :, lanes]
            )
            sums_ref[0, 0:1, lanes] = through[7:8]
            sums_ref[0, 1:2, lanes] = jnp.sum(misfit, axis=0, keepdims=True)
        return carry

    lax.fori_loop(0, blocks, one_block, 0, unroll=8)


def backward_kernel(
    sqrt_ref, density_ref, local_ref, carries_ref, counts_ref, stars_ref, extinct_ref, grad_ref
):
    tile = density_ref.shape[3] // 4
    blocks = tile // LANES

    def one_block(b, carry):
        flow = {}
        for q in range(4):
            lanes = pl.ds(pl.multiple_of(q * tile + b * LANES, LANES), LANES)
            into = carries_ref[0, 0:1, lanes]
            past = carries_ref[0, 1:2, lanes]
            even = local_ref[0, 0, :, lanes] + into
            odd = local_ref[0, 1, :, lanes] + into
            extinct_ref[0, 0, :, lanes] = even.astype(extinct_ref.dtype)
            extinct_ref[0, 1, :, lanes] = odd.astype(extinct_ref.dtype)
            miss_even = counts_ref[0, :, lanes] * (even - stars_ref[0, :, lanes])
            miss_odd = counts_ref[1, :, lanes] * (odd - stars_ref[1, :, lanes])
            behind = running(miss_even + miss_odd, False)
            back_even = behind + past
            back_odd = (shifted(behind, 1, False) + miss_odd) + past
            flow[0, q] = density_ref[0, 0, :, lanes] * back_even
            flow[1, q] = density_ref[0, 1, :, lanes] * back_odd
        for u in range(2):
            for r in range(4):
                total = None
                for t in range(2):
                    for q in range(4):
                        term = sqrt_ref[((t * 4 + q) * 2 + u) * 4 + r] * flow[t, q]
                        total = term if total is None else total + term
                lanes = pl.ds(pl.multiple_of(r * tile + b * LANES, LANES), LANES)
                grad_ref[0, u, :, lanes] = total
        return carry

    lax.fori_loop(0, blocks, one_block, 0, unroll=8)


def by_parity(values):
    lead = values.shape[:-2]
    shells, width = values.shape[-2:]
    values = values.reshape(lead + (shells // 2, 2, width))
    return jnp.swapaxes(values, -2, -3)


def from_parity(values):
    lead = values.shape[:-3]
    _, shells, width = values.shape[-3:]
    return jnp.swapaxes(values, -2, -3).reshape(lead + (2 * shells, width))


def tiles(values):
    flat = values.reshape(-1)
    return jnp.broadcast_to(flat[:, None, None], (flat.shape[0], 8, LANES))


def local_forward(extended, halo_index, excitations, refine_weights, refine_sqrt, counts, stars, widths):
    samples, shells, _ = extended.shape
    slots, pixels = halo_index.shape
    blocks = pixels // BAND
    window = 3 * BAND
    fine_shells = excitations.shape[1]
    fine_pixels = excitations.shape[2]
    windows = jnp.stack(
        [extended[:, :, b * BAND : b * BAND + window] for b in range(blocks)], axis=1
    )
    pieces = split_three(windows)
    pieces = jnp.pad(pieces, ((0, 0), (0, 0), (0, 0), (0, 16 - shells), (0, 0)))
    pieces = pieces.transpose(1, 2, 0, 3, 4).reshape(samples, blocks, 3 * 16, window)
    starts = (jnp.arange(blocks, dtype=jnp.int32) * BAND)[None, :, None]
    local = halo_index.reshape(slots, blocks, BAND) - starts
    spots = jnp.arange(window, dtype=jnp.int32)[None, :, None, None]
    onehot = (local.transpose(1, 0, 2)[:, None] == spots).astype(jnp.bfloat16)
    onehot = onehot.reshape(blocks, window, slots * BAND)
    excite = by_parity(excitations)
    half = fine_shells // 2
    wide = jnp.broadcast_to(widths.reshape(half, 2).T[:, :, None], (2, half, LANES))
    smem = pl.BlockSpec(memory_space=pltpu.SMEM)
    whole = lambda shape: pl.BlockSpec(shape, lambda k: (0,) * len(shape))
    per_sample = lambda shape: pl.BlockSpec(shape, lambda k: (k,) + (0,) * (len(shape) - 1))
    return pl.pallas_call(
        forward_kernel,
        grid=(samples,),
        in_specs=[
            whole((2 * 4 * 3 * slots, 8, LANES)),
            whole((2 * 4 * 2 * 4, 8, LANES)),
            per_sample((1, blocks, 48, window)),
            whole((blocks, window, slots * BAND)),
            per_sample((1, 2, half, fine_pixels)),
            whole((2, half, fine_pixels)),
            whole((2, half, fine_pixels)),
            whole((2, half, LANES)),
        ],
        out_specs=[
            per_sample((1, 2, half, fine_pixels)),
            per_sample((1, 2, half, fine_pixels)),
            per_sample((1, 2, fine_pixels)),
        ],
        out_shape=[
            jax.ShapeDtypeStruct((samples, 2, half, fine_pixels), jnp.float32),
            jax.ShapeDtypeStruct((samples, 2, half, fine_pixels), jnp.float32),
            jax.ShapeDtypeStruct((samples, 2, fine_pixels), jnp.float32),
        ],
        scratch_shapes=[pltpu.VMEM((16, slots * BAND), jnp.float32)],
        interpret=INTERPRET,
    )(
        tiles(refine_weights),
        tiles(refine_sqrt.astype(jnp.float32)),
        pieces,
        onehot,
        excite,
        by_parity(counts),
        by_parity(stars),
        wide,
    )


def local_backward(refine_sqrt, density, local_cum, carries, counts, stars):
    samples, _, half, fine_pixels = density.shape
    smem = pl.BlockSpec(memory_space=pltpu.SMEM)
    whole = lambda shape: pl.BlockSpec(shape, lambda k: (0,) * len(shape))
    per_sample = lambda shape: pl.BlockSpec(shape, lambda k: (k,) + (0,) * (len(shape) - 1))
    extinct, grad = pl.pallas_call(
        backward_kernel,
        grid=(samples,),
        in_specs=[
            smem,
            per_sample((1, 2, half, fine_pixels)),
            per_sample((1, 2, half, fine_pixels)),
            per_sample((1, 2, fine_pixels)),
            whole((2, half, fine_pixels)),
            whole((2, half, fine_pixels)),
        ],
        out_specs=[
            per_sample((1, 2, half, fine_pixels)),
            per_sample((1, 2, half, fine_pixels)),
        ],
        out_shape=[
            jax.ShapeDtypeStruct((samples, 2, half, fine_pixels), jnp.bfloat16),
            jax.ShapeDtypeStruct((samples, 2, half, fine_pixels), jnp.float32),
        ],
        interpret=INTERPRET,
    )(refine_sqrt.astype(jnp.float32).reshape(-1), density, local_cum, carries, by_parity(counts), by_parity(stars))
    return from_parity(extinct), from_parity(grad)


def shards(
    coarse_field, excitations, refine_weights, refine_sqrt, halo_index, star_extinction, star_counts
):
    samples, coarse_shells, coarse_pixels = coarse_field.shape
    fine_shells = 2 * coarse_shells
    fine_pixels = 4 * coarse_pixels
    dist_count = lax.axis_size("dist")
    dist_rank = lax.axis_index("dist")
    all_shells = fine_shells * dist_count
    blocked = coarse_field.reshape(samples, coarse_shells, coarse_pixels // BAND, BAND)
    extended = with_halo(blocked, (("dist", 1), ("sky", 2)), 1)
    extended = extended.reshape(samples, coarse_shells + 2, coarse_pixels + 2 * BAND)
    shells = dist_rank * fine_shells + jnp.arange(fine_shells, dtype=jnp.int32)
    middle = (shells.astype(jnp.float32) + 0.5) / all_shells
    widths = 3.0 * jnp.exp(3.0 * middle - 3.0) / all_shells
    counts = star_counts.astype(jnp.float32)
    density, local_cum, sums = local_forward(
        extended, halo_index, excitations, refine_weights, refine_sqrt, counts, star_extinction, widths
    )
    weight = jnp.sum(counts, axis=0, keepdims=True)
    carry_in, carry_out = block_carries(sums[:, 0], sums[:, 1], weight, "dist")
    carries = jnp.stack([carry_in, carry_out], axis=1)
    return local_backward(refine_sqrt, density, local_cum, carries, counts, star_extinction)


def solution(mesh):
    placed = (
        P(None, "dist", "sky"),
        P(None, "dist", "sky"),
        P(),
        P(),
        P(None, "sky"),
        P("dist", "sky"),
        P("dist", "sky"),
    )
    return jax.shard_map(
        shards,
        mesh=mesh,
        in_specs=placed,
        out_specs=(P(None, "dist", "sky"), P(None, "dist", "sky")),
        check_vma=False,
    )
```

```python
import jax
import jax.numpy as jnp
from jax import lax
from jax.experimental import pallas as pl
from jax.experimental.pallas import tpu as pltpu
from jax.sharding import PartitionSpec as P

BAND = 128


exact_mode = lax.Precision.HIGHEST


def with_halo(block, sides, width):
    for axis, dim in sides:
        count = lax.axis_size(axis)
        forward = [(i, i + 1) for i in range(count - 1)]
        backward = [(target, source) for source, target in forward]
        low = lax.ppermute(
            lax.slice_in_dim(block, block.shape[dim] - width, None, axis=dim), axis, forward
        )
        high = lax.ppermute(lax.slice_in_dim(block, 0, width, axis=dim), axis, backward)
        block = jnp.concatenate([low, block, high], axis=dim)
    return block


def block_carries(totals, partial, weight, axis):
    count = lax.axis_size(axis)
    rows, pixels = totals.shape
    width = pixels // count
    packed = jnp.concatenate([totals, partial, weight], axis=0)
    packed = packed.reshape(packed.shape[0], count, width).transpose(1, 0, 2)
    mine = lax.all_to_all(packed, axis, 0, 0, tiled=True)
    block_totals = mine[:, :rows]
    block_partial = mine[:, rows : 2 * rows]
    block_weight = mine[:, 2 * rows :]
    blocks, height, width = block_totals.shape
    order = jnp.arange(blocks, dtype=jnp.int32)
    earlier = (order[None, :] < order[:, None]).astype(jnp.float32)
    flat = lambda values: values.reshape(blocks, -1)
    carry_in = jnp.dot(earlier, flat(block_totals), precision=exact_mode).reshape(blocks, height, width)
    block_misfit = block_partial + block_weight * carry_in
    carry_out = jnp.dot(earlier.T, flat(block_misfit), precision=exact_mode).reshape(blocks, height, width)
    back = lax.all_to_all(jnp.concatenate([carry_in, carry_out], axis=1), axis, 0, 0, tiled=True)
    back = back.transpose(1, 0, 2).reshape(2 * rows, pixels)
    return back[:rows], back[rows:]


def split_three(values):
    high = lax.reduce_precision(values, exponent_bits=8, mantissa_bits=7)
    rest = values - high
    middle = lax.reduce_precision(rest, exponent_bits=8, mantissa_bits=7)
    low = rest - middle
    return jnp.stack([high, middle, low]).astype(jnp.bfloat16)


def gather_nearby(extended, halo_index):
    samples, shells, _ = extended.shape
    slots, pixels = halo_index.shape
    blocks = pixels // BAND
    window = 3 * BAND
    windows = jnp.stack(
        [extended[:, :, b * BAND : b * BAND + window] for b in range(blocks)]
    ).reshape(blocks, samples * shells, window)
    pieces = split_three(windows).transpose(1, 0, 2, 3).reshape(blocks, 3 * samples * shells, window)
    starts = (jnp.arange(blocks, dtype=jnp.int32) * BAND)[None, :, None]
    local = halo_index.reshape(slots, blocks, BAND) - starts
    spots = jnp.arange(window, dtype=jnp.int32)[None, :, None, None]
    onehot = (local.transpose(1, 0, 2)[:, None] == spots).astype(jnp.bfloat16)
    onehot = onehot.reshape(blocks, window, slots * BAND)
    picked = jnp.einsum("bxw,bwn->bxn", pieces, onehot, preferred_element_type=jnp.float32)
    picked = picked.reshape(blocks, 3, samples, shells, slots, BAND)
    picked = (picked[:, 0] + picked[:, 1]) + picked[:, 2]
    return picked.transpose(1, 2, 3, 0, 4).reshape(samples, shells, slots, pixels)


INTERPRET = False
LANES = 128


def shifted(values, amount, toward_end):
    rows = values.shape[0]
    row = lax.broadcasted_iota(jnp.int32, values.shape, 0)
    forward = pltpu.roll(values, amount, 0)
    backward = pltpu.roll(values, rows - amount, 0)
    probe = pltpu.roll(row, amount, 0)
    plain = probe == jnp.where(row >= amount, row - amount, row + rows - amount)
    if toward_end:
        moved = jnp.where(plain, forward, backward)
        return jnp.where(row >= amount, moved, 0.0)
    moved = jnp.where(plain, backward, forward)
    return jnp.where(row < rows - amount, moved, 0.0)


def running(values, toward_end):
    for amount in (1, 2, 4):
        values = values + shifted(values, amount, toward_end)
    return values


def forward_kernel(
    weights_ref, sqrt_ref, pieces_ref, onehot_ref, excite_ref, counts_ref, stars_ref, widths_ref,
    density_ref, local_ref, sums_ref, picked_ref, weight_tiles, sqrt_tiles, width_tiles,
):
    blocks = onehot_ref.shape[0]
    slots = onehot_ref.shape[2] // LANES
    tile = blocks * LANES

    @pl.when(pl.program_id(0) == 0)
    def _():
        for index in range(weight_tiles.shape[0]):
            weight_tiles[index] = jnp.full((8, LANES), weights_ref[index], jnp.float32)
        for index in range(sqrt_tiles.shape[0]):
            sqrt_tiles[index] = jnp.full((8, LANES), sqrt_ref[index], jnp.float32)
        row = lax.broadcasted_iota(jnp.int32, (8, LANES), 0)
        for t in range(2):
            column = jnp.zeros((8, LANES), jnp.float32)
            for s in range(8):
                column = jnp.where(row == s, widths_ref[2 * s + t], column)
            width_tiles[t] = column

    def one_block(b, carry):
        picked = jnp.dot(pieces_ref[0, b], onehot_ref[b], preferred_element_type=jnp.float32)
        picked_ref[...] = (picked[0:16] + picked[16:32]) + picked[32:48]
        acc = {}
        for t in range(2):
            for q in range(4):
                total = None
                for u in range(2):
                    for r in range(4):
                        lanes = pl.ds(pl.multiple_of(r * tile + b * LANES, LANES), LANES)
                        term = sqrt_tiles[((t * 4 + q) * 2 + u) * 4 + r] * excite_ref[0, u, :, lanes].astype(jnp.float32)
                        total = term if total is None else total + term
                acc[t, q] = total
        for j in range(3):
            for m in range(slots):
                near = picked_ref[pl.ds(j, 8), pl.ds(m * LANES, LANES)]
                for t in range(2):
                    for q in range(4):
                        acc[t, q] = acc[t, q] + weight_tiles[((t * 4 + q) * 3 + j) * 9 + m] * near
        for q in range(4):
            lanes = pl.ds(pl.multiple_of(q * tile + b * LANES, LANES), LANES)
            even = jnp.exp(acc[0, q]) * width_tiles[0]
            odd = jnp.exp(acc[1, q]) * width_tiles[1]
            density_ref[0, 0, :, lanes] = even
            density_ref[0, 1, :, lanes] = odd
            through = running(even + odd, True)
            before = shifted(through, 1, True) + even
            local_ref[0, 0, :, lanes] = before
            local_ref[0, 1, :, lanes] = through
            misfit = counts_ref[0, :, lanes] * (before - stars_ref[0, :, lanes]) + counts_ref[1, :, lanes] * (
                through - stars_ref[1, :, lanes]
            )
            sums_ref[0, 0:1, lanes] = through[7:8]
            sums_ref[0, 1:2, lanes] = jnp.sum(misfit, axis=0, keepdims=True)
        return carry

    lax.fori_loop(0, blocks, one_block, 0, unroll=8)


def backward_kernel(
    sqrt_ref, density_ref, local_ref, carries_ref, counts_ref, stars_ref, extinct_ref, grad_ref
):
    tile = density_ref.shape[3] // 4
    blocks = tile // LANES

    def one_block(b, carry):
        flow = {}
        for q in range(4):
            lanes = pl.ds(pl.multiple_of(q * tile + b * LANES, LANES), LANES)
            into = carries_ref[0, 0:1, lanes]
            past = carries_ref[0, 1:2, lanes]
            even = local_ref[0, 0, :, lanes] + into
            odd = local_ref[0, 1, :, lanes] + into
            extinct_ref[0, 0, :, lanes] = even.astype(extinct_ref.dtype)
            extinct_ref[0, 1, :, lanes] = odd.astype(extinct_ref.dtype)
            miss_even = counts_ref[0, :, lanes] * (even - stars_ref[0, :, lanes])
            miss_odd = counts_ref[1, :, lanes] * (odd - stars_ref[1, :, lanes])
            behind = running(miss_even + miss_odd, False)
            back_even = behind + past
            back_odd = (shifted(behind, 1, False) + miss_odd) + past
            flow[0, q] = density_ref[0, 0, :, lanes] * back_even
            flow[1, q] = density_ref[0, 1, :, lanes] * back_odd
        for u in range(2):
            for r in range(4):
                total = None
                for t in range(2):
                    for q in range(4):
                        term = sqrt_ref[((t * 4 + q) * 2 + u) * 4 + r] * flow[t, q]
                        total = term if total is None else total + term
                lanes = pl.ds(pl.multiple_of(r * tile + b * LANES, LANES), LANES)
                grad_ref[0, u, :, lanes] = total
        return carry

    lax.fori_loop(0, blocks, one_block, 0, unroll=8)


def by_parity(values):
    lead = values.shape[:-2]
    shells, width = values.shape[-2:]
    values = values.reshape(lead + (shells // 2, 2, width))
    return jnp.swapaxes(values, -2, -3)


def from_parity(values):
    lead = values.shape[:-3]
    _, shells, width = values.shape[-3:]
    return jnp.swapaxes(values, -2, -3).reshape(lead + (2 * shells, width))


def tiles(values):
    flat = values.reshape(-1)
    return jnp.broadcast_to(flat[:, None, None], (flat.shape[0], 8, LANES))


def local_forward(extended, halo_index, excitations, refine_weights, refine_sqrt, counts, stars, widths):
    samples, shells, _ = extended.shape
    slots, pixels = halo_index.shape
    blocks = pixels // BAND
    window = 3 * BAND
    fine_shells = excitations.shape[1]
    fine_pixels = excitations.shape[2]
    windows = jnp.stack(
        [extended[:, :, b * BAND : b * BAND + window] for b in range(blocks)], axis=1
    )
    pieces = split_three(windows)
    pieces = jnp.pad(pieces, ((0, 0), (0, 0), (0, 0), (0, 16 - shells), (0, 0)))
    pieces = pieces.transpose(1, 2, 0, 3, 4).reshape(samples, blocks, 3 * 16, window)
    starts = (jnp.arange(blocks, dtype=jnp.int32) * BAND)[None, :, None]
    local = halo_index.reshape(slots, blocks, BAND) - starts
    spots = jnp.arange(window, dtype=jnp.int32)[None, :, None, None]
    onehot = (local.transpose(1, 0, 2)[:, None] == spots).astype(jnp.bfloat16)
    onehot = onehot.reshape(blocks, window, slots * BAND)
    excite = by_parity(excitations)
    half = fine_shells // 2
    smem = pl.BlockSpec(memory_space=pltpu.SMEM)
    whole = lambda shape: pl.BlockSpec(shape, lambda k: (0,) * len(shape))
    per_sample = lambda shape: pl.BlockSpec(shape, lambda k: (k,) + (0,) * (len(shape) - 1))
    return pl.pallas_call(
        forward_kernel,
        grid=(samples,),
        in_specs=[
            smem,
            smem,
            per_sample((1, blocks, 48, window)),
            whole((blocks, window, slots * BAND)),
            per_sample((1, 2, half, fine_pixels)),
            whole((2, half, fine_pixels)),
            whole((2, half, fine_pixels)),
            smem,
        ],
        out_specs=[
            per_sample((1, 2, half, fine_pixels)),
            per_sample((1, 2, half, fine_pixels)),
            per_sample((1, 2, fine_pixels)),
        ],
        out_shape=[
            jax.ShapeDtypeStruct((samples, 2, half, fine_pixels), jnp.float32),
            jax.ShapeDtypeStruct((samples, 2, half, fine_pixels), jnp.float32),
            jax.ShapeDtypeStruct((samples, 2, fine_pixels), jnp.float32),
        ],
        scratch_shapes=[
            pltpu.VMEM((16, slots * BAND), jnp.float32),
            pltpu.VMEM((2 * 4 * 3 * slots, 8, LANES), jnp.float32),
            pltpu.VMEM((2 * 4 * 2 * 4, 8, LANES), jnp.float32),
            pltpu.VMEM((2, 8, LANES), jnp.float32),
        ],
        interpret=INTERPRET,
    )(
        refine_weights.reshape(-1),
        refine_sqrt.astype(jnp.float32).reshape(-1),
        pieces,
        onehot,
        excite,
        by_parity(counts),
        by_parity(stars),
        widths,
    )


def local_backward(refine_sqrt, density, local_cum, carries, counts, stars):
    samples, _, half, fine_pixels = density.shape
    smem = pl.BlockSpec(memory_space=pltpu.SMEM)
    whole = lambda shape: pl.BlockSpec(shape, lambda k: (0,) * len(shape))
    per_sample = lambda shape: pl.BlockSpec(shape, lambda k: (k,) + (0,) * (len(shape) - 1))
    extinct, grad = pl.pallas_call(
        backward_kernel,
        grid=(samples,),
        in_specs=[
            smem,
            per_sample((1, 2, half, fine_pixels)),
            per_sample((1, 2, half, fine_pixels)),
            per_sample((1, 2, fine_pixels)),
            whole((2, half, fine_pixels)),
            whole((2, half, fine_pixels)),
        ],
        out_specs=[
            per_sample((1, 2, half, fine_pixels)),
            per_sample((1, 2, half, fine_pixels)),
        ],
        out_shape=[
            jax.ShapeDtypeStruct((samples, 2, half, fine_pixels), jnp.bfloat16),
            jax.ShapeDtypeStruct((samples, 2, half, fine_pixels), jnp.float32),
        ],
        interpret=INTERPRET,
    )(refine_sqrt.astype(jnp.float32).reshape(-1), density, local_cum, carries, by_parity(counts), by_parity(stars))
    return from_parity(extinct), from_parity(grad)


def shards(
    coarse_field, excitations, refine_weights, refine_sqrt, halo_index, star_extinction, star_counts
):
    samples, coarse_shells, coarse_pixels = coarse_field.shape
    fine_shells = 2 * coarse_shells
    fine_pixels = 4 * coarse_pixels
    dist_count = lax.axis_size("dist")
    dist_rank = lax.axis_index("dist")
    all_shells = fine_shells * dist_count
    blocked = coarse_field.reshape(samples, coarse_shells, coarse_pixels // BAND, BAND)
    extended = with_halo(blocked, (("dist", 1), ("sky", 2)), 1)
    extended = extended.reshape(samples, coarse_shells + 2, coarse_pixels + 2 * BAND)
    shells = dist_rank * fine_shells + jnp.arange(fine_shells, dtype=jnp.int32)
    middle = (shells.astype(jnp.float32) + 0.5) / all_shells
    widths = 3.0 * jnp.exp(3.0 * middle - 3.0) / all_shells
    counts = star_counts.astype(jnp.float32)
    density, local_cum, sums = local_forward(
        extended, halo_index, excitations, refine_weights, refine_sqrt, counts, star_extinction, widths
    )
    weight = jnp.sum(counts, axis=0, keepdims=True)
    carry_in, carry_out = block_carries(sums[:, 0], sums[:, 1], weight, "dist")
    carries = jnp.stack([carry_in, carry_out], axis=1)
    return local_backward(refine_sqrt, density, local_cum, carries, counts, star_extinction)


def solution(mesh):
    placed = (
        P(None, "dist", "sky"),
        P(None, "dist", "sky"),
        P(),
        P(),
        P(None, "sky"),
        P("dist", "sky"),
        P("dist", "sky"),
    )
    return jax.shard_map(
        shards,
        mesh=mesh,
        in_specs=placed,
        out_specs=(P(None, "dist", "sky"), P(None, "dist", "sky")),
        check_vma=False,
    )
```

```python
import jax
import jax.numpy as jnp
from jax import lax
from jax.experimental import pallas as pl
from jax.experimental.pallas import tpu as pltpu
from jax.sharding import PartitionSpec as P

BAND = 128


exact_mode = lax.Precision.HIGHEST


def with_halo(block, sides, width):
    for axis, dim in sides:
        count = lax.axis_size(axis)
        forward = [(i, i + 1) for i in range(count - 1)]
        backward = [(target, source) for source, target in forward]
        low = lax.ppermute(
            lax.slice_in_dim(block, block.shape[dim] - width, None, axis=dim), axis, forward
        )
        high = lax.ppermute(lax.slice_in_dim(block, 0, width, axis=dim), axis, backward)
        block = jnp.concatenate([low, block, high], axis=dim)
    return block


def block_carries(totals, partial, weight, axis):
    count = lax.axis_size(axis)
    rows, pixels = totals.shape
    width = pixels // count
    packed = jnp.concatenate([totals, partial, weight], axis=0)
    packed = packed.reshape(packed.shape[0], count, width).transpose(1, 0, 2)
    mine = lax.all_to_all(packed, axis, 0, 0, tiled=True)
    block_totals = mine[:, :rows]
    block_partial = mine[:, rows : 2 * rows]
    block_weight = mine[:, 2 * rows :]
    blocks, height, width = block_totals.shape
    order = jnp.arange(blocks, dtype=jnp.int32)
    earlier = (order[None, :] < order[:, None]).astype(jnp.float32)
    flat = lambda values: values.reshape(blocks, -1)
    carry_in = jnp.dot(earlier, flat(block_totals), precision=exact_mode).reshape(blocks, height, width)
    block_misfit = block_partial + block_weight * carry_in
    carry_out = jnp.dot(earlier.T, flat(block_misfit), precision=exact_mode).reshape(blocks, height, width)
    back = lax.all_to_all(jnp.concatenate([carry_in, carry_out], axis=1), axis, 0, 0, tiled=True)
    back = back.transpose(1, 0, 2).reshape(2 * rows, pixels)
    return back[:rows], back[rows:]


def split_three(values):
    high = lax.reduce_precision(values, exponent_bits=8, mantissa_bits=7)
    rest = values - high
    middle = lax.reduce_precision(rest, exponent_bits=8, mantissa_bits=7)
    low = rest - middle
    return jnp.stack([high, middle, low]).astype(jnp.bfloat16)


def gather_nearby(extended, halo_index):
    samples, shells, _ = extended.shape
    slots, pixels = halo_index.shape
    blocks = pixels // BAND
    window = 3 * BAND
    windows = jnp.stack(
        [extended[:, :, b * BAND : b * BAND + window] for b in range(blocks)]
    ).reshape(blocks, samples * shells, window)
    pieces = split_three(windows).transpose(1, 0, 2, 3).reshape(blocks, 3 * samples * shells, window)
    starts = (jnp.arange(blocks, dtype=jnp.int32) * BAND)[None, :, None]
    local = halo_index.reshape(slots, blocks, BAND) - starts
    spots = jnp.arange(window, dtype=jnp.int32)[None, :, None, None]
    onehot = (local.transpose(1, 0, 2)[:, None] == spots).astype(jnp.bfloat16)
    onehot = onehot.reshape(blocks, window, slots * BAND)
    picked = jnp.einsum("bxw,bwn->bxn", pieces, onehot, preferred_element_type=jnp.float32)
    picked = picked.reshape(blocks, 3, samples, shells, slots, BAND)
    picked = (picked[:, 0] + picked[:, 1]) + picked[:, 2]
    return picked.transpose(1, 2, 3, 0, 4).reshape(samples, shells, slots, pixels)


INTERPRET = False
LANES = 128


def shifted(values, amount, toward_end):
    rows = values.shape[0]
    row = lax.broadcasted_iota(jnp.int32, values.shape, 0)
    forward = pltpu.roll(values, amount, 0)
    backward = pltpu.roll(values, rows - amount, 0)
    probe = pltpu.roll(row, amount, 0)
    plain = probe == jnp.where(row >= amount, row - amount, row + rows - amount)
    if toward_end:
        moved = jnp.where(plain, forward, backward)
        return jnp.where(row >= amount, moved, 0.0)
    moved = jnp.where(plain, backward, forward)
    return jnp.where(row < rows - amount, moved, 0.0)


def running(values, toward_end):
    for amount in (1, 2, 4):
        values = values + shifted(values, amount, toward_end)
    return values


def paired(values, odd_from_even):
    row = lax.broadcasted_iota(jnp.int32, values.shape, 0)
    if odd_from_even:
        return jnp.where(row % 2 == 1, shifted(values, 1, True), values)
    return jnp.where(row % 2 == 0, shifted(values, 1, False), values)


def alternating(table, index_of, count, target):
    row = lax.broadcasted_iota(jnp.int32, (8, LANES), 0)
    for n in range(count):
        even = jnp.full((8, LANES), table[index_of(n, 0)], jnp.float32)
        odd = jnp.full((8, LANES), table[index_of(n, 1)], jnp.float32)
        target[n] = jnp.where(row % 2 == 0, even, odd)


def forward_kernel(
    weights_ref, sqrt_ref, pieces_ref, onehot_ref, excite_ref, counts_ref, stars_ref, widths_ref,
    density_ref, local_ref, sums_ref, picked_ref, weight_tiles, sqrt_tiles, width_tiles,
):
    blocks = onehot_ref.shape[0]
    slots = onehot_ref.shape[2] // LANES
    tile = blocks * LANES
    rows = picked_ref.shape[0]

    @pl.when(pl.program_id(0) == 0)
    def _():
        alternating(weights_ref, lambda n, t: t * 4 * 3 * slots + n, 4 * 3 * slots, weight_tiles)
        alternating(sqrt_ref, lambda n, t: t * 4 * 2 * 4 + n, 4 * 2 * 4, sqrt_tiles)
        row = lax.broadcasted_iota(jnp.int32, (8, LANES), 0)
        for h in range(2):
            column = jnp.zeros((8, LANES), jnp.float32)
            for i in range(8):
                column = jnp.where(row == i, widths_ref[8 * h + i], column)
            width_tiles[h] = column

    for b in range(blocks):
        picked = jnp.dot(pieces_ref[0, b], onehot_ref[b], preferred_element_type=jnp.float32)
        picked_ref[...] = (picked[0:rows] + picked[rows : 2 * rows]) + picked[2 * rows : 3 * rows]
        acc = {}
        for h in range(2):
            spread = {}
            for r in range(4):
                lanes = pl.ds(r * tile + b * LANES, LANES)
                values = excite_ref[0, pl.ds(8 * h, 8), lanes].astype(jnp.float32)
                spread[0, r] = paired(values, True)
                spread[1, r] = paired(values, False)
            for q in range(4):
                total = None
                for u in range(2):
                    for r in range(4):
                        term = sqrt_tiles[(q * 2 + u) * 4 + r] * spread[u, r]
                        total = term if total is None else total + term
                acc[h, q] = total
        for j in range(3):
            for m in range(slots):
                for h in range(2):
                    near = picked_ref[pl.ds(8 * h + 2 * j, 8), pl.ds(m * LANES, LANES)]
                    for q in range(4):
                        acc[h, q] = acc[h, q] + weight_tiles[(q * 3 + j) * 9 + m] * near
        for q in range(4):
            lanes = pl.ds(q * tile + b * LANES, LANES)
            first = jnp.exp(acc[0, q]) * width_tiles[0]
            second = jnp.exp(acc[1, q]) * width_tiles[1]
            density_ref[0, pl.ds(0, 8), lanes] = first
            density_ref[0, pl.ds(8, 8), lanes] = second
            low = running(first, True)
            high = running(second, True) + jnp.broadcast_to(low[7:8], low.shape)
            local_ref[0, pl.ds(0, 8), lanes] = low
            local_ref[0, pl.ds(8, 8), lanes] = high
            misfit = counts_ref[pl.ds(0, 8), lanes] * (low - stars_ref[pl.ds(0, 8), lanes]) + counts_ref[
                pl.ds(8, 8), lanes
            ] * (high - stars_ref[pl.ds(8, 8), lanes])
            sums_ref[0, 0:1, lanes] = high[7:8]
            sums_ref[0, 1:2, lanes] = jnp.sum(misfit, axis=0, keepdims=True)


def backward_kernel(
    sqrt_ref, density_ref, local_ref, carries_ref, counts_ref, stars_ref, extinct_ref, grad_ref, sqrt_tiles
):
    tile = density_ref.shape[2] // 4
    blocks = tile // LANES

    @pl.when(pl.program_id(0) == 0)
    def _():
        alternating(sqrt_ref, lambda n, u: ((n // 4) * 2 + u) * 4 + n % 4, 2 * 4 * 4, sqrt_tiles)

    for b in range(blocks):
        flow = {}
        for q in range(4):
            lanes = pl.ds(q * tile + b * LANES, LANES)
            into = carries_ref[0, 0:1, lanes]
            past = carries_ref[0, 1:2, lanes]
            low = local_ref[0, pl.ds(0, 8), lanes] + into
            high = local_ref[0, pl.ds(8, 8), lanes] + into
            extinct_ref[0, pl.ds(0, 8), lanes] = low.astype(extinct_ref.dtype)
            extinct_ref[0, pl.ds(8, 8), lanes] = high.astype(extinct_ref.dtype)
            miss_low = counts_ref[pl.ds(0, 8), lanes] * (low - stars_ref[pl.ds(0, 8), lanes])
            miss_high = counts_ref[pl.ds(8, 8), lanes] * (high - stars_ref[pl.ds(8, 8), lanes])
            behind_high = running(miss_high, False)
            behind_low = running(miss_low, False) + jnp.broadcast_to(behind_high[0:1], behind_high.shape)
            for h, behind in ((0, behind_low), (1, behind_high)):
                moving = density_ref[0, pl.ds(8 * h, 8), lanes] * (behind + past)
                flow[h, q, 0] = paired(moving, True)
                flow[h, q, 1] = paired(moving, False)
        for h in range(2):
            for r in range(4):
                total = None
                for t in range(2):
                    for q in range(4):
                        term = sqrt_tiles[(t * 4 + q) * 4 + r] * flow[h, q, t]
                        total = term if total is None else total + term
                grad_ref[0, pl.ds(8 * h, 8), pl.ds(r * tile + b * LANES, LANES)] = total


def by_parity(values):
    lead = values.shape[:-2]
    shells, width = values.shape[-2:]
    values = values.reshape(lead + (shells // 2, 2, width))
    return jnp.swapaxes(values, -2, -3)


def from_parity(values):
    lead = values.shape[:-3]
    _, shells, width = values.shape[-3:]
    return jnp.swapaxes(values, -2, -3).reshape(lead + (2 * shells, width))


def tiles(values):
    flat = values.reshape(-1)
    return jnp.broadcast_to(flat[:, None, None], (flat.shape[0], 8, LANES))


def local_forward(extended, halo_index, excitations, refine_weights, refine_sqrt, counts, stars, widths):
    samples, shells, _ = extended.shape
    slots, pixels = halo_index.shape
    blocks = pixels // BAND
    window = 3 * BAND
    fine_shells = excitations.shape[1]
    fine_pixels = excitations.shape[2]
    windows = jnp.stack(
        [extended[:, :, b * BAND : b * BAND + window] for b in range(blocks)], axis=1
    )
    rows = 2 * (fine_shells // 2 + 4)
    windows = jnp.pad(windows, ((0, 0), (0, 0), (0, rows // 2 - shells), (0, 0)))
    pieces = split_three(jnp.repeat(windows, 2, axis=2))
    pieces = pieces.transpose(1, 2, 0, 3, 4).reshape(samples, blocks, 3 * rows, window)
    starts = (jnp.arange(blocks, dtype=jnp.int32) * BAND)[None, :, None]
    local = halo_index.reshape(slots, blocks, BAND) - starts
    spots = jnp.arange(window, dtype=jnp.int32)[None, :, None, None]
    onehot = (local.transpose(1, 0, 2)[:, None] == spots).astype(jnp.bfloat16)
    onehot = onehot.reshape(blocks, window, slots * BAND)
    half = fine_shells // 2
    smem = pl.BlockSpec(memory_space=pltpu.SMEM)
    whole = lambda shape: pl.BlockSpec(shape, lambda k: (0,) * len(shape))
    per_sample = lambda shape: pl.BlockSpec(shape, lambda k: (k,) + (0,) * (len(shape) - 1))
    return pl.pallas_call(
        forward_kernel,
        grid=(samples,),
        in_specs=[
            smem,
            smem,
            per_sample((1, blocks, 3 * rows, window)),
            whole((blocks, window, slots * BAND)),
            per_sample((1, fine_shells, fine_pixels)),
            whole((fine_shells, fine_pixels)),
            whole((fine_shells, fine_pixels)),
            smem,
        ],
        out_specs=[
            per_sample((1, fine_shells, fine_pixels)),
            per_sample((1, fine_shells, fine_pixels)),
            per_sample((1, 2, fine_pixels)),
        ],
        out_shape=[
            jax.ShapeDtypeStruct((samples, fine_shells, fine_pixels), jnp.float32),
            jax.ShapeDtypeStruct((samples, fine_shells, fine_pixels), jnp.float32),
            jax.ShapeDtypeStruct((samples, 2, fine_pixels), jnp.float32),
        ],
        scratch_shapes=[
            pltpu.VMEM((rows, slots * BAND), jnp.float32),
            pltpu.VMEM((4 * 3 * slots, 8, LANES), jnp.float32),
            pltpu.VMEM((4 * 2 * 4, 8, LANES), jnp.float32),
            pltpu.VMEM((2, 8, LANES), jnp.float32),
        ],
        interpret=INTERPRET,
    )(
        refine_weights.reshape(-1),
        refine_sqrt.astype(jnp.float32).reshape(-1),
        pieces,
        onehot,
        excitations,
        counts,
        stars,
        widths,
    )


def local_backward(refine_sqrt, density, local_cum, carries, counts, stars):
    samples, fine_shells, fine_pixels = density.shape
    smem = pl.BlockSpec(memory_space=pltpu.SMEM)
    whole = lambda shape: pl.BlockSpec(shape, lambda k: (0,) * len(shape))
    per_sample = lambda shape: pl.BlockSpec(shape, lambda k: (k,) + (0,) * (len(shape) - 1))
    return pl.pallas_call(
        backward_kernel,
        grid=(samples,),
        in_specs=[
            smem,
            per_sample((1, fine_shells, fine_pixels)),
            per_sample((1, fine_shells, fine_pixels)),
            per_sample((1, 2, fine_pixels)),
            whole((fine_shells, fine_pixels)),
            whole((fine_shells, fine_pixels)),
        ],
        out_specs=[
            per_sample((1, fine_shells, fine_pixels)),
            per_sample((1, fine_shells, fine_pixels)),
        ],
        out_shape=[
            jax.ShapeDtypeStruct((samples, fine_shells, fine_pixels), jnp.bfloat16),
            jax.ShapeDtypeStruct((samples, fine_shells, fine_pixels), jnp.float32),
        ],
        scratch_shapes=[pltpu.VMEM((2 * 4 * 4, 8, LANES), jnp.float32)],
        interpret=INTERPRET,
    )(refine_sqrt.astype(jnp.float32).reshape(-1), density, local_cum, carries, counts, stars)


def shards(
    coarse_field, excitations, refine_weights, refine_sqrt, halo_index, star_extinction, star_counts
):
    samples, coarse_shells, coarse_pixels = coarse_field.shape
    fine_shells = 2 * coarse_shells
    fine_pixels = 4 * coarse_pixels
    dist_count = lax.axis_size("dist")
    dist_rank = lax.axis_index("dist")
    all_shells = fine_shells * dist_count
    blocked = coarse_field.reshape(samples, coarse_shells, coarse_pixels // BAND, BAND)
    extended = with_halo(blocked, (("dist", 1), ("sky", 2)), 1)
    extended = extended.reshape(samples, coarse_shells + 2, coarse_pixels + 2 * BAND)
    shells = dist_rank * fine_shells + jnp.arange(fine_shells, dtype=jnp.int32)
    middle = (shells.astype(jnp.float32) + 0.5) / all_shells
    widths = 3.0 * jnp.exp(3.0 * middle - 3.0) / all_shells
    counts = star_counts.astype(jnp.float32)
    density, local_cum, sums = local_forward(
        extended, halo_index, excitations, refine_weights, refine_sqrt, counts, star_extinction, widths
    )
    weight = jnp.sum(counts, axis=0, keepdims=True)
    carry_in, carry_out = block_carries(sums[:, 0], sums[:, 1], weight, "dist")
    carries = jnp.stack([carry_in, carry_out], axis=1)
    return local_backward(refine_sqrt, density, local_cum, carries, counts, star_extinction)


def solution(mesh):
    placed = (
        P(None, "dist", "sky"),
        P(None, "dist", "sky"),
        P(),
        P(),
        P(None, "sky"),
        P("dist", "sky"),
        P("dist", "sky"),
    )
    return jax.shard_map(
        shards,
        mesh=mesh,
        in_specs=placed,
        out_specs=(P(None, "dist", "sky"), P(None, "dist", "sky")),
        check_vma=False,
    )
```

```python
import jax
import jax.numpy as jnp
from jax import lax
from jax.experimental import pallas as pl
from jax.experimental.pallas import tpu as pltpu
from jax.sharding import PartitionSpec as P

BAND = 128


exact_mode = lax.Precision.HIGHEST


def with_halo(block, sides, width):
    for axis, dim in sides:
        count = lax.axis_size(axis)
        forward = [(i, i + 1) for i in range(count - 1)]
        backward = [(target, source) for source, target in forward]
        low = lax.ppermute(
            lax.slice_in_dim(block, block.shape[dim] - width, None, axis=dim), axis, forward
        )
        high = lax.ppermute(lax.slice_in_dim(block, 0, width, axis=dim), axis, backward)
        block = jnp.concatenate([low, block, high], axis=dim)
    return block


def block_carries(totals, partial, weight, axis):
    count = lax.axis_size(axis)
    rows, pixels = totals.shape
    width = pixels // count
    packed = jnp.concatenate([totals, partial, weight], axis=0)
    packed = packed.reshape(packed.shape[0], count, width).transpose(1, 0, 2)
    mine = lax.all_to_all(packed, axis, 0, 0, tiled=True)
    block_totals = mine[:, :rows]
    block_partial = mine[:, rows : 2 * rows]
    block_weight = mine[:, 2 * rows :]
    blocks, height, width = block_totals.shape
    order = jnp.arange(blocks, dtype=jnp.int32)
    earlier = (order[None, :] < order[:, None]).astype(jnp.float32)
    flat = lambda values: values.reshape(blocks, -1)
    carry_in = jnp.dot(earlier, flat(block_totals), precision=exact_mode).reshape(blocks, height, width)
    block_misfit = block_partial + block_weight * carry_in
    carry_out = jnp.dot(earlier.T, flat(block_misfit), precision=exact_mode).reshape(blocks, height, width)
    back = lax.all_to_all(jnp.concatenate([carry_in, carry_out], axis=1), axis, 0, 0, tiled=True)
    back = back.transpose(1, 0, 2).reshape(2 * rows, pixels)
    return back[:rows], back[rows:]


def split_three(values):
    high = lax.reduce_precision(values, exponent_bits=8, mantissa_bits=7)
    rest = values - high
    middle = lax.reduce_precision(rest, exponent_bits=8, mantissa_bits=7)
    low = rest - middle
    return jnp.stack([high, middle, low]).astype(jnp.bfloat16)


def gather_nearby(extended, halo_index):
    samples, shells, _ = extended.shape
    slots, pixels = halo_index.shape
    blocks = pixels // BAND
    window = 3 * BAND
    windows = jnp.stack(
        [extended[:, :, b * BAND : b * BAND + window] for b in range(blocks)]
    ).reshape(blocks, samples * shells, window)
    pieces = split_three(windows).transpose(1, 0, 2, 3).reshape(blocks, 3 * samples * shells, window)
    starts = (jnp.arange(blocks, dtype=jnp.int32) * BAND)[None, :, None]
    local = halo_index.reshape(slots, blocks, BAND) - starts
    spots = jnp.arange(window, dtype=jnp.int32)[None, :, None, None]
    onehot = (local.transpose(1, 0, 2)[:, None] == spots).astype(jnp.bfloat16)
    onehot = onehot.reshape(blocks, window, slots * BAND)
    picked = jnp.einsum("bxw,bwn->bxn", pieces, onehot, preferred_element_type=jnp.float32)
    picked = picked.reshape(blocks, 3, samples, shells, slots, BAND)
    picked = (picked[:, 0] + picked[:, 1]) + picked[:, 2]
    return picked.transpose(1, 2, 3, 0, 4).reshape(samples, shells, slots, pixels)


INTERPRET = False
LANES = 128


def shifted(values, amount, toward_end):
    rows = values.shape[0]
    row = lax.broadcasted_iota(jnp.int32, values.shape, 0)
    forward = pltpu.roll(values, amount, 0)
    backward = pltpu.roll(values, rows - amount, 0)
    probe = pltpu.roll(row, amount, 0)
    plain = probe == jnp.where(row >= amount, row - amount, row + rows - amount)
    if toward_end:
        moved = jnp.where(plain, forward, backward)
        return jnp.where(row >= amount, moved, 0.0)
    moved = jnp.where(plain, backward, forward)
    return jnp.where(row < rows - amount, moved, 0.0)


def running(values, toward_end):
    for amount in (1, 2, 4):
        values = values + shifted(values, amount, toward_end)
    return values


def paired(values, odd_from_even):
    row = lax.broadcasted_iota(jnp.int32, values.shape, 0)
    if odd_from_even:
        return jnp.where(row % 2 == 1, shifted(values, 1, True), values)
    return jnp.where(row % 2 == 0, shifted(values, 1, False), values)


def alternating(table, index_of, count, target):
    row = lax.broadcasted_iota(jnp.int32, (8, LANES), 0)
    for n in range(count):
        even = jnp.full((8, LANES), table[index_of(n, 0)], jnp.float32)
        odd = jnp.full((8, LANES), table[index_of(n, 1)], jnp.float32)
        target[n] = jnp.where(row % 2 == 0, even, odd)


def forward_kernel(
    weights_ref, sqrt_ref, pieces_ref, onehot_ref, excite_ref, counts_ref, stars_ref, widths_ref,
    density_ref, local_ref, sums_ref, picked_ref, weight_tiles, sqrt_tiles, width_tiles,
):
    blocks = onehot_ref.shape[0]
    slots = onehot_ref.shape[2] // LANES
    tile = blocks * LANES
    rows = picked_ref.shape[0]

    @pl.when(pl.program_id(0) == 0)
    def _():
        alternating(weights_ref, lambda n, t: t * 4 * 3 * slots + n, 4 * 3 * slots, weight_tiles)
        alternating(sqrt_ref, lambda n, t: t * 4 * 2 * 4 + n, 4 * 2 * 4, sqrt_tiles)
        row = lax.broadcasted_iota(jnp.int32, (8, LANES), 0)
        for h in range(2):
            column = jnp.zeros((8, LANES), jnp.float32)
            for i in range(8):
                column = jnp.where(row == i, widths_ref[8 * h + i], column)
            width_tiles[h] = column

    for b in range(blocks):
        picked = jnp.dot(pieces_ref[0, b], onehot_ref[b], preferred_element_type=jnp.float32)
        picked_ref[...] = (picked[0:rows] + picked[rows : 2 * rows]) + picked[2 * rows : 3 * rows]
        acc = {}
        for h in range(2):
            spread = {}
            for r in range(4):
                lanes = pl.ds(r * tile + b * LANES, LANES)
                values = excite_ref[0, pl.ds(8 * h, 8), lanes].astype(jnp.float32)
                spread[0, r] = paired(values, True)
                spread[1, r] = paired(values, False)
            for q in range(4):
                total = None
                for u in range(2):
                    for r in range(4):
                        term = sqrt_tiles[(q * 2 + u) * 4 + r] * spread[u, r]
                        total = term if total is None else total + term
                acc[h, q] = total
        for j in range(3):
            for m in range(slots):
                for h in range(2):
                    near = picked_ref[pl.ds(8 * h + 2 * j, 8), pl.ds(m * LANES, LANES)]
                    for q in range(4):
                        acc[h, q] = acc[h, q] + weight_tiles[(q * 3 + j) * 9 + m] * near
        for q in range(4):
            lanes = pl.ds(q * tile + b * LANES, LANES)
            first = jnp.exp(acc[0, q]) * width_tiles[0]
            second = jnp.exp(acc[1, q]) * width_tiles[1]
            density_ref[0, pl.ds(0, 8), lanes] = first
            density_ref[0, pl.ds(8, 8), lanes] = second
            low = running(first, True)
            high = running(second, True) + jnp.broadcast_to(low[7:8], low.shape)
            local_ref[0, pl.ds(0, 8), lanes] = low
            local_ref[0, pl.ds(8, 8), lanes] = high
            misfit = counts_ref[pl.ds(0, 8), lanes] * (low - stars_ref[pl.ds(0, 8), lanes]) + counts_ref[
                pl.ds(8, 8), lanes
            ] * (high - stars_ref[pl.ds(8, 8), lanes])
            sums_ref[0, 0:1, lanes] = high[7:8]
            sums_ref[0, 1:2, lanes] = jnp.sum(misfit, axis=0, keepdims=True)


def backward_kernel(
    sqrt_ref, density_ref, local_ref, carries_ref, counts_ref, stars_ref, extinct_ref, grad_ref, sqrt_tiles
):
    tile = density_ref.shape[2] // 4
    blocks = tile // LANES

    @pl.when(pl.program_id(0) == 0)
    def _():
        alternating(sqrt_ref, lambda n, u: ((n // 4) * 2 + u) * 4 + n % 4, 2 * 4 * 4, sqrt_tiles)

    for b in range(blocks):
        flow = {}
        for q in range(4):
            lanes = pl.ds(q * tile + b * LANES, LANES)
            into = carries_ref[0, 0:1, lanes]
            past = carries_ref[0, 1:2, lanes]
            low = local_ref[0, pl.ds(0, 8), lanes] + into
            high = local_ref[0, pl.ds(8, 8), lanes] + into
            extinct_ref[0, pl.ds(0, 8), lanes] = low.astype(extinct_ref.dtype)
            extinct_ref[0, pl.ds(8, 8), lanes] = high.astype(extinct_ref.dtype)
            miss_low = counts_ref[pl.ds(0, 8), lanes] * (low - stars_ref[pl.ds(0, 8), lanes])
            miss_high = counts_ref[pl.ds(8, 8), lanes] * (high - stars_ref[pl.ds(8, 8), lanes])
            behind_high = running(miss_high, False)
            behind_low = running(miss_low, False) + jnp.broadcast_to(behind_high[0:1], behind_high.shape)
            for h, behind in ((0, behind_low), (1, behind_high)):
                moving = density_ref[0, pl.ds(8 * h, 8), lanes] * (behind + past)
                flow[h, q, 0] = paired(moving, True)
                flow[h, q, 1] = paired(moving, False)
        for h in range(2):
            for r in range(4):
                total = None
                for t in range(2):
                    for q in range(4):
                        term = sqrt_tiles[(t * 4 + q) * 4 + r] * flow[h, q, t]
                        total = term if total is None else total + term
                grad_ref[0, pl.ds(8 * h, 8), pl.ds(r * tile + b * LANES, LANES)] = total


def by_parity(values):
    lead = values.shape[:-2]
    shells, width = values.shape[-2:]
    values = values.reshape(lead + (shells // 2, 2, width))
    return jnp.swapaxes(values, -2, -3)


def from_parity(values):
    lead = values.shape[:-3]
    _, shells, width = values.shape[-3:]
    return jnp.swapaxes(values, -2, -3).reshape(lead + (2 * shells, width))


def tiles(values):
    flat = values.reshape(-1)
    return jnp.broadcast_to(flat[:, None, None], (flat.shape[0], 8, LANES))


def local_forward(extended, halo_index, excitations, refine_weights, refine_sqrt, counts, stars, widths):
    samples, shells, _ = extended.shape
    slots, pixels = halo_index.shape
    blocks = pixels // BAND
    window = 3 * BAND
    fine_shells = excitations.shape[1]
    fine_pixels = excitations.shape[2]
    rows = 2 * (fine_shells // 2 + 4)
    split = split_three(extended)
    split = jnp.pad(split, ((0, 0), (0, 0), (0, rows // 2 - shells), (0, 0)))
    split = jnp.repeat(split, 2, axis=2)
    pieces = jnp.stack([split[:, :, :, b * BAND : b * BAND + window] for b in range(blocks)], axis=2)
    pieces = pieces.transpose(1, 2, 0, 3, 4).reshape(samples, blocks, 3 * rows, window)
    starts = (jnp.arange(blocks, dtype=jnp.int32) * BAND)[None, :, None]
    local = halo_index.reshape(slots, blocks, BAND) - starts
    spots = jnp.arange(window, dtype=jnp.int32)[None, :, None, None]
    onehot = (local.transpose(1, 0, 2)[:, None] == spots).astype(jnp.bfloat16)
    onehot = onehot.reshape(blocks, window, slots * BAND)
    half = fine_shells // 2
    smem = pl.BlockSpec(memory_space=pltpu.SMEM)
    whole = lambda shape: pl.BlockSpec(shape, lambda k: (0,) * len(shape))
    per_sample = lambda shape: pl.BlockSpec(shape, lambda k: (k,) + (0,) * (len(shape) - 1))
    return pl.pallas_call(
        forward_kernel,
        grid=(samples,),
        in_specs=[
            smem,
            smem,
            per_sample((1, blocks, 3 * rows, window)),
            whole((blocks, window, slots * BAND)),
            per_sample((1, fine_shells, fine_pixels)),
            whole((fine_shells, fine_pixels)),
            whole((fine_shells, fine_pixels)),
            smem,
        ],
        out_specs=[
            per_sample((1, fine_shells, fine_pixels)),
            per_sample((1, fine_shells, fine_pixels)),
            per_sample((1, 2, fine_pixels)),
        ],
        out_shape=[
            jax.ShapeDtypeStruct((samples, fine_shells, fine_pixels), jnp.float32),
            jax.ShapeDtypeStruct((samples, fine_shells, fine_pixels), jnp.float32),
            jax.ShapeDtypeStruct((samples, 2, fine_pixels), jnp.float32),
        ],
        scratch_shapes=[
            pltpu.VMEM((rows, slots * BAND), jnp.float32),
            pltpu.VMEM((4 * 3 * slots, 8, LANES), jnp.float32),
            pltpu.VMEM((4 * 2 * 4, 8, LANES), jnp.float32),
            pltpu.VMEM((2, 8, LANES), jnp.float32),
        ],
        interpret=INTERPRET,
    )(
        refine_weights.reshape(-1),
        refine_sqrt.astype(jnp.float32).reshape(-1),
        pieces,
        onehot,
        excitations,
        counts,
        stars,
        widths,
    )


def local_backward(refine_sqrt, density, local_cum, carries, counts, stars):
    samples, fine_shells, fine_pixels = density.shape
    smem = pl.BlockSpec(memory_space=pltpu.SMEM)
    whole = lambda shape: pl.BlockSpec(shape, lambda k: (0,) * len(shape))
    per_sample = lambda shape: pl.BlockSpec(shape, lambda k: (k,) + (0,) * (len(shape) - 1))
    return pl.pallas_call(
        backward_kernel,
        grid=(samples,),
        in_specs=[
            smem,
            per_sample((1, fine_shells, fine_pixels)),
            per_sample((1, fine_shells, fine_pixels)),
            per_sample((1, 2, fine_pixels)),
            whole((fine_shells, fine_pixels)),
            whole((fine_shells, fine_pixels)),
        ],
        out_specs=[
            per_sample((1, fine_shells, fine_pixels)),
            per_sample((1, fine_shells, fine_pixels)),
        ],
        out_shape=[
            jax.ShapeDtypeStruct((samples, fine_shells, fine_pixels), jnp.bfloat16),
            jax.ShapeDtypeStruct((samples, fine_shells, fine_pixels), jnp.float32),
        ],
        scratch_shapes=[pltpu.VMEM((2 * 4 * 4, 8, LANES), jnp.float32)],
        interpret=INTERPRET,
    )(refine_sqrt.astype(jnp.float32).reshape(-1), density, local_cum, carries, counts, stars)


def shards(
    coarse_field, excitations, refine_weights, refine_sqrt, halo_index, star_extinction, star_counts
):
    samples, coarse_shells, coarse_pixels = coarse_field.shape
    fine_shells = 2 * coarse_shells
    fine_pixels = 4 * coarse_pixels
    dist_count = lax.axis_size("dist")
    dist_rank = lax.axis_index("dist")
    all_shells = fine_shells * dist_count
    blocked = coarse_field.reshape(samples, coarse_shells, coarse_pixels // BAND, BAND)
    extended = with_halo(blocked, (("dist", 1), ("sky", 2)), 1)
    extended = extended.reshape(samples, coarse_shells + 2, coarse_pixels + 2 * BAND)
    shells = dist_rank * fine_shells + jnp.arange(fine_shells, dtype=jnp.int32)
    middle = (shells.astype(jnp.float32) + 0.5) / all_shells
    widths = 3.0 * jnp.exp(3.0 * middle - 3.0) / all_shells
    counts = star_counts.astype(jnp.float32)
    density, local_cum, sums = local_forward(
        extended, halo_index, excitations, refine_weights, refine_sqrt, counts, star_extinction, widths
    )
    weight = jnp.sum(counts, axis=0, keepdims=True)
    carry_in, carry_out = block_carries(sums[:, 0], sums[:, 1], weight, "dist")
    carries = jnp.stack([carry_in, carry_out], axis=1)
    return local_backward(refine_sqrt, density, local_cum, carries, counts, star_extinction)


def solution(mesh):
    placed = (
        P(None, "dist", "sky"),
        P(None, "dist", "sky"),
        P(),
        P(),
        P(None, "sky"),
        P("dist", "sky"),
        P("dist", "sky"),
    )
    return jax.shard_map(
        shards,
        mesh=mesh,
        in_specs=placed,
        out_specs=(P(None, "dist", "sky"), P(None, "dist", "sky")),
        check_vma=False,
    )
```

```python
import jax
import jax.numpy as jnp
from jax import lax
from jax.experimental import pallas as pl
from jax.experimental.pallas import tpu as pltpu
from jax.sharding import PartitionSpec as P

BAND = 128


exact_mode = lax.Precision.HIGHEST


def with_halo(block, sides, width):
    for axis, dim in sides:
        count = lax.axis_size(axis)
        forward = [(i, i + 1) for i in range(count - 1)]
        backward = [(target, source) for source, target in forward]
        low = lax.ppermute(
            lax.slice_in_dim(block, block.shape[dim] - width, None, axis=dim), axis, forward
        )
        high = lax.ppermute(lax.slice_in_dim(block, 0, width, axis=dim), axis, backward)
        block = jnp.concatenate([low, block, high], axis=dim)
    return block


def block_carries(totals, partial, weight, axis):
    count = lax.axis_size(axis)
    rows, pixels = totals.shape
    width = pixels // count
    packed = jnp.concatenate([totals, partial, weight], axis=0)
    packed = packed.reshape(packed.shape[0], count, width).transpose(1, 0, 2)
    mine = lax.all_to_all(packed, axis, 0, 0, tiled=True)
    block_totals = mine[:, :rows]
    block_partial = mine[:, rows : 2 * rows]
    block_weight = mine[:, 2 * rows :]
    blocks, height, width = block_totals.shape
    order = jnp.arange(blocks, dtype=jnp.int32)
    earlier = (order[None, :] < order[:, None]).astype(jnp.float32)
    flat = lambda values: values.reshape(blocks, -1)
    carry_in = jnp.dot(earlier, flat(block_totals), precision=exact_mode).reshape(blocks, height, width)
    block_misfit = block_partial + block_weight * carry_in
    carry_out = jnp.dot(earlier.T, flat(block_misfit), precision=exact_mode).reshape(blocks, height, width)
    back = lax.all_to_all(jnp.concatenate([carry_in, carry_out], axis=1), axis, 0, 0, tiled=True)
    back = back.transpose(1, 0, 2).reshape(2 * rows, pixels)
    return back[:rows], back[rows:]


def split_three(values):
    high = lax.reduce_precision(values, exponent_bits=8, mantissa_bits=7)
    rest = values - high
    middle = lax.reduce_precision(rest, exponent_bits=8, mantissa_bits=7)
    low = rest - middle
    return jnp.stack([high, middle, low]).astype(jnp.bfloat16)


def gather_nearby(extended, halo_index):
    samples, shells, _ = extended.shape
    slots, pixels = halo_index.shape
    blocks = pixels // BAND
    window = 3 * BAND
    windows = jnp.stack(
        [extended[:, :, b * BAND : b * BAND + window] for b in range(blocks)]
    ).reshape(blocks, samples * shells, window)
    pieces = split_three(windows).transpose(1, 0, 2, 3).reshape(blocks, 3 * samples * shells, window)
    starts = (jnp.arange(blocks, dtype=jnp.int32) * BAND)[None, :, None]
    local = halo_index.reshape(slots, blocks, BAND) - starts
    spots = jnp.arange(window, dtype=jnp.int32)[None, :, None, None]
    onehot = (local.transpose(1, 0, 2)[:, None] == spots).astype(jnp.bfloat16)
    onehot = onehot.reshape(blocks, window, slots * BAND)
    picked = jnp.einsum("bxw,bwn->bxn", pieces, onehot, preferred_element_type=jnp.float32)
    picked = picked.reshape(blocks, 3, samples, shells, slots, BAND)
    picked = (picked[:, 0] + picked[:, 1]) + picked[:, 2]
    return picked.transpose(1, 2, 3, 0, 4).reshape(samples, shells, slots, pixels)


INTERPRET = False
LANES = 128


def shifted(values, amount, toward_end):
    rows = values.shape[0]
    row = lax.broadcasted_iota(jnp.int32, values.shape, 0)
    if toward_end:
        return jnp.where(row >= amount, pltpu.roll(values, amount, 0), 0.0)
    return jnp.where(row < rows - amount, pltpu.roll(values, rows - amount, 0), 0.0)


def running(values, toward_end):
    for amount in (1, 2, 4):
        values = values + shifted(values, amount, toward_end)
    return values


def paired(values, odd_from_even):
    row = lax.broadcasted_iota(jnp.int32, values.shape, 0)
    if odd_from_even:
        return jnp.where(row % 2 == 1, shifted(values, 1, True), values)
    return jnp.where(row % 2 == 0, shifted(values, 1, False), values)


def alternating(table, index_of, count, target):
    row = lax.broadcasted_iota(jnp.int32, (8, LANES), 0)
    for n in range(count):
        even = jnp.full((8, LANES), table[index_of(n, 0)], jnp.float32)
        odd = jnp.full((8, LANES), table[index_of(n, 1)], jnp.float32)
        target[n] = jnp.where(row % 2 == 0, even, odd)


def forward_kernel(
    weights_ref, sqrt_ref, pieces_ref, onehot_ref, excite_ref, counts_ref, stars_ref, widths_ref,
    density_ref, local_ref, sums_ref, picked_ref, weight_tiles, sqrt_tiles, width_tiles,
):
    blocks = onehot_ref.shape[0]
    slots = onehot_ref.shape[2] // LANES
    tile = blocks * LANES
    rows = picked_ref.shape[0]

    @pl.when(pl.program_id(0) == 0)
    def _():
        alternating(weights_ref, lambda n, t: t * 4 * 3 * slots + n, 4 * 3 * slots, weight_tiles)
        alternating(sqrt_ref, lambda n, t: t * 4 * 2 * 4 + n, 4 * 2 * 4, sqrt_tiles)
        row = lax.broadcasted_iota(jnp.int32, (8, LANES), 0)
        for h in range(2):
            column = jnp.zeros((8, LANES), jnp.float32)
            for i in range(8):
                column = jnp.where(row == i, widths_ref[8 * h + i], column)
            width_tiles[h] = column

    for b in range(blocks):
        picked = jnp.dot(pieces_ref[0, b], onehot_ref[b], preferred_element_type=jnp.float32)
        picked_ref[...] = (picked[0:rows] + picked[rows : 2 * rows]) + picked[2 * rows : 3 * rows]
        acc = {}
        for h in range(2):
            spread = {}
            for r in range(4):
                lanes = pl.ds(r * tile + b * LANES, LANES)
                values = excite_ref[0, pl.ds(8 * h, 8), lanes].astype(jnp.float32)
                spread[0, r] = paired(values, True)
                spread[1, r] = paired(values, False)
            for q in range(4):
                total = None
                for u in range(2):
                    for r in range(4):
                        term = sqrt_tiles[(q * 2 + u) * 4 + r] * spread[u, r]
                        total = term if total is None else total + term
                acc[h, q] = total
        for j in range(3):
            for m in range(slots):
                for h in range(2):
                    near = picked_ref[pl.ds(8 * h + 2 * j, 8), pl.ds(m * LANES, LANES)]
                    for q in range(4):
                        acc[h, q] = acc[h, q] + weight_tiles[(q * 3 + j) * 9 + m] * near
        for q in range(4):
            lanes = pl.ds(q * tile + b * LANES, LANES)
            first = jnp.exp(acc[0, q]) * width_tiles[0]
            second = jnp.exp(acc[1, q]) * width_tiles[1]
            density_ref[0, pl.ds(0, 8), lanes] = first
            density_ref[0, pl.ds(8, 8), lanes] = second
            low = running(first, True)
            high = running(second, True) + jnp.broadcast_to(low[7:8], low.shape)
            local_ref[0, pl.ds(0, 8), lanes] = low
            local_ref[0, pl.ds(8, 8), lanes] = high
            misfit = counts_ref[pl.ds(0, 8), lanes] * (low - stars_ref[pl.ds(0, 8), lanes]) + counts_ref[
                pl.ds(8, 8), lanes
            ] * (high - stars_ref[pl.ds(8, 8), lanes])
            sums_ref[0, 0:1, lanes] = high[7:8]
            sums_ref[0, 1:2, lanes] = jnp.sum(misfit, axis=0, keepdims=True)


def backward_kernel(
    sqrt_ref, density_ref, local_ref, carries_ref, counts_ref, stars_ref, extinct_ref, grad_ref, sqrt_tiles
):
    tile = density_ref.shape[2] // 4
    blocks = tile // LANES

    @pl.when(pl.program_id(0) == 0)
    def _():
        alternating(sqrt_ref, lambda n, u: ((n // 4) * 2 + u) * 4 + n % 4, 2 * 4 * 4, sqrt_tiles)

    for b in range(blocks):
        flow = {}
        for q in range(4):
            lanes = pl.ds(q * tile + b * LANES, LANES)
            into = carries_ref[0, 0:1, lanes]
            past = carries_ref[0, 1:2, lanes]
            low = local_ref[0, pl.ds(0, 8), lanes] + into
            high = local_ref[0, pl.ds(8, 8), lanes] + into
            extinct_ref[0, pl.ds(0, 8), lanes] = low.astype(extinct_ref.dtype)
            extinct_ref[0, pl.ds(8, 8), lanes] = high.astype(extinct_ref.dtype)
            miss_low = counts_ref[pl.ds(0, 8), lanes] * (low - stars_ref[pl.ds(0, 8), lanes])
            miss_high = counts_ref[pl.ds(8, 8), lanes] * (high - stars_ref[pl.ds(8, 8), lanes])
            behind_high = running(miss_high, False)
            behind_low = running(miss_low, False) + jnp.broadcast_to(behind_high[0:1], behind_high.shape)
            for h, behind in ((0, behind_low), (1, behind_high)):
                moving = density_ref[0, pl.ds(8 * h, 8), lanes] * (behind + past)
                flow[h, q, 0] = paired(moving, True)
                flow[h, q, 1] = paired(moving, False)
        for h in range(2):
            for r in range(4):
                total = None
                for t in range(2):
                    for q in range(4):
                        term = sqrt_tiles[(t * 4 + q) * 4 + r] * flow[h, q, t]
                        total = term if total is None else total + term
                grad_ref[0, pl.ds(8 * h, 8), pl.ds(r * tile + b * LANES, LANES)] = total


def by_parity(values):
    lead = values.shape[:-2]
    shells, width = values.shape[-2:]
    values = values.reshape(lead + (shells // 2, 2, width))
    return jnp.swapaxes(values, -2, -3)


def from_parity(values):
    lead = values.shape[:-3]
    _, shells, width = values.shape[-3:]
    return jnp.swapaxes(values, -2, -3).reshape(lead + (2 * shells, width))


def tiles(values):
    flat = values.reshape(-1)
    return jnp.broadcast_to(flat[:, None, None], (flat.shape[0], 8, LANES))


def local_forward(extended, halo_index, excitations, refine_weights, refine_sqrt, counts, stars, widths):
    samples, shells, _ = extended.shape
    slots, pixels = halo_index.shape
    blocks = pixels // BAND
    window = 3 * BAND
    fine_shells = excitations.shape[1]
    fine_pixels = excitations.shape[2]
    rows = 2 * (fine_shells // 2 + 4)
    split = split_three(extended)
    split = jnp.pad(split, ((0, 0), (0, 0), (0, rows // 2 - shells), (0, 0)))
    split = jnp.repeat(split, 2, axis=2)
    pieces = jnp.stack([split[:, :, :, b * BAND : b * BAND + window] for b in range(blocks)], axis=2)
    pieces = pieces.transpose(1, 2, 0, 3, 4).reshape(samples, blocks, 3 * rows, window)
    starts = (jnp.arange(blocks, dtype=jnp.int32) * BAND)[None, :, None]
    local = halo_index.reshape(slots, blocks, BAND) - starts
    spots = jnp.arange(window, dtype=jnp.int32)[None, :, None, None]
    onehot = (local.transpose(1, 0, 2)[:, None] == spots).astype(jnp.bfloat16)
    onehot = onehot.reshape(blocks, window, slots * BAND)
    half = fine_shells // 2
    smem = pl.BlockSpec(memory_space=pltpu.SMEM)
    whole = lambda shape: pl.BlockSpec(shape, lambda k: (0,) * len(shape))
    per_sample = lambda shape: pl.BlockSpec(shape, lambda k: (k,) + (0,) * (len(shape) - 1))
    return pl.pallas_call(
        forward_kernel,
        grid=(samples,),
        in_specs=[
            smem,
            smem,
            per_sample((1, blocks, 3 * rows, window)),
            whole((blocks, window, slots * BAND)),
            per_sample((1, fine_shells, fine_pixels)),
            whole((fine_shells, fine_pixels)),
            whole((fine_shells, fine_pixels)),
            smem,
        ],
        out_specs=[
            per_sample((1, fine_shells, fine_pixels)),
            per_sample((1, fine_shells, fine_pixels)),
            per_sample((1, 2, fine_pixels)),
        ],
        out_shape=[
            jax.ShapeDtypeStruct((samples, fine_shells, fine_pixels), jnp.float32),
            jax.ShapeDtypeStruct((samples, fine_shells, fine_pixels), jnp.float32),
            jax.ShapeDtypeStruct((samples, 2, fine_pixels), jnp.float32),
        ],
        scratch_shapes=[
            pltpu.VMEM((rows, slots * BAND), jnp.float32),
            pltpu.VMEM((4 * 3 * slots, 8, LANES), jnp.float32),
            pltpu.VMEM((4 * 2 * 4, 8, LANES), jnp.float32),
            pltpu.VMEM((2, 8, LANES), jnp.float32),
        ],
        interpret=INTERPRET,
    )(
        refine_weights.reshape(-1),
        refine_sqrt.astype(jnp.float32).reshape(-1),
        pieces,
        onehot,
        excitations,
        counts,
        stars,
        widths,
    )


def local_backward(refine_sqrt, density, local_cum, carries, counts, stars):
    samples, fine_shells, fine_pixels = density.shape
    smem = pl.BlockSpec(memory_space=pltpu.SMEM)
    whole = lambda shape: pl.BlockSpec(shape, lambda k: (0,) * len(shape))
    per_sample = lambda shape: pl.BlockSpec(shape, lambda k: (k,) + (0,) * (len(shape) - 1))
    return pl.pallas_call(
        backward_kernel,
        grid=(samples,),
        in_specs=[
            smem,
            per_sample((1, fine_shells, fine_pixels)),
            per_sample((1, fine_shells, fine_pixels)),
            per_sample((1, 2, fine_pixels)),
            whole((fine_shells, fine_pixels)),
            whole((fine_shells, fine_pixels)),
        ],
        out_specs=[
            per_sample((1, fine_shells, fine_pixels)),
            per_sample((1, fine_shells, fine_pixels)),
        ],
        out_shape=[
            jax.ShapeDtypeStruct((samples, fine_shells, fine_pixels), jnp.bfloat16),
            jax.ShapeDtypeStruct((samples, fine_shells, fine_pixels), jnp.float32),
        ],
        scratch_shapes=[pltpu.VMEM((2 * 4 * 4, 8, LANES), jnp.float32)],
        interpret=INTERPRET,
    )(refine_sqrt.astype(jnp.float32).reshape(-1), density, local_cum, carries, counts, stars)


def shards(
    coarse_field, excitations, refine_weights, refine_sqrt, halo_index, star_extinction, star_counts
):
    samples, coarse_shells, coarse_pixels = coarse_field.shape
    fine_shells = 2 * coarse_shells
    fine_pixels = 4 * coarse_pixels
    dist_count = lax.axis_size("dist")
    dist_rank = lax.axis_index("dist")
    all_shells = fine_shells * dist_count
    blocked = coarse_field.reshape(samples, coarse_shells, coarse_pixels // BAND, BAND)
    extended = with_halo(blocked, (("dist", 1), ("sky", 2)), 1)
    extended = extended.reshape(samples, coarse_shells + 2, coarse_pixels + 2 * BAND)
    shells = dist_rank * fine_shells + jnp.arange(fine_shells, dtype=jnp.int32)
    middle = (shells.astype(jnp.float32) + 0.5) / all_shells
    widths = 3.0 * jnp.exp(3.0 * middle - 3.0) / all_shells
    counts = star_counts.astype(jnp.float32)
    density, local_cum, sums = local_forward(
        extended, halo_index, excitations, refine_weights, refine_sqrt, counts, star_extinction, widths
    )
    weight = jnp.sum(counts, axis=0, keepdims=True)
    carry_in, carry_out = block_carries(sums[:, 0], sums[:, 1], weight, "dist")
    carries = jnp.stack([carry_in, carry_out], axis=1)
    return local_backward(refine_sqrt, density, local_cum, carries, counts, star_extinction)


def solution(mesh):
    placed = (
        P(None, "dist", "sky"),
        P(None, "dist", "sky"),
        P(),
        P(),
        P(None, "sky"),
        P("dist", "sky"),
        P("dist", "sky"),
    )
    return jax.shard_map(
        shards,
        mesh=mesh,
        in_specs=placed,
        out_specs=(P(None, "dist", "sky"), P(None, "dist", "sky")),
        check_vma=False,
    )
```

```python
import jax
import jax.numpy as jnp
from jax import lax
from jax.experimental import pallas as pl
from jax.experimental.pallas import tpu as pltpu
from jax.sharding import PartitionSpec as P

BAND = 128


exact_mode = lax.Precision.HIGHEST


def with_halo(block, sides, width):
    for axis, dim in sides:
        count = lax.axis_size(axis)
        forward = [(i, i + 1) for i in range(count - 1)]
        backward = [(target, source) for source, target in forward]
        low = lax.ppermute(
            lax.slice_in_dim(block, block.shape[dim] - width, None, axis=dim), axis, forward
        )
        high = lax.ppermute(lax.slice_in_dim(block, 0, width, axis=dim), axis, backward)
        block = jnp.concatenate([low, block, high], axis=dim)
    return block


def block_carries(totals, partial, weight, axis):
    count = lax.axis_size(axis)
    rows, pixels = totals.shape
    width = pixels // count
    packed = jnp.concatenate([totals, partial, weight], axis=0)
    packed = packed.reshape(packed.shape[0], count, width).transpose(1, 0, 2)
    mine = lax.all_to_all(packed, axis, 0, 0, tiled=True)
    block_totals = mine[:, :rows]
    block_partial = mine[:, rows : 2 * rows]
    block_weight = mine[:, 2 * rows :]
    blocks, height, width = block_totals.shape
    order = jnp.arange(blocks, dtype=jnp.int32)
    earlier = (order[None, :] < order[:, None]).astype(jnp.float32)
    flat = lambda values: values.reshape(blocks, -1)
    carry_in = jnp.dot(earlier, flat(block_totals), precision=exact_mode).reshape(blocks, height, width)
    block_misfit = block_partial + block_weight * carry_in
    carry_out = jnp.dot(earlier.T, flat(block_misfit), precision=exact_mode).reshape(blocks, height, width)
    back = lax.all_to_all(jnp.concatenate([carry_in, carry_out], axis=1), axis, 0, 0, tiled=True)
    back = back.transpose(1, 0, 2).reshape(2 * rows, pixels)
    return back[:rows], back[rows:]


def split_three(values):
    high = lax.reduce_precision(values, exponent_bits=8, mantissa_bits=7)
    rest = values - high
    middle = lax.reduce_precision(rest, exponent_bits=8, mantissa_bits=7)
    low = rest - middle
    return jnp.stack([high, middle, low]).astype(jnp.bfloat16)


def gather_nearby(extended, halo_index):
    samples, shells, _ = extended.shape
    slots, pixels = halo_index.shape
    blocks = pixels // BAND
    window = 3 * BAND
    windows = jnp.stack(
        [extended[:, :, b * BAND : b * BAND + window] for b in range(blocks)]
    ).reshape(blocks, samples * shells, window)
    pieces = split_three(windows).transpose(1, 0, 2, 3).reshape(blocks, 3 * samples * shells, window)
    starts = (jnp.arange(blocks, dtype=jnp.int32) * BAND)[None, :, None]
    local = halo_index.reshape(slots, blocks, BAND) - starts
    spots = jnp.arange(window, dtype=jnp.int32)[None, :, None, None]
    onehot = (local.transpose(1, 0, 2)[:, None] == spots).astype(jnp.bfloat16)
    onehot = onehot.reshape(blocks, window, slots * BAND)
    picked = jnp.einsum("bxw,bwn->bxn", pieces, onehot, preferred_element_type=jnp.float32)
    picked = picked.reshape(blocks, 3, samples, shells, slots, BAND)
    picked = (picked[:, 0] + picked[:, 1]) + picked[:, 2]
    return picked.transpose(1, 2, 3, 0, 4).reshape(samples, shells, slots, pixels)


INTERPRET = False
LANES = 128


def shifted(values, amount, toward_end):
    rows = values.shape[0]
    row = lax.broadcasted_iota(jnp.int32, values.shape, 0)
    if toward_end:
        return jnp.where(row >= amount, pltpu.roll(values, amount, 0), 0.0)
    return jnp.where(row < rows - amount, pltpu.roll(values, rows - amount, 0), 0.0)


def running(values, toward_end):
    for amount in (1, 2, 4):
        values = values + shifted(values, amount, toward_end)
    return values


def paired(values, odd_from_even):
    row = lax.broadcasted_iota(jnp.int32, values.shape, 0)
    if odd_from_even:
        return jnp.where(row % 2 == 1, shifted(values, 1, True), values)
    return jnp.where(row % 2 == 0, shifted(values, 1, False), values)


def alternating(table, index_of, count, target):
    row = lax.broadcasted_iota(jnp.int32, (8, LANES), 0)
    for n in range(count):
        even = jnp.full((8, LANES), table[index_of(n, 0)], jnp.float32)
        odd = jnp.full((8, LANES), table[index_of(n, 1)], jnp.float32)
        target[n] = jnp.where(row % 2 == 0, even, odd)


def forward_kernel(
    weights_ref, sqrt_ref, pieces_ref, onehot_ref, excite_ref, counts_ref, stars_ref, widths_ref,
    density_ref, local_ref, sums_ref, picked_ref, weight_tiles, sqrt_tiles, width_tiles,
):
    blocks = onehot_ref.shape[0]
    slots = onehot_ref.shape[2] // LANES
    tile = blocks * LANES
    rows = picked_ref.shape[0]

    @pl.when(pl.program_id(0) == 0)
    def _():
        alternating(weights_ref, lambda n, t: t * 4 * 3 * slots + n, 4 * 3 * slots, weight_tiles)
        alternating(sqrt_ref, lambda n, t: t * 4 * 2 * 4 + n, 4 * 2 * 4, sqrt_tiles)
        row = lax.broadcasted_iota(jnp.int32, (8, LANES), 0)
        for h in range(2):
            column = jnp.zeros((8, LANES), jnp.float32)
            for i in range(8):
                column = jnp.where(row == i, widths_ref[8 * h + i], column)
            width_tiles[h] = column

    for b in range(blocks):
        picked = jnp.dot(pieces_ref[0, b], onehot_ref[b], preferred_element_type=jnp.float32)
        picked_ref[...] = (picked[0:rows] + picked[rows : 2 * rows]) + picked[2 * rows : 3 * rows]
        acc = {}
        for h in range(2):
            spread = {}
            for r in range(4):
                lanes = pl.ds(r * tile + b * LANES, LANES)
                values = excite_ref[0, pl.ds(8 * h, 8), lanes].astype(jnp.float32)
                spread[0, r] = paired(values, True)
                spread[1, r] = paired(values, False)
            for q in range(4):
                total = None
                for u in range(2):
                    for r in range(4):
                        term = sqrt_tiles[(q * 2 + u) * 4 + r] * spread[u, r]
                        total = term if total is None else total + term
                acc[h, q] = total
        for j in range(3):
            for m in range(slots):
                for h in range(2):
                    near = picked_ref[pl.ds(8 * h + 2 * j, 8), pl.ds(m * LANES, LANES)]
                    for q in range(4):
                        acc[h, q] = acc[h, q] + weight_tiles[(q * 3 + j) * 9 + m] * near
        for q in range(4):
            lanes = pl.ds(q * tile + b * LANES, LANES)
            first = jnp.exp(acc[0, q]) * width_tiles[0]
            second = jnp.exp(acc[1, q]) * width_tiles[1]
            density_ref[0, pl.ds(0, 8), lanes] = first
            density_ref[0, pl.ds(8, 8), lanes] = second
            low = running(first, True)
            high = running(second, True) + jnp.broadcast_to(low[7:8], low.shape)
            local_ref[0, pl.ds(0, 8), lanes] = low
            local_ref[0, pl.ds(8, 8), lanes] = high
            counts_low = counts_ref[pl.ds(0, 8), lanes]
            counts_high = counts_ref[pl.ds(8, 8), lanes]
            misfit = counts_low * (low - stars_ref[pl.ds(0, 8), lanes]) + counts_high * (
                high - stars_ref[pl.ds(8, 8), lanes]
            )
            sums_ref[0, 0:1, lanes] = high[7:8]
            sums_ref[0, 1:2, lanes] = jnp.sum(misfit, axis=0, keepdims=True)
            sums_ref[0, 2:3, lanes] = jnp.sum(counts_low + counts_high, axis=0, keepdims=True)


def backward_kernel(
    sqrt_ref, density_ref, local_ref, carries_ref, counts_ref, stars_ref, extinct_ref, grad_ref, sqrt_tiles
):
    tile = density_ref.shape[2] // 4
    blocks = tile // LANES

    @pl.when(pl.program_id(0) == 0)
    def _():
        alternating(sqrt_ref, lambda n, u: ((n // 4) * 2 + u) * 4 + n % 4, 2 * 4 * 4, sqrt_tiles)

    for b in range(blocks):
        flow = {}
        for q in range(4):
            lanes = pl.ds(q * tile + b * LANES, LANES)
            into = carries_ref[0, 0:1, lanes]
            past = carries_ref[0, 1:2, lanes]
            low = local_ref[0, pl.ds(0, 8), lanes] + into
            high = local_ref[0, pl.ds(8, 8), lanes] + into
            extinct_ref[0, pl.ds(0, 8), lanes] = low.astype(extinct_ref.dtype)
            extinct_ref[0, pl.ds(8, 8), lanes] = high.astype(extinct_ref.dtype)
            miss_low = counts_ref[pl.ds(0, 8), lanes] * (low - stars_ref[pl.ds(0, 8), lanes])
            miss_high = counts_ref[pl.ds(8, 8), lanes] * (high - stars_ref[pl.ds(8, 8), lanes])
            behind_high = running(miss_high, False)
            behind_low = running(miss_low, False) + jnp.broadcast_to(behind_high[0:1], behind_high.shape)
            for h, behind in ((0, behind_low), (1, behind_high)):
                moving = density_ref[0, pl.ds(8 * h, 8), lanes] * (behind + past)
                flow[h, q, 0] = paired(moving, True)
                flow[h, q, 1] = paired(moving, False)
        for h in range(2):
            for r in range(4):
                total = None
                for t in range(2):
                    for q in range(4):
                        term = sqrt_tiles[(t * 4 + q) * 4 + r] * flow[h, q, t]
                        total = term if total is None else total + term
                grad_ref[0, pl.ds(8 * h, 8), pl.ds(r * tile + b * LANES, LANES)] = total


def by_parity(values):
    lead = values.shape[:-2]
    shells, width = values.shape[-2:]
    values = values.reshape(lead + (shells // 2, 2, width))
    return jnp.swapaxes(values, -2, -3)


def from_parity(values):
    lead = values.shape[:-3]
    _, shells, width = values.shape[-3:]
    return jnp.swapaxes(values, -2, -3).reshape(lead + (2 * shells, width))


def tiles(values):
    flat = values.reshape(-1)
    return jnp.broadcast_to(flat[:, None, None], (flat.shape[0], 8, LANES))


def local_forward(extended, halo_index, excitations, refine_weights, refine_sqrt, counts, stars, widths):
    samples, shells, _ = extended.shape
    slots, pixels = halo_index.shape
    blocks = pixels // BAND
    window = 3 * BAND
    fine_shells = excitations.shape[1]
    fine_pixels = excitations.shape[2]
    rows = 2 * (fine_shells // 2 + 4)
    split = split_three(extended)
    split = jnp.pad(split, ((0, 0), (0, 0), (0, rows // 2 - shells), (0, 0)))
    split = jnp.repeat(split, 2, axis=2)
    pieces = jnp.stack([split[:, :, :, b * BAND : b * BAND + window] for b in range(blocks)], axis=2)
    pieces = pieces.transpose(1, 2, 0, 3, 4).reshape(samples, blocks, 3 * rows, window)
    starts = (jnp.arange(blocks, dtype=jnp.int32) * BAND)[None, :, None]
    local = halo_index.reshape(slots, blocks, BAND) - starts
    spots = jnp.arange(window, dtype=jnp.int32)[None, :, None, None]
    onehot = (local.transpose(1, 0, 2)[:, None] == spots).astype(jnp.bfloat16)
    onehot = onehot.reshape(blocks, window, slots * BAND)
    half = fine_shells // 2
    smem = pl.BlockSpec(memory_space=pltpu.SMEM)
    whole = lambda shape: pl.BlockSpec(shape, lambda k: (0,) * len(shape))
    per_sample = lambda shape: pl.BlockSpec(shape, lambda k: (k,) + (0,) * (len(shape) - 1))
    return pl.pallas_call(
        forward_kernel,
        grid=(samples,),
        in_specs=[
            smem,
            smem,
            per_sample((1, blocks, 3 * rows, window)),
            whole((blocks, window, slots * BAND)),
            per_sample((1, fine_shells, fine_pixels)),
            whole((fine_shells, fine_pixels)),
            whole((fine_shells, fine_pixels)),
            smem,
        ],
        out_specs=[
            per_sample((1, fine_shells, fine_pixels)),
            per_sample((1, fine_shells, fine_pixels)),
            per_sample((1, 3, fine_pixels)),
        ],
        out_shape=[
            jax.ShapeDtypeStruct((samples, fine_shells, fine_pixels), jnp.float32),
            jax.ShapeDtypeStruct((samples, fine_shells, fine_pixels), jnp.float32),
            jax.ShapeDtypeStruct((samples, 3, fine_pixels), jnp.float32),
        ],
        scratch_shapes=[
            pltpu.VMEM((rows, slots * BAND), jnp.float32),
            pltpu.VMEM((4 * 3 * slots, 8, LANES), jnp.float32),
            pltpu.VMEM((4 * 2 * 4, 8, LANES), jnp.float32),
            pltpu.VMEM((2, 8, LANES), jnp.float32),
        ],
        interpret=INTERPRET,
    )(
        refine_weights.reshape(-1),
        refine_sqrt.astype(jnp.float32).reshape(-1),
        pieces,
        onehot,
        excitations,
        counts,
        stars,
        widths,
    )


def local_backward(refine_sqrt, density, local_cum, carries, counts, stars):
    samples, fine_shells, fine_pixels = density.shape
    smem = pl.BlockSpec(memory_space=pltpu.SMEM)
    whole = lambda shape: pl.BlockSpec(shape, lambda k: (0,) * len(shape))
    per_sample = lambda shape: pl.BlockSpec(shape, lambda k: (k,) + (0,) * (len(shape) - 1))
    return pl.pallas_call(
        backward_kernel,
        grid=(samples,),
        in_specs=[
            smem,
            per_sample((1, fine_shells, fine_pixels)),
            per_sample((1, fine_shells, fine_pixels)),
            per_sample((1, 2, fine_pixels)),
            whole((fine_shells, fine_pixels)),
            whole((fine_shells, fine_pixels)),
        ],
        out_specs=[
            per_sample((1, fine_shells, fine_pixels)),
            per_sample((1, fine_shells, fine_pixels)),
        ],
        out_shape=[
            jax.ShapeDtypeStruct((samples, fine_shells, fine_pixels), jnp.bfloat16),
            jax.ShapeDtypeStruct((samples, fine_shells, fine_pixels), jnp.float32),
        ],
        scratch_shapes=[pltpu.VMEM((2 * 4 * 4, 8, LANES), jnp.float32)],
        interpret=INTERPRET,
    )(refine_sqrt.astype(jnp.float32).reshape(-1), density, local_cum, carries, counts, stars)


def shards(
    coarse_field, excitations, refine_weights, refine_sqrt, halo_index, star_extinction, star_counts
):
    samples, coarse_shells, coarse_pixels = coarse_field.shape
    fine_shells = 2 * coarse_shells
    fine_pixels = 4 * coarse_pixels
    dist_count = lax.axis_size("dist")
    dist_rank = lax.axis_index("dist")
    all_shells = fine_shells * dist_count
    blocked = coarse_field.reshape(samples, coarse_shells, coarse_pixels // BAND, BAND)
    extended = with_halo(blocked, (("dist", 1), ("sky", 2)), 1)
    extended = extended.reshape(samples, coarse_shells + 2, coarse_pixels + 2 * BAND)
    shells = dist_rank * fine_shells + jnp.arange(fine_shells, dtype=jnp.int32)
    middle = (shells.astype(jnp.float32) + 0.5) / all_shells
    widths = 3.0 * jnp.exp(3.0 * middle - 3.0) / all_shells
    counts = star_counts.astype(jnp.float32)
    density, local_cum, sums = local_forward(
        extended, halo_index, excitations, refine_weights, refine_sqrt, counts, star_extinction, widths
    )
    carry_in, carry_out = block_carries(sums[:, 0], sums[:, 1], sums[:1, 2], "dist")
    carries = jnp.stack([carry_in, carry_out], axis=1)
    return local_backward(refine_sqrt, density, local_cum, carries, counts, star_extinction)


def solution(mesh):
    placed = (
        P(None, "dist", "sky"),
        P(None, "dist", "sky"),
        P(),
        P(),
        P(None, "sky"),
        P("dist", "sky"),
        P("dist", "sky"),
    )
    return jax.shard_map(
        shards,
        mesh=mesh,
        in_specs=placed,
        out_specs=(P(None, "dist", "sky"), P(None, "dist", "sky")),
        check_vma=False,
    )
```

```python
import jax
import jax.numpy as jnp
from jax import lax
from jax.experimental import pallas as pl
from jax.experimental.pallas import tpu as pltpu
from jax.sharding import PartitionSpec as P

BAND = 128


exact_mode = lax.Precision.HIGHEST


def with_halo(block, sides, width):
    for axis, dim in sides:
        count = lax.axis_size(axis)
        forward = [(i, i + 1) for i in range(count - 1)]
        backward = [(target, source) for source, target in forward]
        low = lax.ppermute(
            lax.slice_in_dim(block, block.shape[dim] - width, None, axis=dim), axis, forward
        )
        high = lax.ppermute(lax.slice_in_dim(block, 0, width, axis=dim), axis, backward)
        block = jnp.concatenate([low, block, high], axis=dim)
    return block


def block_carries(totals, partial, weight, axis):
    count = lax.axis_size(axis)
    rows, pixels = totals.shape
    width = pixels // count
    packed = jnp.concatenate([totals, partial, weight], axis=0)
    packed = packed.reshape(packed.shape[0], count, width).transpose(1, 0, 2)
    mine = lax.all_to_all(packed, axis, 0, 0, tiled=True)
    block_totals = mine[:, :rows]
    block_partial = mine[:, rows : 2 * rows]
    block_weight = mine[:, 2 * rows :]
    blocks, height, width = block_totals.shape
    order = jnp.arange(blocks, dtype=jnp.int32)
    earlier = (order[None, :] < order[:, None]).astype(jnp.float32)
    flat = lambda values: values.reshape(blocks, -1)
    carry_in = jnp.dot(earlier, flat(block_totals), precision=exact_mode).reshape(blocks, height, width)
    block_misfit = block_partial + block_weight * carry_in
    carry_out = jnp.dot(earlier.T, flat(block_misfit), precision=exact_mode).reshape(blocks, height, width)
    paired_carries = jnp.stack([carry_in, carry_out], axis=2).reshape(blocks, 2 * rows, width)
    back = lax.all_to_all(paired_carries, axis, 0, 0, tiled=True)
    return back.transpose(1, 0, 2).reshape(rows, 2, pixels)


def split_three(values):
    high = lax.reduce_precision(values, exponent_bits=8, mantissa_bits=7)
    rest = values - high
    middle = lax.reduce_precision(rest, exponent_bits=8, mantissa_bits=7)
    low = rest - middle
    return jnp.stack([high, middle, low]).astype(jnp.bfloat16)


def gather_nearby(extended, halo_index):
    samples, shells, _ = extended.shape
    slots, pixels = halo_index.shape
    blocks = pixels // BAND
    window = 3 * BAND
    windows = jnp.stack(
        [extended[:, :, b * BAND : b * BAND + window] for b in range(blocks)]
    ).reshape(blocks, samples * shells, window)
    pieces = split_three(windows).transpose(1, 0, 2, 3).reshape(blocks, 3 * samples * shells, window)
    starts = (jnp.arange(blocks, dtype=jnp.int32) * BAND)[None, :, None]
    local = halo_index.reshape(slots, blocks, BAND) - starts
    spots = jnp.arange(window, dtype=jnp.int32)[None, :, None, None]
    onehot = (local.transpose(1, 0, 2)[:, None] == spots).astype(jnp.bfloat16)
    onehot = onehot.reshape(blocks, window, slots * BAND)
    picked = jnp.einsum("bxw,bwn->bxn", pieces, onehot, preferred_element_type=jnp.float32)
    picked = picked.reshape(blocks, 3, samples, shells, slots, BAND)
    picked = (picked[:, 0] + picked[:, 1]) + picked[:, 2]
    return picked.transpose(1, 2, 3, 0, 4).reshape(samples, shells, slots, pixels)


INTERPRET = False
LANES = 128


def shifted(values, amount, toward_end):
    rows = values.shape[0]
    row = lax.broadcasted_iota(jnp.int32, values.shape, 0)
    if toward_end:
        return jnp.where(row >= amount, pltpu.roll(values, amount, 0), 0.0)
    return jnp.where(row < rows - amount, pltpu.roll(values, rows - amount, 0), 0.0)


def running(values, toward_end):
    for amount in (1, 2, 4):
        values = values + shifted(values, amount, toward_end)
    return values


def paired(values, odd_from_even):
    row = lax.broadcasted_iota(jnp.int32, values.shape, 0)
    if odd_from_even:
        return jnp.where(row % 2 == 1, shifted(values, 1, True), values)
    return jnp.where(row % 2 == 0, shifted(values, 1, False), values)


def alternating(table, index_of, count, target):
    row = lax.broadcasted_iota(jnp.int32, (8, LANES), 0)
    for n in range(count):
        even = jnp.full((8, LANES), table[index_of(n, 0)], jnp.float32)
        odd = jnp.full((8, LANES), table[index_of(n, 1)], jnp.float32)
        target[n] = jnp.where(row % 2 == 0, even, odd)


def forward_kernel(
    weights_ref, sqrt_ref, pieces_ref, onehot_ref, excite_ref, counts_ref, stars_ref, widths_ref,
    density_ref, local_ref, sums_ref, picked_ref, weight_tiles, sqrt_tiles, width_tiles,
):
    blocks = onehot_ref.shape[0]
    slots = onehot_ref.shape[2] // LANES
    tile = blocks * LANES
    rows = picked_ref.shape[0]

    @pl.when(pl.program_id(0) == 0)
    def _():
        alternating(weights_ref, lambda n, t: t * 4 * 3 * slots + n, 4 * 3 * slots, weight_tiles)
        alternating(sqrt_ref, lambda n, t: t * 4 * 2 * 4 + n, 4 * 2 * 4, sqrt_tiles)
        row = lax.broadcasted_iota(jnp.int32, (8, LANES), 0)
        for h in range(2):
            column = jnp.zeros((8, LANES), jnp.float32)
            for i in range(8):
                column = jnp.where(row == i, widths_ref[8 * h + i], column)
            width_tiles[h] = column

    for b in range(blocks):
        picked = jnp.dot(pieces_ref[0, b], onehot_ref[b], preferred_element_type=jnp.float32)
        picked_ref[...] = (picked[0:rows] + picked[rows : 2 * rows]) + picked[2 * rows : 3 * rows]
        acc = {}
        for h in range(2):
            spread = {}
            for r in range(4):
                lanes = pl.ds(r * tile + b * LANES, LANES)
                values = excite_ref[0, pl.ds(8 * h, 8), lanes].astype(jnp.float32)
                spread[0, r] = paired(values, True)
                spread[1, r] = paired(values, False)
            for q in range(4):
                total = None
                for u in range(2):
                    for r in range(4):
                        term = sqrt_tiles[(q * 2 + u) * 4 + r] * spread[u, r]
                        total = term if total is None else total + term
                acc[h, q] = total
        for j in range(3):
            for m in range(slots):
                for h in range(2):
                    near = picked_ref[pl.ds(8 * h + 2 * j, 8), pl.ds(m * LANES, LANES)]
                    for q in range(4):
                        acc[h, q] = acc[h, q] + weight_tiles[(q * 3 + j) * 9 + m] * near
        for q in range(4):
            lanes = pl.ds(q * tile + b * LANES, LANES)
            first = jnp.exp(acc[0, q]) * width_tiles[0]
            second = jnp.exp(acc[1, q]) * width_tiles[1]
            density_ref[0, pl.ds(0, 8), lanes] = first
            density_ref[0, pl.ds(8, 8), lanes] = second
            low = running(first, True)
            high = running(second, True) + jnp.broadcast_to(low[7:8], low.shape)
            local_ref[0, pl.ds(0, 8), lanes] = low
            local_ref[0, pl.ds(8, 8), lanes] = high
            misfit = counts_ref[pl.ds(0, 8), lanes] * (low - stars_ref[pl.ds(0, 8), lanes]) + counts_ref[
                pl.ds(8, 8), lanes
            ] * (high - stars_ref[pl.ds(8, 8), lanes])
            sums_ref[0, 0:1, lanes] = high[7:8]
            sums_ref[0, 1:2, lanes] = jnp.sum(misfit, axis=0, keepdims=True)


def backward_kernel(
    sqrt_ref, density_ref, local_ref, carries_ref, counts_ref, stars_ref, extinct_ref, grad_ref, sqrt_tiles
):
    tile = density_ref.shape[2] // 4
    blocks = tile // LANES

    @pl.when(pl.program_id(0) == 0)
    def _():
        alternating(sqrt_ref, lambda n, u: ((n // 4) * 2 + u) * 4 + n % 4, 2 * 4 * 4, sqrt_tiles)

    for b in range(blocks):
        flow = {}
        for q in range(4):
            lanes = pl.ds(q * tile + b * LANES, LANES)
            into = carries_ref[0, 0:1, lanes]
            past = carries_ref[0, 1:2, lanes]
            low = local_ref[0, pl.ds(0, 8), lanes] + into
            high = local_ref[0, pl.ds(8, 8), lanes] + into
            extinct_ref[0, pl.ds(0, 8), lanes] = low.astype(extinct_ref.dtype)
            extinct_ref[0, pl.ds(8, 8), lanes] = high.astype(extinct_ref.dtype)
            miss_low = counts_ref[pl.ds(0, 8), lanes] * (low - stars_ref[pl.ds(0, 8), lanes])
            miss_high = counts_ref[pl.ds(8, 8), lanes] * (high - stars_ref[pl.ds(8, 8), lanes])
            behind_high = running(miss_high, False)
            behind_low = running(miss_low, False) + jnp.broadcast_to(behind_high[0:1], behind_high.shape)
            for h, behind in ((0, behind_low), (1, behind_high)):
                moving = density_ref[0, pl.ds(8 * h, 8), lanes] * (behind + past)
                flow[h, q, 0] = paired(moving, True)
                flow[h, q, 1] = paired(moving, False)
        for h in range(2):
            for r in range(4):
                total = None
                for t in range(2):
                    for q in range(4):
                        term = sqrt_tiles[(t * 4 + q) * 4 + r] * flow[h, q, t]
                        total = term if total is None else total + term
                grad_ref[0, pl.ds(8 * h, 8), pl.ds(r * tile + b * LANES, LANES)] = total


def by_parity(values):
    lead = values.shape[:-2]
    shells, width = values.shape[-2:]
    values = values.reshape(lead + (shells // 2, 2, width))
    return jnp.swapaxes(values, -2, -3)


def from_parity(values):
    lead = values.shape[:-3]
    _, shells, width = values.shape[-3:]
    return jnp.swapaxes(values, -2, -3).reshape(lead + (2 * shells, width))


def tiles(values):
    flat = values.reshape(-1)
    return jnp.broadcast_to(flat[:, None, None], (flat.shape[0], 8, LANES))


def local_forward(extended, halo_index, excitations, refine_weights, refine_sqrt, counts, stars, widths):
    samples, shells, _ = extended.shape
    slots, pixels = halo_index.shape
    blocks = pixels // BAND
    window = 3 * BAND
    fine_shells = excitations.shape[1]
    fine_pixels = excitations.shape[2]
    rows = 2 * (fine_shells // 2 + 4)
    split = split_three(extended)
    split = jnp.pad(split, ((0, 0), (0, 0), (0, rows // 2 - shells), (0, 0)))
    split = jnp.repeat(split, 2, axis=2)
    pieces = jnp.stack([split[:, :, :, b * BAND : b * BAND + window] for b in range(blocks)], axis=2)
    pieces = pieces.transpose(1, 2, 0, 3, 4).reshape(samples, blocks, 3 * rows, window)
    starts = (jnp.arange(blocks, dtype=jnp.int32) * BAND)[None, :, None]
    local = halo_index.reshape(slots, blocks, BAND) - starts
    spots = jnp.arange(window, dtype=jnp.int32)[None, :, None, None]
    onehot = (local.transpose(1, 0, 2)[:, None] == spots).astype(jnp.bfloat16)
    onehot = onehot.reshape(blocks, window, slots * BAND)
    half = fine_shells // 2
    smem = pl.BlockSpec(memory_space=pltpu.SMEM)
    whole = lambda shape: pl.BlockSpec(shape, lambda k: (0,) * len(shape))
    per_sample = lambda shape: pl.BlockSpec(shape, lambda k: (k,) + (0,) * (len(shape) - 1))
    return pl.pallas_call(
        forward_kernel,
        grid=(samples,),
        in_specs=[
            smem,
            smem,
            per_sample((1, blocks, 3 * rows, window)),
            whole((blocks, window, slots * BAND)),
            per_sample((1, fine_shells, fine_pixels)),
            whole((fine_shells, fine_pixels)),
            whole((fine_shells, fine_pixels)),
            smem,
        ],
        out_specs=[
            per_sample((1, fine_shells, fine_pixels)),
            per_sample((1, fine_shells, fine_pixels)),
            per_sample((1, 2, fine_pixels)),
        ],
        out_shape=[
            jax.ShapeDtypeStruct((samples, fine_shells, fine_pixels), jnp.float32),
            jax.ShapeDtypeStruct((samples, fine_shells, fine_pixels), jnp.float32),
            jax.ShapeDtypeStruct((samples, 2, fine_pixels), jnp.float32),
        ],
        scratch_shapes=[
            pltpu.VMEM((rows, slots * BAND), jnp.float32),
            pltpu.VMEM((4 * 3 * slots, 8, LANES), jnp.float32),
            pltpu.VMEM((4 * 2 * 4, 8, LANES), jnp.float32),
            pltpu.VMEM((2, 8, LANES), jnp.float32),
        ],
        interpret=INTERPRET,
    )(
        refine_weights.reshape(-1),
        refine_sqrt.astype(jnp.float32).reshape(-1),
        pieces,
        onehot,
        excitations,
        counts,
        stars,
        widths,
    )


def local_backward(refine_sqrt, density, local_cum, carries, counts, stars):
    samples, fine_shells, fine_pixels = density.shape
    smem = pl.BlockSpec(memory_space=pltpu.SMEM)
    whole = lambda shape: pl.BlockSpec(shape, lambda k: (0,) * len(shape))
    per_sample = lambda shape: pl.BlockSpec(shape, lambda k: (k,) + (0,) * (len(shape) - 1))
    return pl.pallas_call(
        backward_kernel,
        grid=(samples,),
        in_specs=[
            smem,
            per_sample((1, fine_shells, fine_pixels)),
            per_sample((1, fine_shells, fine_pixels)),
            per_sample((1, 2, fine_pixels)),
            whole((fine_shells, fine_pixels)),
            whole((fine_shells, fine_pixels)),
        ],
        out_specs=[
            per_sample((1, fine_shells, fine_pixels)),
            per_sample((1, fine_shells, fine_pixels)),
        ],
        out_shape=[
            jax.ShapeDtypeStruct((samples, fine_shells, fine_pixels), jnp.bfloat16),
            jax.ShapeDtypeStruct((samples, fine_shells, fine_pixels), jnp.float32),
        ],
        scratch_shapes=[pltpu.VMEM((2 * 4 * 4, 8, LANES), jnp.float32)],
        interpret=INTERPRET,
    )(refine_sqrt.astype(jnp.float32).reshape(-1), density, local_cum, carries, counts, stars)


def shards(
    coarse_field, excitations, refine_weights, refine_sqrt, halo_index, star_extinction, star_counts
):
    samples, coarse_shells, coarse_pixels = coarse_field.shape
    fine_shells = 2 * coarse_shells
    fine_pixels = 4 * coarse_pixels
    dist_count = lax.axis_size("dist")
    dist_rank = lax.axis_index("dist")
    all_shells = fine_shells * dist_count
    blocked = coarse_field.reshape(samples, coarse_shells, coarse_pixels // BAND, BAND)
    extended = with_halo(blocked, (("dist", 1), ("sky", 2)), 1)
    extended = extended.reshape(samples, coarse_shells + 2, coarse_pixels + 2 * BAND)
    shells = dist_rank * fine_shells + jnp.arange(fine_shells, dtype=jnp.int32)
    middle = (shells.astype(jnp.float32) + 0.5) / all_shells
    widths = 3.0 * jnp.exp(3.0 * middle - 3.0) / all_shells
    counts = star_counts.astype(jnp.float32)
    density, local_cum, sums = local_forward(
        extended, halo_index, excitations, refine_weights, refine_sqrt, counts, star_extinction, widths
    )
    weight = jnp.sum(counts, axis=0, keepdims=True)
    carries = block_carries(sums[:, 0], sums[:, 1], weight, "dist")
    return local_backward(refine_sqrt, density, local_cum, carries, counts, star_extinction)


def solution(mesh):
    placed = (
        P(None, "dist", "sky"),
        P(None, "dist", "sky"),
        P(),
        P(),
        P(None, "sky"),
        P("dist", "sky"),
        P("dist", "sky"),
    )
    return jax.shard_map(
        shards,
        mesh=mesh,
        in_specs=placed,
        out_specs=(P(None, "dist", "sky"), P(None, "dist", "sky")),
        check_vma=False,
    )
```

```python
import jax
import jax.numpy as jnp
from jax import lax
from jax.experimental import pallas as pl
from jax.experimental.pallas import tpu as pltpu
from jax.sharding import PartitionSpec as P

BAND = 128


exact_mode = lax.Precision.HIGHEST


def with_halo(block, sides, width):
    for axis, dim in sides:
        count = lax.axis_size(axis)
        forward = [(i, i + 1) for i in range(count - 1)]
        backward = [(target, source) for source, target in forward]
        low = lax.ppermute(
            lax.slice_in_dim(block, block.shape[dim] - width, None, axis=dim), axis, forward
        )
        high = lax.ppermute(lax.slice_in_dim(block, 0, width, axis=dim), axis, backward)
        block = jnp.concatenate([low, block, high], axis=dim)
    return block


def block_carries(totals, partial, weight, axis):
    count = lax.axis_size(axis)
    rows, pixels = totals.shape
    width = pixels // count
    packed = jnp.concatenate([totals, partial, weight], axis=0)
    packed = packed.reshape(packed.shape[0], count, width).transpose(1, 0, 2)
    mine = lax.all_to_all(packed, axis, 0, 0, tiled=True)
    block_totals = mine[:, :rows]
    block_partial = mine[:, rows : 2 * rows]
    block_weight = mine[:, 2 * rows :]
    blocks, height, width = block_totals.shape
    order = jnp.arange(blocks, dtype=jnp.int32)
    earlier = (order[None, :] < order[:, None]).astype(jnp.float32)
    flat = lambda values: values.reshape(blocks, -1)
    carry_in = jnp.dot(earlier, flat(block_totals), precision=exact_mode).reshape(blocks, height, width)
    block_misfit = block_partial + block_weight * carry_in
    carry_out = jnp.dot(earlier.T, flat(block_misfit), precision=exact_mode).reshape(blocks, height, width)
    paired_carries = jnp.stack([carry_in, carry_out], axis=2).reshape(blocks, 2 * rows, width)
    back = lax.all_to_all(paired_carries, axis, 0, 0, tiled=True)
    return back.transpose(1, 0, 2).reshape(rows, 2, pixels)


def split_three(values):
    high = lax.reduce_precision(values, exponent_bits=8, mantissa_bits=7)
    rest = values - high
    middle = lax.reduce_precision(rest, exponent_bits=8, mantissa_bits=7)
    low = rest - middle
    return jnp.stack([high, middle, low]).astype(jnp.bfloat16)


def gather_nearby(extended, halo_index):
    samples, shells, _ = extended.shape
    slots, pixels = halo_index.shape
    blocks = pixels // BAND
    window = 3 * BAND
    windows = jnp.stack(
        [extended[:, :, b * BAND : b * BAND + window] for b in range(blocks)]
    ).reshape(blocks, samples * shells, window)
    pieces = split_three(windows).transpose(1, 0, 2, 3).reshape(blocks, 3 * samples * shells, window)
    starts = (jnp.arange(blocks, dtype=jnp.int32) * BAND)[None, :, None]
    local = halo_index.reshape(slots, blocks, BAND) - starts
    spots = jnp.arange(window, dtype=jnp.int32)[None, :, None, None]
    onehot = (local.transpose(1, 0, 2)[:, None] == spots).astype(jnp.bfloat16)
    onehot = onehot.reshape(blocks, window, slots * BAND)
    picked = jnp.einsum("bxw,bwn->bxn", pieces, onehot, preferred_element_type=jnp.float32)
    picked = picked.reshape(blocks, 3, samples, shells, slots, BAND)
    picked = (picked[:, 0] + picked[:, 1]) + picked[:, 2]
    return picked.transpose(1, 2, 3, 0, 4).reshape(samples, shells, slots, pixels)


INTERPRET = False
LANES = 128


def shifted(values, amount, toward_end):
    rows = values.shape[0]
    row = lax.broadcasted_iota(jnp.int32, values.shape, 0)
    if toward_end:
        return jnp.where(row >= amount, pltpu.roll(values, amount, 0), 0.0)
    return jnp.where(row < rows - amount, pltpu.roll(values, rows - amount, 0), 0.0)


def running(values, toward_end):
    for amount in (1, 2, 4):
        values = values + shifted(values, amount, toward_end)
    return values


def paired(values, odd_from_even):
    row = lax.broadcasted_iota(jnp.int32, values.shape, 0)
    if odd_from_even:
        return jnp.where(row % 2 == 1, shifted(values, 1, True), values)
    return jnp.where(row % 2 == 0, shifted(values, 1, False), values)


def alternating(table, index_of, count, target):
    row = lax.broadcasted_iota(jnp.int32, (8, LANES), 0)
    for n in range(count):
        even = jnp.full((8, LANES), table[index_of(n, 0)], jnp.float32)
        odd = jnp.full((8, LANES), table[index_of(n, 1)], jnp.float32)
        target[n] = jnp.where(row % 2 == 0, even, odd)


def forward_kernel(
    weights_ref, sqrt_ref, pieces_ref, onehot_ref, excite_ref, counts_ref, stars_ref, widths_ref,
    density_ref, local_ref, sums_ref, picked_ref, weight_tiles, sqrt_tiles, width_tiles,
):
    blocks = onehot_ref.shape[0]
    slots = onehot_ref.shape[2] // LANES
    tile = blocks * LANES
    rows = picked_ref.shape[0]

    @pl.when(pl.program_id(0) == 0)
    def _():
        alternating(weights_ref, lambda n, t: t * 4 * 3 * slots + n, 4 * 3 * slots, weight_tiles)
        alternating(sqrt_ref, lambda n, t: t * 4 * 2 * 4 + n, 4 * 2 * 4, sqrt_tiles)
        row = lax.broadcasted_iota(jnp.int32, (8, LANES), 0)
        for h in range(2):
            column = jnp.zeros((8, LANES), jnp.float32)
            for i in range(8):
                column = jnp.where(row == i, widths_ref[8 * h + i], column)
            width_tiles[h] = column

    for b in range(blocks):
        picked = jnp.dot(pieces_ref[0, b], onehot_ref[b], preferred_element_type=jnp.float32)
        picked_ref[...] = (picked[0:rows] + picked[rows : 2 * rows]) + picked[2 * rows : 3 * rows]
        acc = {}
        for h in range(2):
            spread = {}
            for r in range(4):
                lanes = pl.ds(r * tile + b * LANES, LANES)
                values = excite_ref[0, pl.ds(8 * h, 8), lanes].astype(jnp.float32)
                spread[0, r] = paired(values, True)
                spread[1, r] = paired(values, False)
            for q in range(4):
                total = None
                for u in range(2):
                    for r in range(4):
                        term = sqrt_tiles[(q * 2 + u) * 4 + r] * spread[u, r]
                        total = term if total is None else total + term
                acc[h, q] = total
        for j in range(3):
            for m in range(slots):
                for h in range(2):
                    near = picked_ref[pl.ds(8 * h + 2 * j, 8), pl.ds(m * LANES, LANES)]
                    for q in range(4):
                        acc[h, q] = acc[h, q] + weight_tiles[(q * 3 + j) * 9 + m] * near
        for q in range(4):
            lanes = pl.ds(q * tile + b * LANES, LANES)
            first = jnp.exp(acc[0, q]) * width_tiles[0]
            second = jnp.exp(acc[1, q]) * width_tiles[1]
            density_ref[0, pl.ds(0, 8), lanes] = first
            density_ref[0, pl.ds(8, 8), lanes] = second
            low = running(first, True)
            high = running(second, True) + jnp.broadcast_to(low[7:8], low.shape)
            local_ref[0, pl.ds(0, 8), lanes] = low
            local_ref[0, pl.ds(8, 8), lanes] = high
            misfit = counts_ref[pl.ds(0, 8), lanes].astype(jnp.float32) * (low - stars_ref[pl.ds(0, 8), lanes]) + counts_ref[
                pl.ds(8, 8), lanes
            ].astype(jnp.float32) * (high - stars_ref[pl.ds(8, 8), lanes])
            sums_ref[0, 0:1, lanes] = high[7:8]
            sums_ref[0, 1:2, lanes] = jnp.sum(misfit, axis=0, keepdims=True)


def backward_kernel(
    sqrt_ref, density_ref, local_ref, carries_ref, counts_ref, stars_ref, extinct_ref, grad_ref, sqrt_tiles
):
    tile = density_ref.shape[2] // 4
    blocks = tile // LANES

    @pl.when(pl.program_id(0) == 0)
    def _():
        alternating(sqrt_ref, lambda n, u: ((n // 4) * 2 + u) * 4 + n % 4, 2 * 4 * 4, sqrt_tiles)

    for b in range(blocks):
        flow = {}
        for q in range(4):
            lanes = pl.ds(q * tile + b * LANES, LANES)
            into = carries_ref[0, 0:1, lanes]
            past = carries_ref[0, 1:2, lanes]
            low = local_ref[0, pl.ds(0, 8), lanes] + into
            high = local_ref[0, pl.ds(8, 8), lanes] + into
            extinct_ref[0, pl.ds(0, 8), lanes] = low.astype(extinct_ref.dtype)
            extinct_ref[0, pl.ds(8, 8), lanes] = high.astype(extinct_ref.dtype)
            miss_low = counts_ref[pl.ds(0, 8), lanes].astype(jnp.float32) * (low - stars_ref[pl.ds(0, 8), lanes])
            miss_high = counts_ref[pl.ds(8, 8), lanes].astype(jnp.float32) * (high - stars_ref[pl.ds(8, 8), lanes])
            behind_high = running(miss_high, False)
            behind_low = running(miss_low, False) + jnp.broadcast_to(behind_high[0:1], behind_high.shape)
            for h, behind in ((0, behind_low), (1, behind_high)):
                moving = density_ref[0, pl.ds(8 * h, 8), lanes] * (behind + past)
                flow[h, q, 0] = paired(moving, True)
                flow[h, q, 1] = paired(moving, False)
        for h in range(2):
            for r in range(4):
                total = None
                for t in range(2):
                    for q in range(4):
                        term = sqrt_tiles[(t * 4 + q) * 4 + r] * flow[h, q, t]
                        total = term if total is None else total + term
                grad_ref[0, pl.ds(8 * h, 8), pl.ds(r * tile + b * LANES, LANES)] = total


def by_parity(values):
    lead = values.shape[:-2]
    shells, width = values.shape[-2:]
    values = values.reshape(lead + (shells // 2, 2, width))
    return jnp.swapaxes(values, -2, -3)


def from_parity(values):
    lead = values.shape[:-3]
    _, shells, width = values.shape[-3:]
    return jnp.swapaxes(values, -2, -3).reshape(lead + (2 * shells, width))


def tiles(values):
    flat = values.reshape(-1)
    return jnp.broadcast_to(flat[:, None, None], (flat.shape[0], 8, LANES))


def local_forward(extended, halo_index, excitations, refine_weights, refine_sqrt, counts, stars, widths):
    samples, shells, _ = extended.shape
    slots, pixels = halo_index.shape
    blocks = pixels // BAND
    window = 3 * BAND
    fine_shells = excitations.shape[1]
    fine_pixels = excitations.shape[2]
    rows = 2 * (fine_shells // 2 + 4)
    split = split_three(extended)
    split = jnp.pad(split, ((0, 0), (0, 0), (0, rows // 2 - shells), (0, 0)))
    split = jnp.repeat(split, 2, axis=2)
    pieces = jnp.stack([split[:, :, :, b * BAND : b * BAND + window] for b in range(blocks)], axis=2)
    pieces = pieces.transpose(1, 2, 0, 3, 4).reshape(samples, blocks, 3 * rows, window)
    starts = (jnp.arange(blocks, dtype=jnp.int32) * BAND)[None, :, None]
    local = halo_index.reshape(slots, blocks, BAND) - starts
    spots = jnp.arange(window, dtype=jnp.int32)[None, :, None, None]
    onehot = (local.transpose(1, 0, 2)[:, None] == spots).astype(jnp.bfloat16)
    onehot = onehot.reshape(blocks, window, slots * BAND)
    half = fine_shells // 2
    smem = pl.BlockSpec(memory_space=pltpu.SMEM)
    whole = lambda shape: pl.BlockSpec(shape, lambda k: (0,) * len(shape))
    per_sample = lambda shape: pl.BlockSpec(shape, lambda k: (k,) + (0,) * (len(shape) - 1))
    return pl.pallas_call(
        forward_kernel,
        grid=(samples,),
        in_specs=[
            smem,
            smem,
            per_sample((1, blocks, 3 * rows, window)),
            whole((blocks, window, slots * BAND)),
            per_sample((1, fine_shells, fine_pixels)),
            whole((fine_shells, fine_pixels)),
            whole((fine_shells, fine_pixels)),
            smem,
        ],
        out_specs=[
            per_sample((1, fine_shells, fine_pixels)),
            per_sample((1, fine_shells, fine_pixels)),
            per_sample((1, 2, fine_pixels)),
        ],
        out_shape=[
            jax.ShapeDtypeStruct((samples, fine_shells, fine_pixels), jnp.float32),
            jax.ShapeDtypeStruct((samples, fine_shells, fine_pixels), jnp.float32),
            jax.ShapeDtypeStruct((samples, 2, fine_pixels), jnp.float32),
        ],
        scratch_shapes=[
            pltpu.VMEM((rows, slots * BAND), jnp.float32),
            pltpu.VMEM((4 * 3 * slots, 8, LANES), jnp.float32),
            pltpu.VMEM((4 * 2 * 4, 8, LANES), jnp.float32),
            pltpu.VMEM((2, 8, LANES), jnp.float32),
        ],
        interpret=INTERPRET,
    )(
        refine_weights.reshape(-1),
        refine_sqrt.astype(jnp.float32).reshape(-1),
        pieces,
        onehot,
        excitations,
        counts,
        stars,
        widths,
    )


def local_backward(refine_sqrt, density, local_cum, carries, counts, stars):
    samples, fine_shells, fine_pixels = density.shape
    smem = pl.BlockSpec(memory_space=pltpu.SMEM)
    whole = lambda shape: pl.BlockSpec(shape, lambda k: (0,) * len(shape))
    per_sample = lambda shape: pl.BlockSpec(shape, lambda k: (k,) + (0,) * (len(shape) - 1))
    return pl.pallas_call(
        backward_kernel,
        grid=(samples,),
        in_specs=[
            smem,
            per_sample((1, fine_shells, fine_pixels)),
            per_sample((1, fine_shells, fine_pixels)),
            per_sample((1, 2, fine_pixels)),
            whole((fine_shells, fine_pixels)),
            whole((fine_shells, fine_pixels)),
        ],
        out_specs=[
            per_sample((1, fine_shells, fine_pixels)),
            per_sample((1, fine_shells, fine_pixels)),
        ],
        out_shape=[
            jax.ShapeDtypeStruct((samples, fine_shells, fine_pixels), jnp.bfloat16),
            jax.ShapeDtypeStruct((samples, fine_shells, fine_pixels), jnp.float32),
        ],
        scratch_shapes=[pltpu.VMEM((2 * 4 * 4, 8, LANES), jnp.float32)],
        interpret=INTERPRET,
    )(refine_sqrt.astype(jnp.float32).reshape(-1), density, local_cum, carries, counts, stars)


def shards(
    coarse_field, excitations, refine_weights, refine_sqrt, halo_index, star_extinction, star_counts
):
    samples, coarse_shells, coarse_pixels = coarse_field.shape
    fine_shells = 2 * coarse_shells
    fine_pixels = 4 * coarse_pixels
    dist_count = lax.axis_size("dist")
    dist_rank = lax.axis_index("dist")
    all_shells = fine_shells * dist_count
    blocked = coarse_field.reshape(samples, coarse_shells, coarse_pixels // BAND, BAND)
    extended = with_halo(blocked, (("dist", 1), ("sky", 2)), 1)
    extended = extended.reshape(samples, coarse_shells + 2, coarse_pixels + 2 * BAND)
    shells = dist_rank * fine_shells + jnp.arange(fine_shells, dtype=jnp.int32)
    middle = (shells.astype(jnp.float32) + 0.5) / all_shells
    widths = 3.0 * jnp.exp(3.0 * middle - 3.0) / all_shells
    counts = star_counts
    density, local_cum, sums = local_forward(
        extended, halo_index, excitations, refine_weights, refine_sqrt, counts, star_extinction, widths
    )
    weight = jnp.sum(counts, axis=0, keepdims=True).astype(jnp.float32)
    carries = block_carries(sums[:, 0], sums[:, 1], weight, "dist")
    return local_backward(refine_sqrt, density, local_cum, carries, counts, star_extinction)


def solution(mesh):
    placed = (
        P(None, "dist", "sky"),
        P(None, "dist", "sky"),
        P(),
        P(),
        P(None, "sky"),
        P("dist", "sky"),
        P("dist", "sky"),
    )
    return jax.shard_map(
        shards,
        mesh=mesh,
        in_specs=placed,
        out_specs=(P(None, "dist", "sky"), P(None, "dist", "sky")),
        check_vma=False,
    )
```
